32 devices in a mesh: groups: 2 (over x), wide: 16 (over z, y, core).
Axes of the slice: x: 2, y: 2, z: 4, core: 2. Of those that a mesh axis runs over, the one named last changes fastest.
Arguments:
- activity: bfloat16 [1024, 16, 512], P(('groups', 'wide')), parts along dimension 0, may hold values from -6 to 6
- grad_out: bfloat16 [1024, 16, 512], P('groups', 'wide'), parts along dimension 0, may hold values from -6 to 6
- spatial_weights: bfloat16 [512, 2048], replicated, may hold values from -8 to 8
- temporal_weights: bfloat16 [512, 2048], replicated, may hold values from -8 to 8
- spatial_gain: float32 [512], replicated, may hold values from 0.25 to 1.75
- temporal_gain: float32 [512], replicated, may hold values from 0.25 to 1.75
- adjacency: int32 [16, 16], replicated, may hold values from 0 to 1
- channel_count: int32 [8], P('groups'), parts along dimension 0, may hold values from 128 to 2048
- session_id: int32 [1024], P('groups'), parts along dimension 0, may hold values from 0 to 3, never falling along the last dimension, each value on 1 to 256 neighbouring positions
Outputs:
- layer_out: bfloat16 [1024, 16, 512], P('groups', 'wide'), parts along dimension 0
- grad_activity: bfloat16 [1024, 16, 512], P(('groups', 'wide')), parts along dimension 0
- spatial_grad: float32 [1024, 2048], P(('groups', 'wide')), parts along dimension 0
- temporal_grad: float32 [1024, 2048], P(('groups', 'wide')), parts along dimension 0
The draws below stay inside these ranges and needn't reach their ends.
There are 2 independent parts, one for each index of `groups`. The reference program is written for one: setup_inputs(seed, part) draws one part's arguments, and reference() takes and returns one part's arrays. A program takes and returns all parts, laid end to end along the dimension named above; an argument that names none is the same for every part. Nothing has to cross between parts.
Inputs may be any that keep to these rules, and one draw needn't show every extreme that they name: `session_id`: session ids never fall along time; every session holds 1 to 256 bins, one exactly 256.
All inputs are finite; a program needn't handle non-finite values.
Results may differ from the reference program's by a relative error of at most 0.015.
Values may be sent and summed in bfloat16 or wider, within the bound.
No kernel may reach another device: no remote copies, remote signals or barrier semaphores. Data moves between devices by JAX's collectives and lax.ppermute only.
A program may use at most 192 MiB of HBM per device.

```python
import math
import jax
import jax.numpy as jnp
import numpy as np
from jax import lax

D = 512
HEADS = 8
SESS = 4
BINS = 512
BLOCKS = 16


def projection_weights(key):
    drawn = jnp.clip(jax.random.normal(key, (D, 4 * D), jnp.float32), -6.0, 6.0) * D ** (-0.5)
    return drawn.astype(jnp.bfloat16)


def draw_spatial_weights(key, part):
    return projection_weights(jax.random.fold_in(key, 11))


def draw_temporal_weights(key, part):
    return projection_weights(jax.random.fold_in(key, 23))


def place_ends(array, key, smallest, top_value):
    extent = array.shape
    spot = [jax.random.randint(jax.random.fold_in(key, axis), (), 0, extent[axis]) for axis in range(len(extent))]
    array = array.at[tuple(spot)].set(smallest)
    longest = extent.index(max(extent))
    spot[longest] = (spot[longest] + 1) % extent[longest]
    return array.at[tuple(spot)].set(top_value)


def level_of(key, extent, cuts, least, high):
    level = 1.0
    for dim, shards_of in cuts:
        steps = jax.random.uniform(jax.random.fold_in(jax.random.fold_in(key, 6), dim), (shards_of,), jnp.float32, least / len(cuts), high / len(cuts))
        level = level * jnp.repeat(jnp.exp(steps), extent[dim] // shards_of).reshape((-1,) + (1,) * (len(extent) - 1 - dim))
    return level


def profile(number_of, total, most, lean):
    portions = [(1 << 20) // math.isqrt(grade ** lean) + 1 for grade in range(2, number_of + 1)]
    surplus, holding = total - most - (number_of - 1), [1] * (number_of - 1)
    while surplus > 0:
        candidates = [i for i in range(number_of - 1) if holding[i] < most]
        mass, budget = sum([portions[i] for i in candidates]), surplus
        for i in candidates:
            addition = min(most - holding[i], max(1, budget * portions[i] // mass), surplus)
            holding[i] = holding[i] + addition
            surplus = surplus - addition
    return np.array([most] + holding)


def uneven(key, count, total, limit, lean):
    if count == 2:
        one = jax.random.randint(key, (), max(1, total - limit), min(limit, total - 1) + 1)
        return jnp.stack([one, total - one])
    tallies = jnp.asarray(profile(count, total, limit, lean), jnp.int32)
    pairs = (count - 1) // 2
    giver, receiver = tallies[1:1 + 2 * pairs:2], tallies[2:2 + 2 * pairs:2]
    room = jnp.minimum(giver - 1, limit - receiver)
    moved = jax.random.randint(jax.random.fold_in(key, 1), (pairs,), 0, 1 << 20) % (room + 1)
    tallies = tallies.at[1:1 + 2 * pairs:2].set(giver - moved).at[2:2 + 2 * pairs:2].set(receiver + moved)
    return tallies[jax.random.permutation(jax.random.fold_in(key, 2), count)]


def scatter_about(rng, dims, deviation, most, shards=(), kind=jnp.bfloat16):
    values = deviation * jax.random.normal(rng, dims, jnp.float32)
    if shards:
        values = values * level_of(rng, dims, shards, -0.22, 0.18)
    return jnp.clip(values, -most, most).astype(kind)


def setup_inputs(seed: int = 0, part: int = 0) -> dict:
    seeds = jax.random.split(jax.random.key(seed), 10)
    part_splits = jax.random.split(jax.random.fold_in(seeds[9], part), 10)
    activity = scatter_about(part_splits[0], (BINS, BLOCKS, D), 1.0, 6.0, ((0, 16),))
    grad_out = scatter_about(part_splits[1], (BINS, BLOCKS, D), 1.0, 6.0, ((1, 16),))
    spatial_weights = draw_spatial_weights(jax.random.fold_in(seeds[9], 71), part)
    temporal_weights = draw_temporal_weights(jax.random.fold_in(seeds[9], 71), part)
    spatial_gain = jnp.clip(1.0 + 0.15 * jax.random.normal(seeds[4], (D,), jnp.float32), 0.25, 1.75)
    temporal_gain = jnp.clip(1.0 + 0.15 * jax.random.normal(seeds[5], (D,), jnp.float32), 0.25, 1.75)
    adjacency = place_ends(jax.random.randint(seeds[6], (BLOCKS, BLOCKS), 0, 2), jax.random.fold_in(seeds[6], 1), 0, 1).astype(jnp.int32)
    channel_count = place_ends(jax.random.randint(part_splits[7], (SESS,), 128, BLOCKS * 128 + 1), jax.random.fold_in(part_splits[7], 1), 128, BLOCKS * 128).astype(jnp.int32)
    session_id = jnp.searchsorted(jnp.cumsum(uneven(part_splits[8], SESS, BINS, BINS // 2, 1)), jnp.arange(BINS), side="right").astype(jnp.int32)
    return dict(activity=activity, grad_out=grad_out, spatial_weights=spatial_weights, temporal_weights=temporal_weights, spatial_gain=spatial_gain, temporal_gain=temporal_gain, adjacency=adjacency, channel_count=channel_count, session_id=session_id)


eps_norm = 1e-05
block_channels = 128

def norm_inverse(rows):
    values = rows.astype(jnp.float32)
    return lax.rsqrt(lax.optimization_barrier(jnp.mean(values * values, axis=-1, keepdims=True)) + eps_norm)

def norm_forward(rows, gain):
    inverse = norm_inverse(rows)
    return ((rows.astype(jnp.float32) * inverse * gain).astype(jnp.bfloat16), inverse)

def norm_backward(rows, gain, inverse, grad_normed):
    values = rows.astype(jnp.float32)
    scaled = grad_normed * gain
    inner = lax.optimization_barrier(jnp.mean(values * scaled, axis=-1, keepdims=True))
    return inverse * scaled - values * inverse * inverse * inverse * inner

def normalized_affinity(asking_vectors, lookup_array, admissible_pairs, sharpness_divisor):
    unnormalized_affinities = jnp.einsum('...uo,...ao->...ua', asking_vectors, lookup_array, preferred_element_type=jnp.float32) * sharpness_divisor
    unnormalized_affinities = jnp.where(admissible_pairs, unnormalized_affinities, -1e+30)
    row_max = lax.optimization_barrier(jnp.max(unnormalized_affinities, axis=-1, keepdims=True))
    expo = jnp.exp(unnormalized_affinities - row_max)
    return expo / lax.optimization_barrier(jnp.sum(expo, axis=-1, keepdims=True))

def compute_affinity_outputs(asking_vectors, lookup_array, payload_array, admissible_pairs, sharpness_divisor):
    truncated_outcome = normalized_affinity(asking_vectors, lookup_array, admissible_pairs, sharpness_divisor).astype(jnp.bfloat16)
    return jnp.einsum('...qk,...kd->...qd', truncated_outcome, payload_array, preferred_element_type=jnp.float32).astype(jnp.bfloat16)

def compute_affinity_derivatives(asking_vectors, lookup_array, payload_array, admissible_pairs, sharpness_divisor, combined_output, blended_output_derivative):
    coefficient_array = normalized_affinity(asking_vectors, lookup_array, admissible_pairs, sharpness_divisor)
    truncated_outcome = coefficient_array.astype(jnp.bfloat16)
    grad_values = jnp.einsum('...qk,...qd->...kd', truncated_outcome, blended_output_derivative, preferred_element_type=jnp.float32)
    coefficient_derivative = jnp.einsum('...uo,...ao->...ua', blended_output_derivative, payload_array, preferred_element_type=jnp.float32)
    paired_inner_sums = lax.optimization_barrier(jnp.sum(blended_output_derivative.astype(jnp.float32) * combined_output.astype(jnp.float32), axis=-1, keepdims=True))
    affinity_derivative = (coefficient_array * (coefficient_derivative - paired_inner_sums) * sharpness_divisor).astype(jnp.bfloat16)
    grad_queries = jnp.einsum('...qk,...kd->...qd', affinity_derivative, lookup_array, preferred_element_type=jnp.float32)
    grad_keys = jnp.einsum('...qk,...qd->...kd', affinity_derivative, asking_vectors, preferred_element_type=jnp.float32)
    return (grad_queries.astype(jnp.bfloat16), grad_keys.astype(jnp.bfloat16), grad_values.astype(jnp.bfloat16))

def temporal_split(projected):
    pieces = projected.reshape(projected.shape[0], 3, HEADS, projected.shape[1] // (3 * HEADS))
    return [pieces[:, index].transpose(1, 0, 2) for index in range(3)]

def temporal_forward(projected, admissible_pairs):
    asking_vectors, lookup_array, payload_array = temporal_split(projected)
    sharpness_divisor = float(asking_vectors.shape[-1]) ** (-0.5)
    combined_output = compute_affinity_outputs(asking_vectors, lookup_array, payload_array, admissible_pairs[None], sharpness_divisor)
    return combined_output.transpose(1, 0, 2).reshape(projected.shape[0], -1)

def temporal_backward(projected, admissible_pairs, combined_output, blended_output_derivative):
    asking_vectors, lookup_array, payload_array = temporal_split(projected)
    sharpness_divisor = float(asking_vectors.shape[-1]) ** (-0.5)
    bins = projected.shape[0]
    subspace_outputs = combined_output.reshape(bins, HEADS, -1).transpose(1, 0, 2)
    subspace_derivative = blended_output_derivative.reshape(bins, HEADS, -1).transpose(1, 0, 2)
    derivative_collection = compute_affinity_derivatives(asking_vectors, lookup_array, payload_array, admissible_pairs[None], sharpness_divisor, subspace_outputs, subspace_derivative)
    return jnp.stack(derivative_collection, axis=0).transpose(2, 0, 1, 3).reshape(bins, -1)

def spatial_split(projected):
    pieces = projected.reshape(projected.shape[0], projected.shape[1], 3, HEADS, projected.shape[2] // (3 * HEADS))
    return [pieces[:, :, index].transpose(0, 2, 1, 3) for index in range(3)]

def spatial_forward(projected, admissible_pairs):
    asking_vectors, lookup_array, payload_array = spatial_split(projected)
    sharpness_divisor = float(asking_vectors.shape[-1]) ** (-0.5)
    combined_output = compute_affinity_outputs(asking_vectors, lookup_array, payload_array, admissible_pairs, sharpness_divisor)
    return combined_output.transpose(0, 2, 1, 3).reshape(projected.shape[0], projected.shape[1], -1)

def spatial_backward(projected, admissible_pairs, combined_output, blended_output_derivative):
    asking_vectors, lookup_array, payload_array = spatial_split(projected)
    sharpness_divisor = float(asking_vectors.shape[-1]) ** (-0.5)
    bins, blocks = (projected.shape[0], projected.shape[1])
    subspace_outputs = combined_output.reshape(bins, blocks, HEADS, -1).transpose(0, 2, 1, 3)
    subspace_derivative = blended_output_derivative.reshape(bins, blocks, HEADS, -1).transpose(0, 2, 1, 3)
    derivative_collection = compute_affinity_derivatives(asking_vectors, lookup_array, payload_array, admissible_pairs, sharpness_divisor, subspace_outputs, subspace_derivative)
    return jnp.stack(derivative_collection, axis=0).transpose(1, 3, 0, 2, 4).reshape(bins, blocks, -1)

def spatial_allowed(sessions_here, channel_count, adjacency):
    block_count = adjacency.shape[0]
    block_ids = jnp.arange(block_count, dtype=jnp.int32)
    session_pick = (sessions_here[:, None] == jnp.arange(channel_count.shape[0], dtype=jnp.int32)[None, :]).astype(jnp.int32)
    count_rows = lax.optimization_barrier(jnp.sum(session_pick * channel_count[None, :], axis=1))
    live_block = block_ids[None, :] * block_channels < count_rows[:, None]
    linked = adjacency > 0
    itself = block_ids[:, None] == block_ids[None, :]
    admissible_pairs = linked[None, :, :] & live_block[:, None, :] | itself[None, :, :]
    return admissible_pairs[:, None, :, :]

def project(rows, coefficient_array):
    return jnp.einsum('tbd,de->tbe', rows, coefficient_array, preferred_element_type=jnp.float32)

def project_back(derivative_collection, coefficient_array):
    return jnp.einsum('tbe,de->tbd', derivative_collection, coefficient_array, preferred_element_type=jnp.float32)

def weight_term(left, right):
    return jnp.einsum('tbd,tbe->de', left, right, preferred_element_type=jnp.float32)

def reference(activity, grad_out, spatial_weights, temporal_weights, spatial_gain, temporal_gain, adjacency, channel_count, session_id):
    model_width = activity.shape[2]
    normed_one, inverse_one = norm_forward(activity, spatial_gain)
    spatial_proj = project(normed_one, spatial_weights[:, :3 * model_width]).astype(jnp.bfloat16)
    allowed_space = spatial_allowed(session_id, channel_count, adjacency)
    spatial_context = spatial_forward(spatial_proj, allowed_space)
    middle = (activity.astype(jnp.float32) + project(spatial_context, spatial_weights[:, 3 * model_width:])).astype(jnp.bfloat16)
    normed_two, inverse_two = norm_forward(middle, temporal_gain)
    temporal_proj = project(normed_two, temporal_weights[:, :3 * model_width]).astype(jnp.bfloat16)
    allowed_time = session_id[:, None] == session_id[None, :]
    by_block = jnp.moveaxis(temporal_proj, 1, 0)
    temporal_context = jnp.moveaxis(lax.map(lambda block_rows: temporal_forward(block_rows, allowed_time), by_block), 0, 1)
    layer_out = (middle.astype(jnp.float32) + project(temporal_context, temporal_weights[:, 3 * model_width:])).astype(jnp.bfloat16)
    grad_temporal_context = project_back(grad_out, temporal_weights[:, 3 * model_width:]).astype(jnp.bfloat16)
    stacked = (by_block, jnp.moveaxis(temporal_context, 1, 0), jnp.moveaxis(grad_temporal_context, 1, 0))
    grad_temporal_proj = jnp.moveaxis(lax.map(lambda items: temporal_backward(items[0], allowed_time, items[1], items[2]), stacked), 0, 1)
    grad_normed_two = project_back(grad_temporal_proj, temporal_weights[:, :3 * model_width])
    grad_middle = (grad_out.astype(jnp.float32) + norm_backward(middle, temporal_gain, inverse_two, grad_normed_two)).astype(jnp.bfloat16)
    temporal_grad = jnp.concatenate([weight_term(normed_two, grad_temporal_proj), weight_term(temporal_context, grad_out)], axis=1)
    grad_spatial_context = project_back(grad_middle, spatial_weights[:, 3 * model_width:]).astype(jnp.bfloat16)
    grad_spatial_proj = spatial_backward(spatial_proj, allowed_space, spatial_context, grad_spatial_context)
    grad_normed_one = project_back(grad_spatial_proj, spatial_weights[:, :3 * model_width])
    grad_activity = (grad_middle.astype(jnp.float32) + norm_backward(activity, spatial_gain, inverse_one, grad_normed_one)).astype(jnp.bfloat16)
    spatial_grad = jnp.concatenate([weight_term(normed_one, grad_spatial_proj), weight_term(spatial_context, grad_middle)], axis=1)
    return (layer_out, grad_activity, spatial_grad, temporal_grad)
```

```python
import jax
import jax.numpy as jnp
from jax import lax
from jax.sharding import Mesh, PartitionSpec as P

HEADS = 8


eps_norm = 1e-05
block_channels = 128


def norm_inverse(rows):
    values = rows.astype(jnp.float32)
    return lax.rsqrt(jnp.mean(values * values, axis=-1, keepdims=True) + eps_norm)


def norm_forward(rows, gain):
    inverse = norm_inverse(rows)
    return ((rows.astype(jnp.float32) * inverse * gain).astype(jnp.bfloat16), inverse)


def norm_backward(rows, gain, inverse, grad_normed):
    values = rows.astype(jnp.float32)
    scaled = grad_normed * gain
    inner = jnp.mean(values * scaled, axis=-1, keepdims=True)
    return inverse * scaled - values * inverse * inverse * inverse * inner


def normalized_affinity(asking_vectors, lookup_array, admissible_pairs, sharpness_divisor):
    unnormalized_affinities = (
        jnp.einsum(
            "...uo,...ao->...ua", asking_vectors, lookup_array, preferred_element_type=jnp.float32
        )
        * sharpness_divisor
    )
    unnormalized_affinities = jnp.where(admissible_pairs, unnormalized_affinities, -1e30)
    row_max = jnp.max(unnormalized_affinities, axis=-1, keepdims=True)
    expo = jnp.exp(unnormalized_affinities - row_max)
    return expo / jnp.sum(expo, axis=-1, keepdims=True)


def compute_affinity_outputs(
    asking_vectors, lookup_array, payload_array, admissible_pairs, sharpness_divisor
):
    truncated_outcome = normalized_affinity(
        asking_vectors, lookup_array, admissible_pairs, sharpness_divisor
    ).astype(jnp.bfloat16)
    return jnp.einsum(
        "...qk,...kd->...qd", truncated_outcome, payload_array, preferred_element_type=jnp.float32
    ).astype(jnp.bfloat16)


def compute_affinity_derivatives(
    asking_vectors,
    lookup_array,
    payload_array,
    admissible_pairs,
    sharpness_divisor,
    combined_output,
    blended_output_derivative,
):
    coefficient_array = normalized_affinity(
        asking_vectors, lookup_array, admissible_pairs, sharpness_divisor
    )
    truncated_outcome = coefficient_array.astype(jnp.bfloat16)
    grad_values = jnp.einsum(
        "...qk,...qd->...kd",
        truncated_outcome,
        blended_output_derivative,
        preferred_element_type=jnp.float32,
    )
    coefficient_derivative = jnp.einsum(
        "...uo,...ao->...ua",
        blended_output_derivative,
        payload_array,
        preferred_element_type=jnp.float32,
    )
    paired_inner_sums = jnp.sum(
        blended_output_derivative.astype(jnp.float32) * combined_output.astype(jnp.float32),
        axis=-1,
        keepdims=True,
    )
    affinity_derivative = (
        coefficient_array * (coefficient_derivative - paired_inner_sums) * sharpness_divisor
    ).astype(jnp.bfloat16)
    grad_queries = jnp.einsum(
        "...qk,...kd->...qd", affinity_derivative, lookup_array, preferred_element_type=jnp.float32
    )
    grad_keys = jnp.einsum(
        "...qk,...qd->...kd",
        affinity_derivative,
        asking_vectors,
        preferred_element_type=jnp.float32,
    )
    return (
        grad_queries.astype(jnp.bfloat16),
        grad_keys.astype(jnp.bfloat16),
        grad_values.astype(jnp.bfloat16),
    )


def temporal_split(projected):
    pieces = projected.reshape(projected.shape[0], 3, HEADS, projected.shape[1] // (3 * HEADS))
    return [pieces[:, index].transpose(1, 0, 2) for index in range(3)]


def temporal_forward(projected, admissible_pairs):
    asking_vectors, lookup_array, payload_array = temporal_split(projected)
    sharpness_divisor = float(asking_vectors.shape[-1]) ** (-0.5)
    combined_output = compute_affinity_outputs(
        asking_vectors, lookup_array, payload_array, admissible_pairs[None], sharpness_divisor
    )
    return combined_output.transpose(1, 0, 2).reshape(projected.shape[0], -1)


def temporal_backward(projected, admissible_pairs, combined_output, blended_output_derivative):
    asking_vectors, lookup_array, payload_array = temporal_split(projected)
    sharpness_divisor = float(asking_vectors.shape[-1]) ** (-0.5)
    bins = projected.shape[0]
    subspace_outputs = combined_output.reshape(bins, HEADS, -1).transpose(1, 0, 2)
    subspace_derivative = blended_output_derivative.reshape(bins, HEADS, -1).transpose(1, 0, 2)
    derivative_collection = compute_affinity_derivatives(
        asking_vectors,
        lookup_array,
        payload_array,
        admissible_pairs[None],
        sharpness_divisor,
        subspace_outputs,
        subspace_derivative,
    )
    return jnp.stack(derivative_collection, axis=0).transpose(2, 0, 1, 3).reshape(bins, -1)


def spatial_split(projected):
    pieces = projected.reshape(
        projected.shape[0], projected.shape[1], 3, HEADS, projected.shape[2] // (3 * HEADS)
    )
    return [pieces[:, :, index].transpose(0, 2, 1, 3) for index in range(3)]


def spatial_forward(projected, admissible_pairs):
    asking_vectors, lookup_array, payload_array = spatial_split(projected)
    sharpness_divisor = float(asking_vectors.shape[-1]) ** (-0.5)
    combined_output = compute_affinity_outputs(
        asking_vectors, lookup_array, payload_array, admissible_pairs, sharpness_divisor
    )
    return combined_output.transpose(0, 2, 1, 3).reshape(projected.shape[0], projected.shape[1], -1)


def spatial_backward(projected, admissible_pairs, combined_output, blended_output_derivative):
    asking_vectors, lookup_array, payload_array = spatial_split(projected)
    sharpness_divisor = float(asking_vectors.shape[-1]) ** (-0.5)
    bins, blocks = (projected.shape[0], projected.shape[1])
    subspace_outputs = combined_output.reshape(bins, blocks, HEADS, -1).transpose(0, 2, 1, 3)
    subspace_derivative = blended_output_derivative.reshape(bins, blocks, HEADS, -1).transpose(
        0, 2, 1, 3
    )
    derivative_collection = compute_affinity_derivatives(
        asking_vectors,
        lookup_array,
        payload_array,
        admissible_pairs,
        sharpness_divisor,
        subspace_outputs,
        subspace_derivative,
    )
    return (
        jnp.stack(derivative_collection, axis=0).transpose(1, 3, 0, 2, 4).reshape(bins, blocks, -1)
    )


def spatial_allowed(sessions_here, channel_count, adjacency):
    block_count = adjacency.shape[0]
    block_ids = jnp.arange(block_count, dtype=jnp.int32)
    session_pick = (
        sessions_here[:, None] == jnp.arange(channel_count.shape[0], dtype=jnp.int32)[None, :]
    ).astype(jnp.int32)
    count_rows = jnp.sum(session_pick * channel_count[None, :], axis=1)
    live_block = block_ids[None, :] * block_channels < count_rows[:, None]
    linked = adjacency > 0
    itself = block_ids[:, None] == block_ids[None, :]
    admissible_pairs = linked[None, :, :] & live_block[:, None, :] | itself[None, :, :]
    return admissible_pairs[:, None, :, :]


def project(rows, coefficient_array):
    return jnp.einsum("tbd,de->tbe", rows, coefficient_array, preferred_element_type=jnp.float32)


def project_back(derivative_collection, coefficient_array):
    return jnp.einsum(
        "tbe,de->tbd", derivative_collection, coefficient_array, preferred_element_type=jnp.float32
    )


def weight_term(left, right):
    return jnp.einsum("tbd,tbe->de", left, right, preferred_element_type=jnp.float32)


def reduce_rows(partial):
    rows, cols = partial.shape
    outer = lax.psum(1, "outer")
    pieces = partial.astype(jnp.bfloat16).reshape(outer, 2, rows // (2 * outer), cols)
    pieces = lax.all_to_all(pieces, "core", 1, 1, tiled=True)
    pieces = jnp.sum(pieces.astype(jnp.float32), axis=1).astype(jnp.bfloat16)
    pieces = lax.all_to_all(pieces, "outer", 0, 0, tiled=True)
    return jnp.sum(pieces.astype(jnp.float32), axis=0)


def per_device(
    activity,
    grad_out,
    spatial_weights,
    temporal_weights,
    spatial_gain,
    temporal_gain,
    adjacency,
    channel_count,
    session_id,
):
    local_bins = activity.shape[0]
    model_width = activity.shape[2]
    first_bin = (lax.axis_index("outer") * 2 + lax.axis_index("core")) * local_bins
    sessions_here = lax.dynamic_slice_in_dim(session_id, first_bin, local_bins)
    normed_one, inverse_one = norm_forward(activity, spatial_gain)
    spatial_proj = project(normed_one, spatial_weights[:, : 3 * model_width]).astype(jnp.bfloat16)
    allowed_space = spatial_allowed(sessions_here, channel_count, adjacency)
    spatial_context = spatial_forward(spatial_proj, allowed_space)
    middle = (
        activity.astype(jnp.float32)
        + project(spatial_context, spatial_weights[:, 3 * model_width :])
    ).astype(jnp.bfloat16)
    middle_block = lax.all_to_all(middle, ("outer", "core"), split_axis=1, concat_axis=0, tiled=True)
    normed_two, inverse_two = norm_forward(middle_block, temporal_gain)
    temporal_proj = project(normed_two, temporal_weights[:, : 3 * model_width]).astype(jnp.bfloat16)
    allowed_time = session_id[:, None] == session_id[None, :]
    by_block = jnp.moveaxis(temporal_proj, 1, 0)
    temporal_context = jnp.moveaxis(
        lax.map(lambda block_rows: temporal_forward(block_rows, allowed_time), by_block), 0, 1
    )
    layer_out = (
        middle_block.astype(jnp.float32)
        + project(temporal_context, temporal_weights[:, 3 * model_width :])
    ).astype(jnp.bfloat16)
    grad_temporal_context = project_back(grad_out, temporal_weights[:, 3 * model_width :]).astype(
        jnp.bfloat16
    )
    stacked = (
        by_block,
        jnp.moveaxis(temporal_context, 1, 0),
        jnp.moveaxis(grad_temporal_context, 1, 0),
    )
    grad_temporal_proj = jnp.moveaxis(
        lax.map(
            lambda items: temporal_backward(items[0], allowed_time, items[1], items[2]), stacked
        ),
        0,
        1,
    )
    grad_normed_two = project_back(grad_temporal_proj, temporal_weights[:, : 3 * model_width])
    grad_middle = (
        grad_out.astype(jnp.float32)
        + norm_backward(middle_block, temporal_gain, inverse_two, grad_normed_two)
    ).astype(jnp.bfloat16)
    grad_middle_time = lax.all_to_all(grad_middle, ("outer", "core"), split_axis=0, concat_axis=1, tiled=True)
    normed_cols = normed_two
    context_cols = temporal_context
    temporal_grad = reduce_rows(
        jnp.concatenate(
            [weight_term(normed_cols, grad_temporal_proj), weight_term(context_cols, grad_out)],
            axis=1,
        )
    )
    grad_spatial_context = project_back(
        grad_middle_time, spatial_weights[:, 3 * model_width :]
    ).astype(jnp.bfloat16)
    grad_spatial_proj = spatial_backward(
        spatial_proj, allowed_space, spatial_context, grad_spatial_context
    )
    grad_normed_one = project_back(grad_spatial_proj, spatial_weights[:, : 3 * model_width])
    grad_activity = (
        grad_middle_time.astype(jnp.float32)
        + norm_backward(activity, spatial_gain, inverse_one, grad_normed_one)
    ).astype(jnp.bfloat16)
    normed_cols = normed_one
    context_cols = spatial_context
    spatial_grad = reduce_rows(
        jnp.concatenate(
            [
                weight_term(normed_cols, grad_spatial_proj),
                weight_term(context_cols, grad_middle_time),
            ],
            axis=1,
        )
    )
    return (layer_out, grad_activity, spatial_grad, temporal_grad)


def solution(mesh):
    groups, wide = mesh.devices.shape
    mesh = Mesh(mesh.devices.reshape(groups, wide // 2, 2), ("groups", "outer", "core"))
    placed = (
        P(("groups", "outer", "core"), None, None),
        P("groups", ("outer", "core"), None),
        P(),
        P(),
        P(),
        P(),
        P(),
        P("groups"),
        P("groups"),
    )
    return jax.shard_map(
        per_device,
        mesh=mesh,
        in_specs=placed,
        out_specs=(
            P("groups", ("outer", "core"), None),
            P(("groups", "outer", "core"), None, None),
            P(("groups", "outer", "core"), None),
            P(("groups", "outer", "core"), None),
        ),
        check_vma=False,
    )
```

```python
import jax
import jax.numpy as jnp
from jax import lax
from jax.sharding import Mesh, PartitionSpec as P

HEADS = 8


eps_norm = 1e-05
block_channels = 128


def norm_inverse(rows):
    values = rows.astype(jnp.float32)
    return lax.rsqrt(jnp.mean(values * values, axis=-1, keepdims=True) + eps_norm)


def norm_forward(rows, gain):
    inverse = norm_inverse(rows)
    return ((rows.astype(jnp.float32) * inverse * gain).astype(jnp.bfloat16), inverse)


def norm_backward(rows, gain, inverse, grad_normed):
    values = rows.astype(jnp.float32)
    scaled = grad_normed * gain
    inner = jnp.mean(values * scaled, axis=-1, keepdims=True)
    return inverse * scaled - values * inverse * inverse * inverse * inner


def normalized_affinity(asking_vectors, lookup_array, admissible_pairs, sharpness_divisor):
    unnormalized_affinities = (
        jnp.einsum(
            "...uo,...ao->...ua", asking_vectors, lookup_array, preferred_element_type=jnp.float32
        )
        * sharpness_divisor
    )
    unnormalized_affinities = jnp.where(admissible_pairs, unnormalized_affinities, -1e30)
    row_max = jnp.max(unnormalized_affinities, axis=-1, keepdims=True)
    expo = jnp.exp(unnormalized_affinities - row_max)
    return expo / jnp.sum(expo, axis=-1, keepdims=True)


def compute_affinity_outputs(
    asking_vectors, lookup_array, payload_array, admissible_pairs, sharpness_divisor
):
    truncated_outcome = normalized_affinity(
        asking_vectors, lookup_array, admissible_pairs, sharpness_divisor
    ).astype(jnp.bfloat16)
    return jnp.einsum(
        "...qk,...kd->...qd", truncated_outcome, payload_array, preferred_element_type=jnp.float32
    ).astype(jnp.bfloat16)


def compute_affinity_derivatives(
    asking_vectors,
    lookup_array,
    payload_array,
    admissible_pairs,
    sharpness_divisor,
    combined_output,
    blended_output_derivative,
):
    coefficient_array = normalized_affinity(
        asking_vectors, lookup_array, admissible_pairs, sharpness_divisor
    )
    truncated_outcome = coefficient_array.astype(jnp.bfloat16)
    grad_values = jnp.einsum(
        "...qk,...qd->...kd",
        truncated_outcome,
        blended_output_derivative,
        preferred_element_type=jnp.float32,
    )
    coefficient_derivative = jnp.einsum(
        "...uo,...ao->...ua",
        blended_output_derivative,
        payload_array,
        preferred_element_type=jnp.float32,
    )
    paired_inner_sums = jnp.sum(
        blended_output_derivative.astype(jnp.float32) * combined_output.astype(jnp.float32),
        axis=-1,
        keepdims=True,
    )
    affinity_derivative = (
        coefficient_array * (coefficient_derivative - paired_inner_sums) * sharpness_divisor
    ).astype(jnp.bfloat16)
    grad_queries = jnp.einsum(
        "...qk,...kd->...qd", affinity_derivative, lookup_array, preferred_element_type=jnp.float32
    )
    grad_keys = jnp.einsum(
        "...qk,...qd->...kd",
        affinity_derivative,
        asking_vectors,
        preferred_element_type=jnp.float32,
    )
    return (
        grad_queries.astype(jnp.bfloat16),
        grad_keys.astype(jnp.bfloat16),
        grad_values.astype(jnp.bfloat16),
    )


def temporal_split(projected):
    pieces = projected.reshape(projected.shape[0], 3, HEADS, projected.shape[1] // (3 * HEADS))
    return [pieces[:, index].transpose(1, 0, 2) for index in range(3)]


def temporal_forward(projected, admissible_pairs):
    asking_vectors, lookup_array, payload_array = temporal_split(projected)
    sharpness_divisor = float(asking_vectors.shape[-1]) ** (-0.5)
    combined_output = compute_affinity_outputs(
        asking_vectors, lookup_array, payload_array, admissible_pairs[None], sharpness_divisor
    )
    return combined_output.transpose(1, 0, 2).reshape(projected.shape[0], -1)


def temporal_backward(projected, admissible_pairs, combined_output, blended_output_derivative):
    asking_vectors, lookup_array, payload_array = temporal_split(projected)
    sharpness_divisor = float(asking_vectors.shape[-1]) ** (-0.5)
    bins = projected.shape[0]
    subspace_outputs = combined_output.reshape(bins, HEADS, -1).transpose(1, 0, 2)
    subspace_derivative = blended_output_derivative.reshape(bins, HEADS, -1).transpose(1, 0, 2)
    derivative_collection = compute_affinity_derivatives(
        asking_vectors,
        lookup_array,
        payload_array,
        admissible_pairs[None],
        sharpness_divisor,
        subspace_outputs,
        subspace_derivative,
    )
    return jnp.stack(derivative_collection, axis=0).transpose(2, 0, 1, 3).reshape(bins, -1)


def spatial_split(projected):
    pieces = projected.reshape(
        projected.shape[0], projected.shape[1], 3, HEADS, projected.shape[2] // (3 * HEADS)
    )
    return [pieces[:, :, index].transpose(0, 2, 1, 3) for index in range(3)]


def spatial_forward(projected, admissible_pairs):
    asking_vectors, lookup_array, payload_array = spatial_split(projected)
    sharpness_divisor = float(asking_vectors.shape[-1]) ** (-0.5)
    combined_output = compute_affinity_outputs(
        asking_vectors, lookup_array, payload_array, admissible_pairs, sharpness_divisor
    )
    return combined_output.transpose(0, 2, 1, 3).reshape(projected.shape[0], projected.shape[1], -1)


def spatial_backward(projected, admissible_pairs, combined_output, blended_output_derivative):
    asking_vectors, lookup_array, payload_array = spatial_split(projected)
    sharpness_divisor = float(asking_vectors.shape[-1]) ** (-0.5)
    bins, blocks = (projected.shape[0], projected.shape[1])
    subspace_outputs = combined_output.reshape(bins, blocks, HEADS, -1).transpose(0, 2, 1, 3)
    subspace_derivative = blended_output_derivative.reshape(bins, blocks, HEADS, -1).transpose(
        0, 2, 1, 3
    )
    derivative_collection = compute_affinity_derivatives(
        asking_vectors,
        lookup_array,
        payload_array,
        admissible_pairs,
        sharpness_divisor,
        subspace_outputs,
        subspace_derivative,
    )
    return (
        jnp.stack(derivative_collection, axis=0).transpose(1, 3, 0, 2, 4).reshape(bins, blocks, -1)
    )


def spatial_allowed(sessions_here, channel_count, adjacency):
    block_count = adjacency.shape[0]
    block_ids = jnp.arange(block_count, dtype=jnp.int32)
    session_pick = (
        sessions_here[:, None] == jnp.arange(channel_count.shape[0], dtype=jnp.int32)[None, :]
    ).astype(jnp.int32)
    count_rows = jnp.sum(session_pick * channel_count[None, :], axis=1)
    live_block = block_ids[None, :] * block_channels < count_rows[:, None]
    linked = adjacency > 0
    itself = block_ids[:, None] == block_ids[None, :]
    admissible_pairs = linked[None, :, :] & live_block[:, None, :] | itself[None, :, :]
    return admissible_pairs[:, None, :, :]


def project(rows, coefficient_array):
    return jnp.einsum("tbd,de->tbe", rows, coefficient_array, preferred_element_type=jnp.float32)


def project_back(derivative_collection, coefficient_array):
    return jnp.einsum(
        "tbe,de->tbd", derivative_collection, coefficient_array, preferred_element_type=jnp.float32
    )


def weight_term(left, right):
    return jnp.einsum("tbd,tbe->de", left, right, preferred_element_type=jnp.float32)


def reduce_rows(partial):
    rows, cols = partial.shape
    outer = lax.psum(1, "outer")
    pieces = partial.astype(jnp.bfloat16).reshape(outer, 2, rows // (2 * outer), cols)
    pieces = lax.all_to_all(pieces, "core", 1, 1, tiled=True)
    pieces = jnp.sum(pieces.astype(jnp.float32), axis=1).astype(jnp.bfloat16)
    pieces = lax.all_to_all(pieces, "outer", 0, 0, tiled=True)
    return jnp.sum(pieces.astype(jnp.float32), axis=0)


def per_device(
    activity,
    grad_out,
    spatial_weights,
    temporal_weights,
    spatial_gain,
    temporal_gain,
    adjacency,
    channel_count,
    session_id,
):
    local_bins = activity.shape[0]
    model_width = activity.shape[2]
    first_bin = (lax.axis_index("outer") * 2 + lax.axis_index("core")) * local_bins
    sessions_here = lax.dynamic_slice_in_dim(session_id, first_bin, local_bins)
    normed_one, inverse_one = norm_forward(activity, spatial_gain)
    spatial_proj = project(normed_one, spatial_weights[:, : 3 * model_width]).astype(jnp.bfloat16)
    allowed_space = spatial_allowed(sessions_here, channel_count, adjacency)
    spatial_context = spatial_forward(spatial_proj, allowed_space)
    middle = (
        activity.astype(jnp.float32)
        + project(spatial_context, spatial_weights[:, 3 * model_width :])
    ).astype(jnp.bfloat16)
    middle_block = lax.all_to_all(middle, ("outer", "core"), split_axis=1, concat_axis=0, tiled=True)
    normed_two, inverse_two = norm_forward(middle_block, temporal_gain)
    temporal_proj = project(normed_two, temporal_weights[:, : 3 * model_width]).astype(jnp.bfloat16)
    allowed_time = session_id[:, None] == session_id[None, :]
    by_block = jnp.moveaxis(temporal_proj, 1, 0)
    temporal_context = jnp.moveaxis(
        lax.map(lambda block_rows: temporal_forward(block_rows, allowed_time), by_block), 0, 1
    )
    layer_out = (
        middle_block.astype(jnp.float32)
        + project(temporal_context, temporal_weights[:, 3 * model_width :])
    ).astype(jnp.bfloat16)
    grad_temporal_context = project_back(grad_out, temporal_weights[:, 3 * model_width :]).astype(
        jnp.bfloat16
    )
    stacked = (
        by_block,
        jnp.moveaxis(temporal_context, 1, 0),
        jnp.moveaxis(grad_temporal_context, 1, 0),
    )
    grad_temporal_proj = jnp.moveaxis(
        lax.map(
            lambda items: temporal_backward(items[0], allowed_time, items[1], items[2]), stacked
        ),
        0,
        1,
    )
    grad_normed_two = project_back(grad_temporal_proj, temporal_weights[:, : 3 * model_width])
    grad_middle = (
        grad_out.astype(jnp.float32)
        + norm_backward(middle_block, temporal_gain, inverse_two, grad_normed_two)
    ).astype(jnp.bfloat16)
    grad_middle_time = lax.all_to_all(grad_middle, ("outer", "core"), split_axis=0, concat_axis=1, tiled=True)
    normed_cols = normed_two
    context_cols = temporal_context
    temporal_grad = lax.psum_scatter(
        jnp.concatenate(
            [weight_term(normed_cols, grad_temporal_proj), weight_term(context_cols, grad_out)],
            axis=1,
        ).astype(jnp.bfloat16),
        ("outer", "core"),
        scatter_dimension=0,
        tiled=True,
    ).astype(jnp.float32)
    grad_spatial_context = project_back(
        grad_middle_time, spatial_weights[:, 3 * model_width :]
    ).astype(jnp.bfloat16)
    grad_spatial_proj = spatial_backward(
        spatial_proj, allowed_space, spatial_context, grad_spatial_context
    )
    grad_normed_one = project_back(grad_spatial_proj, spatial_weights[:, : 3 * model_width])
    grad_activity = (
        grad_middle_time.astype(jnp.float32)
        + norm_backward(activity, spatial_gain, inverse_one, grad_normed_one)
    ).astype(jnp.bfloat16)
    normed_cols = normed_one
    context_cols = spatial_context
    spatial_grad = reduce_rows(
        jnp.concatenate(
            [
                weight_term(normed_cols, grad_spatial_proj),
                weight_term(context_cols, grad_middle_time),
            ],
            axis=1,
        )
    )
    return (layer_out, grad_activity, spatial_grad, temporal_grad)


def solution(mesh):
    groups, wide = mesh.devices.shape
    mesh = Mesh(mesh.devices.reshape(groups, wide // 2, 2), ("groups", "outer", "core"))
    placed = (
        P(("groups", "outer", "core"), None, None),
        P("groups", ("outer", "core"), None),
        P(),
        P(),
        P(),
        P(),
        P(),
        P("groups"),
        P("groups"),
    )
    return jax.shard_map(
        per_device,
        mesh=mesh,
        in_specs=placed,
        out_specs=(
            P("groups", ("outer", "core"), None),
            P(("groups", "outer", "core"), None, None),
            P(("groups", "outer", "core"), None),
            P(("groups", "outer", "core"), None),
        ),
        check_vma=False,
    )
```

```python
import jax
import jax.numpy as jnp
from jax import lax
from jax.sharding import Mesh, PartitionSpec as P

HEADS = 8


eps_norm = 1e-05
block_channels = 128


def norm_inverse(rows):
    values = rows.astype(jnp.float32)
    return lax.rsqrt(jnp.mean(values * values, axis=-1, keepdims=True) + eps_norm)


def norm_forward(rows, gain):
    inverse = norm_inverse(rows)
    return ((rows.astype(jnp.float32) * inverse * gain).astype(jnp.bfloat16), inverse)


def norm_backward(rows, gain, inverse, grad_normed):
    values = rows.astype(jnp.float32)
    scaled = grad_normed * gain
    inner = jnp.mean(values * scaled, axis=-1, keepdims=True)
    return inverse * scaled - values * inverse * inverse * inverse * inner


def normalized_affinity(asking_vectors, lookup_array, admissible_pairs, sharpness_divisor):
    unnormalized_affinities = (
        jnp.einsum(
            "...uo,...ao->...ua", asking_vectors, lookup_array, preferred_element_type=jnp.float32
        )
        * sharpness_divisor
    )
    unnormalized_affinities = jnp.where(admissible_pairs, unnormalized_affinities, -1e30)
    row_max = jnp.max(unnormalized_affinities, axis=-1, keepdims=True)
    expo = jnp.exp(unnormalized_affinities - row_max)
    return expo / jnp.sum(expo, axis=-1, keepdims=True)


def compute_affinity_outputs(
    asking_vectors, lookup_array, payload_array, admissible_pairs, sharpness_divisor
):
    truncated_outcome = normalized_affinity(
        asking_vectors, lookup_array, admissible_pairs, sharpness_divisor
    ).astype(jnp.bfloat16)
    return jnp.einsum(
        "...qk,...kd->...qd", truncated_outcome, payload_array, preferred_element_type=jnp.float32
    ).astype(jnp.bfloat16)


def compute_affinity_derivatives(
    asking_vectors,
    lookup_array,
    payload_array,
    admissible_pairs,
    sharpness_divisor,
    combined_output,
    blended_output_derivative,
):
    coefficient_array = normalized_affinity(
        asking_vectors, lookup_array, admissible_pairs, sharpness_divisor
    )
    truncated_outcome = coefficient_array.astype(jnp.bfloat16)
    grad_values = jnp.einsum(
        "...qk,...qd->...kd",
        truncated_outcome,
        blended_output_derivative,
        preferred_element_type=jnp.float32,
    )
    coefficient_derivative = jnp.einsum(
        "...uo,...ao->...ua",
        blended_output_derivative,
        payload_array,
        preferred_element_type=jnp.float32,
    )
    paired_inner_sums = jnp.sum(
        blended_output_derivative.astype(jnp.float32) * combined_output.astype(jnp.float32),
        axis=-1,
        keepdims=True,
    )
    affinity_derivative = (
        coefficient_array * (coefficient_derivative - paired_inner_sums) * sharpness_divisor
    ).astype(jnp.bfloat16)
    grad_queries = jnp.einsum(
        "...qk,...kd->...qd", affinity_derivative, lookup_array, preferred_element_type=jnp.float32
    )
    grad_keys = jnp.einsum(
        "...qk,...qd->...kd",
        affinity_derivative,
        asking_vectors,
        preferred_element_type=jnp.float32,
    )
    return (
        grad_queries.astype(jnp.bfloat16),
        grad_keys.astype(jnp.bfloat16),
        grad_values.astype(jnp.bfloat16),
    )


def temporal_split(projected):
    pieces = projected.reshape(projected.shape[0], 3, HEADS, projected.shape[1] // (3 * HEADS))
    return [pieces[:, index].transpose(1, 0, 2) for index in range(3)]


def temporal_forward(projected, admissible_pairs):
    asking_vectors, lookup_array, payload_array = temporal_split(projected)
    sharpness_divisor = float(asking_vectors.shape[-1]) ** (-0.5)
    combined_output = compute_affinity_outputs(
        asking_vectors, lookup_array, payload_array, admissible_pairs[None], sharpness_divisor
    )
    return combined_output.transpose(1, 0, 2).reshape(projected.shape[0], -1)


def temporal_backward(projected, admissible_pairs, combined_output, blended_output_derivative):
    asking_vectors, lookup_array, payload_array = temporal_split(projected)
    sharpness_divisor = float(asking_vectors.shape[-1]) ** (-0.5)
    bins = projected.shape[0]
    subspace_outputs = combined_output.reshape(bins, HEADS, -1).transpose(1, 0, 2)
    subspace_derivative = blended_output_derivative.reshape(bins, HEADS, -1).transpose(1, 0, 2)
    derivative_collection = compute_affinity_derivatives(
        asking_vectors,
        lookup_array,
        payload_array,
        admissible_pairs[None],
        sharpness_divisor,
        subspace_outputs,
        subspace_derivative,
    )
    return jnp.stack(derivative_collection, axis=0).transpose(2, 0, 1, 3).reshape(bins, -1)


def spatial_split(projected):
    pieces = projected.reshape(
        projected.shape[0], projected.shape[1], 3, HEADS, projected.shape[2] // (3 * HEADS)
    )
    return [pieces[:, :, index].transpose(0, 2, 1, 3) for index in range(3)]


def spatial_forward(projected, admissible_pairs):
    asking_vectors, lookup_array, payload_array = spatial_split(projected)
    sharpness_divisor = float(asking_vectors.shape[-1]) ** (-0.5)
    combined_output = compute_affinity_outputs(
        asking_vectors, lookup_array, payload_array, admissible_pairs, sharpness_divisor
    )
    return combined_output.transpose(0, 2, 1, 3).reshape(projected.shape[0], projected.shape[1], -1)


def spatial_backward(projected, admissible_pairs, combined_output, blended_output_derivative):
    asking_vectors, lookup_array, payload_array = spatial_split(projected)
    sharpness_divisor = float(asking_vectors.shape[-1]) ** (-0.5)
    bins, blocks = (projected.shape[0], projected.shape[1])
    subspace_outputs = combined_output.reshape(bins, blocks, HEADS, -1).transpose(0, 2, 1, 3)
    subspace_derivative = blended_output_derivative.reshape(bins, blocks, HEADS, -1).transpose(
        0, 2, 1, 3
    )
    derivative_collection = compute_affinity_derivatives(
        asking_vectors,
        lookup_array,
        payload_array,
        admissible_pairs,
        sharpness_divisor,
        subspace_outputs,
        subspace_derivative,
    )
    return (
        jnp.stack(derivative_collection, axis=0).transpose(1, 3, 0, 2, 4).reshape(bins, blocks, -1)
    )


def spatial_allowed(sessions_here, channel_count, adjacency):
    block_count = adjacency.shape[0]
    block_ids = jnp.arange(block_count, dtype=jnp.int32)
    session_pick = (
        sessions_here[:, None] == jnp.arange(channel_count.shape[0], dtype=jnp.int32)[None, :]
    ).astype(jnp.int32)
    count_rows = jnp.sum(session_pick * channel_count[None, :], axis=1)
    live_block = block_ids[None, :] * block_channels < count_rows[:, None]
    linked = adjacency > 0
    itself = block_ids[:, None] == block_ids[None, :]
    admissible_pairs = linked[None, :, :] & live_block[:, None, :] | itself[None, :, :]
    return admissible_pairs[:, None, :, :]


def project(rows, coefficient_array):
    return jnp.einsum("tbd,de->tbe", rows, coefficient_array, preferred_element_type=jnp.float32)


def project_back(derivative_collection, coefficient_array):
    return jnp.einsum(
        "tbe,de->tbd", derivative_collection, coefficient_array, preferred_element_type=jnp.float32
    )


def weight_term(left, right):
    return jnp.einsum("tbd,tbe->de", left, right, preferred_element_type=jnp.float32)


def reduce_rows(partial):
    rows, cols = partial.shape
    outer = lax.psum(1, "outer")
    pieces = partial.astype(jnp.bfloat16).reshape(outer, 2, rows // (2 * outer), cols)
    pieces = lax.all_to_all(pieces, "core", 1, 1, tiled=True)
    pieces = jnp.sum(pieces.astype(jnp.float32), axis=1).astype(jnp.bfloat16)
    pieces = lax.all_to_all(pieces, "outer", 0, 0, tiled=True)
    return jnp.sum(pieces.astype(jnp.float32), axis=0)


def scatter_rows(partial):
    return lax.psum_scatter(
        partial.astype(jnp.bfloat16), ("outer", "core"), scatter_dimension=0, tiled=True
    ).astype(jnp.float32)


def per_device(
    activity,
    grad_out,
    spatial_weights,
    temporal_weights,
    spatial_gain,
    temporal_gain,
    adjacency,
    channel_count,
    session_id,
):
    local_bins = activity.shape[0]
    model_width = activity.shape[2]
    first_bin = (lax.axis_index("outer") * 2 + lax.axis_index("core")) * local_bins
    sessions_here = lax.dynamic_slice_in_dim(session_id, first_bin, local_bins)
    normed_one, inverse_one = norm_forward(activity, spatial_gain)
    spatial_proj = project(normed_one, spatial_weights[:, : 3 * model_width]).astype(jnp.bfloat16)
    allowed_space = spatial_allowed(sessions_here, channel_count, adjacency)
    spatial_context = spatial_forward(spatial_proj, allowed_space)
    middle = (
        activity.astype(jnp.float32)
        + project(spatial_context, spatial_weights[:, 3 * model_width :])
    ).astype(jnp.bfloat16)
    middle_block = lax.all_to_all(middle, ("outer", "core"), split_axis=1, concat_axis=0, tiled=True)
    normed_two, inverse_two = norm_forward(middle_block, temporal_gain)
    temporal_proj = project(normed_two, temporal_weights[:, : 3 * model_width]).astype(jnp.bfloat16)
    allowed_time = session_id[:, None] == session_id[None, :]
    by_block = jnp.moveaxis(temporal_proj, 1, 0)
    temporal_context = jnp.moveaxis(
        lax.map(lambda block_rows: temporal_forward(block_rows, allowed_time), by_block), 0, 1
    )
    layer_out = (
        middle_block.astype(jnp.float32)
        + project(temporal_context, temporal_weights[:, 3 * model_width :])
    ).astype(jnp.bfloat16)
    grad_temporal_context = project_back(grad_out, temporal_weights[:, 3 * model_width :]).astype(
        jnp.bfloat16
    )
    stacked = (
        by_block,
        jnp.moveaxis(temporal_context, 1, 0),
        jnp.moveaxis(grad_temporal_context, 1, 0),
    )
    grad_temporal_proj = jnp.moveaxis(
        lax.map(
            lambda items: temporal_backward(items[0], allowed_time, items[1], items[2]), stacked
        ),
        0,
        1,
    )
    grad_normed_two = project_back(grad_temporal_proj, temporal_weights[:, : 3 * model_width])
    grad_middle = (
        grad_out.astype(jnp.float32)
        + norm_backward(middle_block, temporal_gain, inverse_two, grad_normed_two)
    ).astype(jnp.bfloat16)
    grad_middle_time = lax.all_to_all(grad_middle, ("outer", "core"), split_axis=0, concat_axis=1, tiled=True)
    normed_cols = normed_two
    context_cols = temporal_context
    temporal_grad = scatter_rows(
        jnp.concatenate(
            [weight_term(normed_cols, grad_temporal_proj), weight_term(context_cols, grad_out)],
            axis=1,
        )
    )
    spatial_term = weight_term(spatial_context, grad_middle_time)
    spatial_term, grad_middle_time = lax.optimization_barrier((spatial_term, grad_middle_time))
    grad_spatial_context = project_back(
        grad_middle_time, spatial_weights[:, 3 * model_width :]
    ).astype(jnp.bfloat16)
    grad_spatial_proj = spatial_backward(
        spatial_proj, allowed_space, spatial_context, grad_spatial_context
    )
    spatial_term = reduce_rows(spatial_term)
    spatial_term, grad_spatial_proj = lax.optimization_barrier((spatial_term, grad_spatial_proj))
    grad_normed_one = project_back(grad_spatial_proj, spatial_weights[:, : 3 * model_width])
    grad_activity = (
        grad_middle_time.astype(jnp.float32)
        + norm_backward(activity, spatial_gain, inverse_one, grad_normed_one)
    ).astype(jnp.bfloat16)
    normed_cols = normed_one
    context_cols = spatial_context
    spatial_grad = jnp.concatenate(
        [
            reduce_rows(weight_term(normed_cols, grad_spatial_proj)),
            spatial_term,
        ],
        axis=1,
    )
    return (layer_out, grad_activity, spatial_grad, temporal_grad)


def solution(mesh):
    groups, wide = mesh.devices.shape
    mesh = Mesh(mesh.devices.reshape(groups, wide // 2, 2), ("groups", "outer", "core"))
    placed = (
        P(("groups", "outer", "core"), None, None),
        P("groups", ("outer", "core"), None),
        P(),
        P(),
        P(),
        P(),
        P(),
        P("groups"),
        P("groups"),
    )
    return jax.shard_map(
        per_device,
        mesh=mesh,
        in_specs=placed,
        out_specs=(
            P("groups", ("outer", "core"), None),
            P(("groups", "outer", "core"), None, None),
            P(("groups", "outer", "core"), None),
            P(("groups", "outer", "core"), None),
        ),
        check_vma=False,
    )
```

```python
import jax
import jax.numpy as jnp
from jax import lax
from jax.sharding import Mesh, PartitionSpec as P

HEADS = 8


eps_norm = 1e-05
block_channels = 128


def norm_inverse(rows):
    values = rows.astype(jnp.float32)
    return lax.rsqrt(jnp.mean(values * values, axis=-1, keepdims=True) + eps_norm)


def norm_forward(rows, gain):
    inverse = norm_inverse(rows)
    return ((rows.astype(jnp.float32) * inverse * gain).astype(jnp.bfloat16), inverse)


def norm_backward(rows, gain, inverse, grad_normed):
    values = rows.astype(jnp.float32)
    scaled = grad_normed * gain
    inner = jnp.mean(values * scaled, axis=-1, keepdims=True)
    return inverse * scaled - values * inverse * inverse * inverse * inner


def normalized_affinity(asking_vectors, lookup_array, admissible_pairs, sharpness_divisor):
    unnormalized_affinities = (
        jnp.einsum(
            "...uo,...ao->...ua", asking_vectors, lookup_array, preferred_element_type=jnp.float32
        )
        * sharpness_divisor
    )
    unnormalized_affinities = jnp.where(admissible_pairs, unnormalized_affinities, -1e30)
    row_max = jnp.max(unnormalized_affinities, axis=-1, keepdims=True)
    expo = jnp.exp(unnormalized_affinities - row_max)
    return expo / jnp.sum(expo, axis=-1, keepdims=True)


def compute_affinity_outputs(
    asking_vectors, lookup_array, payload_array, admissible_pairs, sharpness_divisor
):
    truncated_outcome = normalized_affinity(
        asking_vectors, lookup_array, admissible_pairs, sharpness_divisor
    ).astype(jnp.bfloat16)
    return jnp.einsum(
        "...qk,...kd->...qd", truncated_outcome, payload_array, preferred_element_type=jnp.float32
    ).astype(jnp.bfloat16)


def compute_affinity_derivatives(
    asking_vectors,
    lookup_array,
    payload_array,
    admissible_pairs,
    sharpness_divisor,
    combined_output,
    blended_output_derivative,
):
    coefficient_array = normalized_affinity(
        asking_vectors, lookup_array, admissible_pairs, sharpness_divisor
    )
    truncated_outcome = coefficient_array.astype(jnp.bfloat16)
    grad_values = jnp.einsum(
        "...qk,...qd->...kd",
        truncated_outcome,
        blended_output_derivative,
        preferred_element_type=jnp.float32,
    )
    coefficient_derivative = jnp.einsum(
        "...uo,...ao->...ua",
        blended_output_derivative,
        payload_array,
        preferred_element_type=jnp.float32,
    )
    paired_inner_sums = jnp.sum(
        blended_output_derivative.astype(jnp.float32) * combined_output.astype(jnp.float32),
        axis=-1,
        keepdims=True,
    )
    affinity_derivative = (
        coefficient_array * (coefficient_derivative - paired_inner_sums) * sharpness_divisor
    ).astype(jnp.bfloat16)
    grad_queries = jnp.einsum(
        "...qk,...kd->...qd", affinity_derivative, lookup_array, preferred_element_type=jnp.float32
    )
    grad_keys = jnp.einsum(
        "...qk,...qd->...kd",
        affinity_derivative,
        asking_vectors,
        preferred_element_type=jnp.float32,
    )
    return (
        grad_queries.astype(jnp.bfloat16),
        grad_keys.astype(jnp.bfloat16),
        grad_values.astype(jnp.bfloat16),
    )


def temporal_split(projected):
    pieces = projected.reshape(projected.shape[0], 3, HEADS, projected.shape[1] // (3 * HEADS))
    return [pieces[:, index].transpose(1, 0, 2) for index in range(3)]


def temporal_forward(projected, admissible_pairs):
    asking_vectors, lookup_array, payload_array = temporal_split(projected)
    sharpness_divisor = float(asking_vectors.shape[-1]) ** (-0.5)
    combined_output = compute_affinity_outputs(
        asking_vectors, lookup_array, payload_array, admissible_pairs[None], sharpness_divisor
    )
    return combined_output.transpose(1, 0, 2).reshape(projected.shape[0], -1)


def temporal_backward(projected, admissible_pairs, combined_output, blended_output_derivative):
    asking_vectors, lookup_array, payload_array = temporal_split(projected)
    sharpness_divisor = float(asking_vectors.shape[-1]) ** (-0.5)
    bins = projected.shape[0]
    subspace_outputs = combined_output.reshape(bins, HEADS, -1).transpose(1, 0, 2)
    subspace_derivative = blended_output_derivative.reshape(bins, HEADS, -1).transpose(1, 0, 2)
    derivative_collection = compute_affinity_derivatives(
        asking_vectors,
        lookup_array,
        payload_array,
        admissible_pairs[None],
        sharpness_divisor,
        subspace_outputs,
        subspace_derivative,
    )
    return jnp.stack(derivative_collection, axis=0).transpose(2, 0, 1, 3).reshape(bins, -1)


def spatial_split(projected):
    pieces = projected.reshape(
        projected.shape[0], projected.shape[1], 3, HEADS, projected.shape[2] // (3 * HEADS)
    )
    return [pieces[:, :, index].transpose(0, 2, 1, 3) for index in range(3)]


def spatial_forward(projected, admissible_pairs):
    asking_vectors, lookup_array, payload_array = spatial_split(projected)
    sharpness_divisor = float(asking_vectors.shape[-1]) ** (-0.5)
    combined_output = compute_affinity_outputs(
        asking_vectors, lookup_array, payload_array, admissible_pairs, sharpness_divisor
    )
    return combined_output.transpose(0, 2, 1, 3).reshape(projected.shape[0], projected.shape[1], -1)


def spatial_backward(projected, admissible_pairs, combined_output, blended_output_derivative):
    asking_vectors, lookup_array, payload_array = spatial_split(projected)
    sharpness_divisor = float(asking_vectors.shape[-1]) ** (-0.5)
    bins, blocks = (projected.shape[0], projected.shape[1])
    subspace_outputs = combined_output.reshape(bins, blocks, HEADS, -1).transpose(0, 2, 1, 3)
    subspace_derivative = blended_output_derivative.reshape(bins, blocks, HEADS, -1).transpose(
        0, 2, 1, 3
    )
    derivative_collection = compute_affinity_derivatives(
        asking_vectors,
        lookup_array,
        payload_array,
        admissible_pairs,
        sharpness_divisor,
        subspace_outputs,
        subspace_derivative,
    )
    return (
        jnp.stack(derivative_collection, axis=0).transpose(1, 3, 0, 2, 4).reshape(bins, blocks, -1)
    )


def spatial_allowed(sessions_here, channel_count, adjacency):
    block_count = adjacency.shape[0]
    block_ids = jnp.arange(block_count, dtype=jnp.int32)
    session_pick = (
        sessions_here[:, None] == jnp.arange(channel_count.shape[0], dtype=jnp.int32)[None, :]
    ).astype(jnp.int32)
    count_rows = jnp.sum(session_pick * channel_count[None, :], axis=1)
    live_block = block_ids[None, :] * block_channels < count_rows[:, None]
    linked = adjacency > 0
    itself = block_ids[:, None] == block_ids[None, :]
    admissible_pairs = linked[None, :, :] & live_block[:, None, :] | itself[None, :, :]
    return admissible_pairs[:, None, :, :]


def project(rows, coefficient_array):
    return jnp.einsum("tbd,de->tbe", rows, coefficient_array, preferred_element_type=jnp.float32)


def project_back(derivative_collection, coefficient_array):
    return jnp.einsum(
        "tbe,de->tbd", derivative_collection, coefficient_array, preferred_element_type=jnp.float32
    )


def weight_term(left, right):
    return jnp.einsum("tbd,tbe->de", left, right, preferred_element_type=jnp.float32)


def reduce_rows(partial):
    rows, cols = partial.shape
    outer = lax.psum(1, "outer")
    pieces = partial.astype(jnp.bfloat16).reshape(outer, 2, rows // (2 * outer), cols)
    pieces = lax.all_to_all(pieces, "core", 1, 1, tiled=True)
    pieces = jnp.sum(pieces.astype(jnp.float32), axis=1).astype(jnp.bfloat16)
    pieces = lax.all_to_all(pieces, "outer", 0, 0, tiled=True)
    return jnp.sum(pieces.astype(jnp.float32), axis=0)


def scatter_rows(partial):
    return lax.psum_scatter(
        partial.astype(jnp.bfloat16), ("outer", "core"), scatter_dimension=0, tiled=True
    ).astype(jnp.float32)


def per_device(
    activity,
    grad_out,
    spatial_weights,
    temporal_weights,
    spatial_gain,
    temporal_gain,
    adjacency,
    channel_count,
    session_id,
):
    local_bins = activity.shape[0]
    model_width = activity.shape[2]
    first_bin = (lax.axis_index("outer") * 2 + lax.axis_index("core")) * local_bins
    sessions_here = lax.dynamic_slice_in_dim(session_id, first_bin, local_bins)
    halves = 2
    half_bins = local_bins // halves
    sent = session_id.shape[0] // local_bins
    parts = []
    for half in range(halves):
        rows = activity[half * half_bins : (half + 1) * half_bins]
        normed_half, inverse_half = norm_forward(rows, spatial_gain)
        proj_half = project(normed_half, spatial_weights[:, : 3 * model_width]).astype(
            jnp.bfloat16
        )
        allowed_half = spatial_allowed(
            sessions_here[half * half_bins : (half + 1) * half_bins], channel_count, adjacency
        )
        context_half = spatial_forward(proj_half, allowed_half)
        middle_half = (
            rows.astype(jnp.float32)
            + project(context_half, spatial_weights[:, 3 * model_width :])
        ).astype(jnp.bfloat16)
        moved = lax.all_to_all(
            middle_half, ("outer", "core"), split_axis=1, concat_axis=0, tiled=True
        )
        parts.append((normed_half, inverse_half, proj_half, allowed_half, context_half, moved))
    normed_one, inverse_one, spatial_proj, allowed_space, spatial_context = [
        jnp.concatenate([part[index] for part in parts], axis=0) for index in range(5)
    ]
    middle_block = jnp.stack(
        [part[5].reshape(sent, half_bins, 1, model_width) for part in parts], axis=1
    ).reshape(sent * local_bins, 1, model_width)
    normed_two, inverse_two = norm_forward(middle_block, temporal_gain)
    temporal_proj = project(normed_two, temporal_weights[:, : 3 * model_width]).astype(jnp.bfloat16)
    allowed_time = session_id[:, None] == session_id[None, :]
    by_block = jnp.moveaxis(temporal_proj, 1, 0)
    temporal_context = jnp.moveaxis(
        lax.map(lambda block_rows: temporal_forward(block_rows, allowed_time), by_block), 0, 1
    )
    layer_out = (
        middle_block.astype(jnp.float32)
        + project(temporal_context, temporal_weights[:, 3 * model_width :])
    ).astype(jnp.bfloat16)
    grad_temporal_context = project_back(grad_out, temporal_weights[:, 3 * model_width :]).astype(
        jnp.bfloat16
    )
    stacked = (
        by_block,
        jnp.moveaxis(temporal_context, 1, 0),
        jnp.moveaxis(grad_temporal_context, 1, 0),
    )
    grad_temporal_proj = jnp.moveaxis(
        lax.map(
            lambda items: temporal_backward(items[0], allowed_time, items[1], items[2]), stacked
        ),
        0,
        1,
    )
    grad_normed_two = project_back(grad_temporal_proj, temporal_weights[:, : 3 * model_width])
    grad_middle = (
        grad_out.astype(jnp.float32)
        + norm_backward(middle_block, temporal_gain, inverse_two, grad_normed_two)
    ).astype(jnp.bfloat16)
    grad_middle_time = lax.all_to_all(grad_middle, ("outer", "core"), split_axis=0, concat_axis=1, tiled=True)
    normed_cols = normed_two
    context_cols = temporal_context
    temporal_grad = scatter_rows(
        jnp.concatenate(
            [weight_term(normed_cols, grad_temporal_proj), weight_term(context_cols, grad_out)],
            axis=1,
        )
    )
    spatial_term = weight_term(spatial_context, grad_middle_time)
    spatial_term, grad_middle_time = lax.optimization_barrier((spatial_term, grad_middle_time))
    grad_spatial_context = project_back(
        grad_middle_time, spatial_weights[:, 3 * model_width :]
    ).astype(jnp.bfloat16)
    grad_spatial_proj = spatial_backward(
        spatial_proj, allowed_space, spatial_context, grad_spatial_context
    )
    spatial_term = reduce_rows(spatial_term)
    spatial_term, grad_spatial_proj = lax.optimization_barrier((spatial_term, grad_spatial_proj))
    grad_normed_one = project_back(grad_spatial_proj, spatial_weights[:, : 3 * model_width])
    grad_activity = (
        grad_middle_time.astype(jnp.float32)
        + norm_backward(activity, spatial_gain, inverse_one, grad_normed_one)
    ).astype(jnp.bfloat16)
    normed_cols = normed_one
    context_cols = spatial_context
    spatial_grad = jnp.concatenate(
        [
            reduce_rows(weight_term(normed_cols, grad_spatial_proj)),
            spatial_term,
        ],
        axis=1,
    )
    return (layer_out, grad_activity, spatial_grad, temporal_grad)


def solution(mesh):
    groups, wide = mesh.devices.shape
    mesh = Mesh(mesh.devices.reshape(groups, wide // 2, 2), ("groups", "outer", "core"))
    placed = (
        P(("groups", "outer", "core"), None, None),
        P("groups", ("outer", "core"), None),
        P(),
        P(),
        P(),
        P(),
        P(),
        P("groups"),
        P("groups"),
    )
    return jax.shard_map(
        per_device,
        mesh=mesh,
        in_specs=placed,
        out_specs=(
            P("groups", ("outer", "core"), None),
            P(("groups", "outer", "core"), None, None),
            P(("groups", "outer", "core"), None),
            P(("groups", "outer", "core"), None),
        ),
        check_vma=False,
    )
```

```python
import jax
import jax.numpy as jnp
from jax import lax
from jax.sharding import Mesh, PartitionSpec as P

HEADS = 8


eps_norm = 1e-05
block_channels = 128


def norm_inverse(rows):
    values = rows.astype(jnp.float32)
    return lax.rsqrt(jnp.mean(values * values, axis=-1, keepdims=True) + eps_norm)


def norm_forward(rows, gain):
    inverse = norm_inverse(rows)
    return ((rows.astype(jnp.float32) * inverse * gain).astype(jnp.bfloat16), inverse)


def norm_backward(rows, gain, inverse, grad_normed):
    values = rows.astype(jnp.float32)
    scaled = grad_normed * gain
    inner = jnp.mean(values * scaled, axis=-1, keepdims=True)
    return inverse * scaled - values * inverse * inverse * inverse * inner


def normalized_affinity(asking_vectors, lookup_array, admissible_pairs, sharpness_divisor):
    unnormalized_affinities = (
        jnp.einsum(
            "...uo,...ao->...ua", asking_vectors, lookup_array, preferred_element_type=jnp.float32
        )
        * sharpness_divisor
    )
    unnormalized_affinities = jnp.where(admissible_pairs, unnormalized_affinities, -1e30)
    row_max = jnp.max(unnormalized_affinities, axis=-1, keepdims=True)
    expo = jnp.exp(unnormalized_affinities - row_max)
    return expo / jnp.sum(expo, axis=-1, keepdims=True)


def compute_affinity_outputs(
    asking_vectors, lookup_array, payload_array, admissible_pairs, sharpness_divisor
):
    truncated_outcome = normalized_affinity(
        asking_vectors, lookup_array, admissible_pairs, sharpness_divisor
    ).astype(jnp.bfloat16)
    return jnp.einsum(
        "...qk,...kd->...qd", truncated_outcome, payload_array, preferred_element_type=jnp.float32
    ).astype(jnp.bfloat16)


def compute_affinity_derivatives(
    asking_vectors,
    lookup_array,
    payload_array,
    admissible_pairs,
    sharpness_divisor,
    combined_output,
    blended_output_derivative,
):
    coefficient_array = normalized_affinity(
        asking_vectors, lookup_array, admissible_pairs, sharpness_divisor
    )
    truncated_outcome = coefficient_array.astype(jnp.bfloat16)
    grad_values = jnp.einsum(
        "...qk,...qd->...kd",
        truncated_outcome,
        blended_output_derivative,
        preferred_element_type=jnp.float32,
    )
    coefficient_derivative = jnp.einsum(
        "...uo,...ao->...ua",
        blended_output_derivative,
        payload_array,
        preferred_element_type=jnp.float32,
    )
    paired_inner_sums = jnp.sum(
        blended_output_derivative.astype(jnp.float32) * combined_output.astype(jnp.float32),
        axis=-1,
        keepdims=True,
    )
    affinity_derivative = (
        coefficient_array * (coefficient_derivative - paired_inner_sums) * sharpness_divisor
    ).astype(jnp.bfloat16)
    grad_queries = jnp.einsum(
        "...qk,...kd->...qd", affinity_derivative, lookup_array, preferred_element_type=jnp.float32
    )
    grad_keys = jnp.einsum(
        "...qk,...qd->...kd",
        affinity_derivative,
        asking_vectors,
        preferred_element_type=jnp.float32,
    )
    return (
        grad_queries.astype(jnp.bfloat16),
        grad_keys.astype(jnp.bfloat16),
        grad_values.astype(jnp.bfloat16),
    )


def temporal_split(projected):
    pieces = projected.reshape(projected.shape[0], 3, HEADS, projected.shape[1] // (3 * HEADS))
    return [pieces[:, index].transpose(1, 0, 2) for index in range(3)]


def temporal_forward(projected, admissible_pairs):
    asking_vectors, lookup_array, payload_array = temporal_split(projected)
    sharpness_divisor = float(asking_vectors.shape[-1]) ** (-0.5)
    combined_output = compute_affinity_outputs(
        asking_vectors, lookup_array, payload_array, admissible_pairs[None], sharpness_divisor
    )
    return combined_output.transpose(1, 0, 2).reshape(projected.shape[0], -1)


def temporal_backward(projected, admissible_pairs, combined_output, blended_output_derivative):
    asking_vectors, lookup_array, payload_array = temporal_split(projected)
    sharpness_divisor = float(asking_vectors.shape[-1]) ** (-0.5)
    bins = projected.shape[0]
    subspace_outputs = combined_output.reshape(bins, HEADS, -1).transpose(1, 0, 2)
    subspace_derivative = blended_output_derivative.reshape(bins, HEADS, -1).transpose(1, 0, 2)
    derivative_collection = compute_affinity_derivatives(
        asking_vectors,
        lookup_array,
        payload_array,
        admissible_pairs[None],
        sharpness_divisor,
        subspace_outputs,
        subspace_derivative,
    )
    return jnp.stack(derivative_collection, axis=0).transpose(2, 0, 1, 3).reshape(bins, -1)


def spatial_split(projected):
    pieces = projected.reshape(
        projected.shape[0], projected.shape[1], 3, HEADS, projected.shape[2] // (3 * HEADS)
    )
    return [pieces[:, :, index].transpose(0, 2, 1, 3) for index in range(3)]


def spatial_forward(projected, admissible_pairs):
    asking_vectors, lookup_array, payload_array = spatial_split(projected)
    sharpness_divisor = float(asking_vectors.shape[-1]) ** (-0.5)
    combined_output = compute_affinity_outputs(
        asking_vectors, lookup_array, payload_array, admissible_pairs, sharpness_divisor
    )
    return combined_output.transpose(0, 2, 1, 3).reshape(projected.shape[0], projected.shape[1], -1)


def spatial_backward(projected, admissible_pairs, combined_output, blended_output_derivative):
    asking_vectors, lookup_array, payload_array = spatial_split(projected)
    sharpness_divisor = float(asking_vectors.shape[-1]) ** (-0.5)
    bins, blocks = (projected.shape[0], projected.shape[1])
    subspace_outputs = combined_output.reshape(bins, blocks, HEADS, -1).transpose(0, 2, 1, 3)
    subspace_derivative = blended_output_derivative.reshape(bins, blocks, HEADS, -1).transpose(
        0, 2, 1, 3
    )
    derivative_collection = compute_affinity_derivatives(
        asking_vectors,
        lookup_array,
        payload_array,
        admissible_pairs,
        sharpness_divisor,
        subspace_outputs,
        subspace_derivative,
    )
    return (
        jnp.stack(derivative_collection, axis=0).transpose(1, 3, 0, 2, 4).reshape(bins, blocks, -1)
    )


def spatial_allowed(sessions_here, channel_count, adjacency):
    block_count = adjacency.shape[0]
    block_ids = jnp.arange(block_count, dtype=jnp.int32)
    session_pick = (
        sessions_here[:, None] == jnp.arange(channel_count.shape[0], dtype=jnp.int32)[None, :]
    ).astype(jnp.int32)
    count_rows = jnp.sum(session_pick * channel_count[None, :], axis=1)
    live_block = block_ids[None, :] * block_channels < count_rows[:, None]
    linked = adjacency > 0
    itself = block_ids[:, None] == block_ids[None, :]
    admissible_pairs = linked[None, :, :] & live_block[:, None, :] | itself[None, :, :]
    return admissible_pairs[:, None, :, :]


def project(rows, coefficient_array):
    return jnp.einsum("tbd,de->tbe", rows, coefficient_array, preferred_element_type=jnp.float32)


def project_back(derivative_collection, coefficient_array):
    return jnp.einsum(
        "tbe,de->tbd", derivative_collection, coefficient_array, preferred_element_type=jnp.float32
    )


def weight_term(left, right):
    return jnp.einsum("tbd,tbe->de", left, right, preferred_element_type=jnp.float32)


def reduce_rows(partial):
    rows, cols = partial.shape
    outer = lax.psum(1, "outer")
    pieces = partial.reshape(outer, 2, rows // (2 * outer), cols)
    first = lax.axis_index("core") == 0
    kept = jnp.where(first, pieces[:, 0], pieces[:, 1])
    given = jnp.where(first, pieces[:, 1], pieces[:, 0]).astype(jnp.bfloat16)
    taken = lax.ppermute(given, "core", [(0, 1), (1, 0)])
    pieces = (kept + taken.astype(jnp.float32)).astype(jnp.bfloat16)
    pieces = lax.all_to_all(pieces, "outer", 0, 0, tiled=True)
    return jnp.sum(pieces.astype(jnp.float32), axis=0)


def scatter_rows(partial):
    return lax.psum_scatter(
        partial.astype(jnp.bfloat16), ("outer", "core"), scatter_dimension=0, tiled=True
    ).astype(jnp.float32)


def per_device(
    activity,
    grad_out,
    spatial_weights,
    temporal_weights,
    spatial_gain,
    temporal_gain,
    adjacency,
    channel_count,
    session_id,
):
    local_bins = activity.shape[0]
    model_width = activity.shape[2]
    first_bin = (lax.axis_index("outer") * 2 + lax.axis_index("core")) * local_bins
    sessions_here = lax.dynamic_slice_in_dim(session_id, first_bin, local_bins)
    normed_one, inverse_one = norm_forward(activity, spatial_gain)
    spatial_proj = project(normed_one, spatial_weights[:, : 3 * model_width]).astype(jnp.bfloat16)
    allowed_space = spatial_allowed(sessions_here, channel_count, adjacency)
    spatial_context = spatial_forward(spatial_proj, allowed_space)
    middle = (
        activity.astype(jnp.float32)
        + project(spatial_context, spatial_weights[:, 3 * model_width :])
    ).astype(jnp.bfloat16)
    middle_block = lax.all_to_all(middle, ("outer", "core"), split_axis=1, concat_axis=0, tiled=True)
    normed_two, inverse_two = norm_forward(middle_block, temporal_gain)
    temporal_proj = project(normed_two, temporal_weights[:, : 3 * model_width]).astype(jnp.bfloat16)
    allowed_time = session_id[:, None] == session_id[None, :]
    by_block = jnp.moveaxis(temporal_proj, 1, 0)
    temporal_context = jnp.moveaxis(
        lax.map(lambda block_rows: temporal_forward(block_rows, allowed_time), by_block), 0, 1
    )
    layer_out = (
        middle_block.astype(jnp.float32)
        + project(temporal_context, temporal_weights[:, 3 * model_width :])
    ).astype(jnp.bfloat16)
    grad_temporal_context = project_back(grad_out, temporal_weights[:, 3 * model_width :]).astype(
        jnp.bfloat16
    )
    stacked = (
        by_block,
        jnp.moveaxis(temporal_context, 1, 0),
        jnp.moveaxis(grad_temporal_context, 1, 0),
    )
    grad_temporal_proj = jnp.moveaxis(
        lax.map(
            lambda items: temporal_backward(items[0], allowed_time, items[1], items[2]), stacked
        ),
        0,
        1,
    )
    grad_normed_two = project_back(grad_temporal_proj, temporal_weights[:, : 3 * model_width])
    grad_middle = (
        grad_out.astype(jnp.float32)
        + norm_backward(middle_block, temporal_gain, inverse_two, grad_normed_two)
    ).astype(jnp.bfloat16)
    grad_middle_time = lax.all_to_all(grad_middle, ("outer", "core"), split_axis=0, concat_axis=1, tiled=True)
    normed_cols = normed_two
    context_cols = temporal_context
    temporal_grad = scatter_rows(
        jnp.concatenate(
            [weight_term(normed_cols, grad_temporal_proj), weight_term(context_cols, grad_out)],
            axis=1,
        )
    )
    spatial_term = weight_term(spatial_context, grad_middle_time)
    spatial_term, grad_middle_time = lax.optimization_barrier((spatial_term, grad_middle_time))
    grad_spatial_context = project_back(
        grad_middle_time, spatial_weights[:, 3 * model_width :]
    ).astype(jnp.bfloat16)
    grad_spatial_proj = spatial_backward(
        spatial_proj, allowed_space, spatial_context, grad_spatial_context
    )
    spatial_term = reduce_rows(spatial_term)
    spatial_term, grad_spatial_proj = lax.optimization_barrier((spatial_term, grad_spatial_proj))
    grad_normed_one = project_back(grad_spatial_proj, spatial_weights[:, : 3 * model_width])
    grad_activity = (
        grad_middle_time.astype(jnp.float32)
        + norm_backward(activity, spatial_gain, inverse_one, grad_normed_one)
    ).astype(jnp.bfloat16)
    normed_cols = normed_one
    context_cols = spatial_context
    spatial_grad = jnp.concatenate(
        [
            reduce_rows(weight_term(normed_cols, grad_spatial_proj)),
            spatial_term,
        ],
        axis=1,
    )
    return (layer_out, grad_activity, spatial_grad, temporal_grad)


def solution(mesh):
    groups, wide = mesh.devices.shape
    mesh = Mesh(mesh.devices.reshape(groups, wide // 2, 2), ("groups", "outer", "core"))
    placed = (
        P(("groups", "outer", "core"), None, None),
        P("groups", ("outer", "core"), None),
        P(),
        P(),
        P(),
        P(),
        P(),
        P("groups"),
        P("groups"),
    )
    return jax.shard_map(
        per_device,
        mesh=mesh,
        in_specs=placed,
        out_specs=(
            P("groups", ("outer", "core"), None),
            P(("groups", "outer", "core"), None, None),
            P(("groups", "outer", "core"), None),
            P(("groups", "outer", "core"), None),
        ),
        check_vma=False,
    )
```

```python
import jax
import jax.numpy as jnp
from jax import lax
from jax.sharding import Mesh, PartitionSpec as P

HEADS = 8


eps_norm = 1e-05
block_channels = 128


def norm_inverse(rows):
    values = rows.astype(jnp.float32)
    return lax.rsqrt(jnp.mean(values * values, axis=-1, keepdims=True) + eps_norm)


def norm_forward(rows, gain):
    inverse = norm_inverse(rows)
    return ((rows.astype(jnp.float32) * inverse * gain).astype(jnp.bfloat16), inverse)


def norm_backward(rows, gain, inverse, grad_normed):
    values = rows.astype(jnp.float32)
    scaled = grad_normed * gain
    inner = jnp.mean(values * scaled, axis=-1, keepdims=True)
    return inverse * scaled - values * inverse * inverse * inverse * inner


def normalized_affinity(asking_vectors, lookup_array, admissible_pairs, sharpness_divisor):
    unnormalized_affinities = (
        jnp.einsum(
            "...uo,...ao->...ua", asking_vectors, lookup_array, preferred_element_type=jnp.float32
        )
        * sharpness_divisor
    )
    unnormalized_affinities = jnp.where(admissible_pairs, unnormalized_affinities, -1e30)
    row_max = jnp.max(unnormalized_affinities, axis=-1, keepdims=True)
    expo = jnp.exp(unnormalized_affinities - row_max)
    return expo / jnp.sum(expo, axis=-1, keepdims=True)


def compute_affinity_outputs(
    asking_vectors, lookup_array, payload_array, admissible_pairs, sharpness_divisor
):
    truncated_outcome = normalized_affinity(
        asking_vectors, lookup_array, admissible_pairs, sharpness_divisor
    ).astype(jnp.bfloat16)
    return jnp.einsum(
        "...qk,...kd->...qd", truncated_outcome, payload_array, preferred_element_type=jnp.float32
    ).astype(jnp.bfloat16)


def compute_affinity_derivatives(
    asking_vectors,
    lookup_array,
    payload_array,
    admissible_pairs,
    sharpness_divisor,
    combined_output,
    blended_output_derivative,
):
    coefficient_array = normalized_affinity(
        asking_vectors, lookup_array, admissible_pairs, sharpness_divisor
    )
    truncated_outcome = coefficient_array.astype(jnp.bfloat16)
    grad_values = jnp.einsum(
        "...qk,...qd->...kd",
        truncated_outcome,
        blended_output_derivative,
        preferred_element_type=jnp.float32,
    )
    coefficient_derivative = jnp.einsum(
        "...uo,...ao->...ua",
        blended_output_derivative,
        payload_array,
        preferred_element_type=jnp.float32,
    )
    paired_inner_sums = jnp.sum(
        blended_output_derivative.astype(jnp.float32) * combined_output.astype(jnp.float32),
        axis=-1,
        keepdims=True,
    )
    affinity_derivative = (
        coefficient_array * (coefficient_derivative - paired_inner_sums) * sharpness_divisor
    ).astype(jnp.bfloat16)
    grad_queries = jnp.einsum(
        "...qk,...kd->...qd", affinity_derivative, lookup_array, preferred_element_type=jnp.float32
    )
    grad_keys = jnp.einsum(
        "...qk,...qd->...kd",
        affinity_derivative,
        asking_vectors,
        preferred_element_type=jnp.float32,
    )
    return (
        grad_queries.astype(jnp.bfloat16),
        grad_keys.astype(jnp.bfloat16),
        grad_values.astype(jnp.bfloat16),
    )


def temporal_split(projected):
    pieces = projected.reshape(projected.shape[0], 3, HEADS, projected.shape[1] // (3 * HEADS))
    return [pieces[:, index].transpose(1, 0, 2) for index in range(3)]


def temporal_forward(projected, admissible_pairs):
    asking_vectors, lookup_array, payload_array = temporal_split(projected)
    sharpness_divisor = float(asking_vectors.shape[-1]) ** (-0.5)
    combined_output = compute_affinity_outputs(
        asking_vectors, lookup_array, payload_array, admissible_pairs[None], sharpness_divisor
    )
    return combined_output.transpose(1, 0, 2).reshape(projected.shape[0], -1)


def temporal_backward(projected, admissible_pairs, combined_output, blended_output_derivative):
    asking_vectors, lookup_array, payload_array = temporal_split(projected)
    sharpness_divisor = float(asking_vectors.shape[-1]) ** (-0.5)
    bins = projected.shape[0]
    subspace_outputs = combined_output.reshape(bins, HEADS, -1).transpose(1, 0, 2)
    subspace_derivative = blended_output_derivative.reshape(bins, HEADS, -1).transpose(1, 0, 2)
    derivative_collection = compute_affinity_derivatives(
        asking_vectors,
        lookup_array,
        payload_array,
        admissible_pairs[None],
        sharpness_divisor,
        subspace_outputs,
        subspace_derivative,
    )
    return jnp.stack(derivative_collection, axis=0).transpose(2, 0, 1, 3).reshape(bins, -1)


def spatial_split(projected):
    pieces = projected.reshape(
        projected.shape[0], projected.shape[1], 3, HEADS, projected.shape[2] // (3 * HEADS)
    )
    return [pieces[:, :, index].transpose(0, 2, 1, 3) for index in range(3)]


def spatial_forward(projected, admissible_pairs):
    asking_vectors, lookup_array, payload_array = spatial_split(projected)
    sharpness_divisor = float(asking_vectors.shape[-1]) ** (-0.5)
    combined_output = compute_affinity_outputs(
        asking_vectors, lookup_array, payload_array, admissible_pairs, sharpness_divisor
    )
    return combined_output.transpose(0, 2, 1, 3).reshape(projected.shape[0], projected.shape[1], -1)


def spatial_backward(projected, admissible_pairs, combined_output, blended_output_derivative):
    asking_vectors, lookup_array, payload_array = spatial_split(projected)
    sharpness_divisor = float(asking_vectors.shape[-1]) ** (-0.5)
    bins, blocks = (projected.shape[0], projected.shape[1])
    subspace_outputs = combined_output.reshape(bins, blocks, HEADS, -1).transpose(0, 2, 1, 3)
    subspace_derivative = blended_output_derivative.reshape(bins, blocks, HEADS, -1).transpose(
        0, 2, 1, 3
    )
    derivative_collection = compute_affinity_derivatives(
        asking_vectors,
        lookup_array,
        payload_array,
        admissible_pairs,
        sharpness_divisor,
        subspace_outputs,
        subspace_derivative,
    )
    return (
        jnp.stack(derivative_collection, axis=0).transpose(1, 3, 0, 2, 4).reshape(bins, blocks, -1)
    )


def spatial_allowed(sessions_here, channel_count, adjacency):
    block_count = adjacency.shape[0]
    block_ids = jnp.arange(block_count, dtype=jnp.int32)
    session_pick = (
        sessions_here[:, None] == jnp.arange(channel_count.shape[0], dtype=jnp.int32)[None, :]
    ).astype(jnp.int32)
    count_rows = jnp.sum(session_pick * channel_count[None, :], axis=1)
    live_block = block_ids[None, :] * block_channels < count_rows[:, None]
    linked = adjacency > 0
    itself = block_ids[:, None] == block_ids[None, :]
    admissible_pairs = linked[None, :, :] & live_block[:, None, :] | itself[None, :, :]
    return admissible_pairs[:, None, :, :]


def project(rows, coefficient_array):
    return jnp.einsum("tbd,de->tbe", rows, coefficient_array, preferred_element_type=jnp.float32)


def project_back(derivative_collection, coefficient_array):
    return jnp.einsum(
        "tbe,de->tbd", derivative_collection, coefficient_array, preferred_element_type=jnp.float32
    )


def weight_term(left, right):
    return jnp.einsum("tbd,tbe->de", left, right, preferred_element_type=jnp.float32)


def reduce_rows(partial):
    rows, cols = partial.shape
    outer = lax.psum(1, "outer")
    pieces = partial.reshape(outer, 2, rows // (2 * outer), cols)
    first = lax.axis_index("core") == 0
    kept = jnp.where(first, pieces[:, 0], pieces[:, 1])
    given = jnp.where(first, pieces[:, 1], pieces[:, 0]).astype(jnp.bfloat16)
    taken = lax.ppermute(given, "core", [(0, 1), (1, 0)])
    pieces = (kept + taken.astype(jnp.float32)).astype(jnp.bfloat16)
    pieces = lax.all_to_all(pieces, "outer", 0, 0, tiled=True)
    return jnp.sum(pieces.astype(jnp.float32), axis=0)


def scatter_rows(partial):
    return lax.psum_scatter(
        partial.astype(jnp.bfloat16), ("outer", "core"), scatter_dimension=0, tiled=True
    ).astype(jnp.float32)


def per_device(
    activity,
    grad_out,
    spatial_weights,
    temporal_weights,
    spatial_gain,
    temporal_gain,
    adjacency,
    channel_count,
    session_id,
):
    local_bins = activity.shape[0]
    model_width = activity.shape[2]
    first_bin = (lax.axis_index("outer") * 2 + lax.axis_index("core")) * local_bins
    sessions_here = lax.dynamic_slice_in_dim(session_id, first_bin, local_bins)
    normed_one, inverse_one = norm_forward(activity, spatial_gain)
    spatial_proj = project(normed_one, spatial_weights[:, : 3 * model_width]).astype(jnp.bfloat16)
    allowed_space = spatial_allowed(sessions_here, channel_count, adjacency)
    spatial_context = spatial_forward(spatial_proj, allowed_space)
    middle = (
        activity.astype(jnp.float32)
        + project(spatial_context, spatial_weights[:, 3 * model_width :])
    ).astype(jnp.bfloat16)
    middle_block = lax.all_to_all(middle, ("outer", "core"), split_axis=1, concat_axis=0, tiled=True)
    normed_two, inverse_two = norm_forward(middle_block, temporal_gain)
    temporal_proj = project(normed_two, temporal_weights[:, : 3 * model_width]).astype(jnp.bfloat16)
    allowed_time = session_id[:, None] == session_id[None, :]
    by_block = jnp.moveaxis(temporal_proj, 1, 0)
    temporal_context = jnp.moveaxis(
        lax.map(lambda block_rows: temporal_forward(block_rows, allowed_time), by_block), 0, 1
    )
    layer_out = (
        middle_block.astype(jnp.float32)
        + project(temporal_context, temporal_weights[:, 3 * model_width :])
    ).astype(jnp.bfloat16)
    grad_temporal_context = project_back(grad_out, temporal_weights[:, 3 * model_width :]).astype(
        jnp.bfloat16
    )
    stacked = (
        by_block,
        jnp.moveaxis(temporal_context, 1, 0),
        jnp.moveaxis(grad_temporal_context, 1, 0),
    )
    grad_temporal_proj = jnp.moveaxis(
        lax.map(
            lambda items: temporal_backward(items[0], allowed_time, items[1], items[2]), stacked
        ),
        0,
        1,
    )
    grad_normed_two = project_back(grad_temporal_proj, temporal_weights[:, : 3 * model_width])
    grad_middle = (
        grad_out.astype(jnp.float32)
        + norm_backward(middle_block, temporal_gain, inverse_two, grad_normed_two)
    ).astype(jnp.bfloat16)
    grad_middle_time = lax.all_to_all(grad_middle, ("outer", "core"), split_axis=0, concat_axis=1, tiled=True)
    normed_cols = normed_two
    context_cols = temporal_context
    temporal_grad = reduce_rows(
        jnp.concatenate(
            [weight_term(normed_cols, grad_temporal_proj), weight_term(context_cols, grad_out)],
            axis=1,
        )
    )
    spatial_term = weight_term(spatial_context, grad_middle_time)
    spatial_term, grad_middle_time = lax.optimization_barrier((spatial_term, grad_middle_time))
    grad_spatial_context = project_back(
        grad_middle_time, spatial_weights[:, 3 * model_width :]
    ).astype(jnp.bfloat16)
    grad_spatial_proj = spatial_backward(
        spatial_proj, allowed_space, spatial_context, grad_spatial_context
    )
    spatial_term = reduce_rows(spatial_term)
    spatial_term, temporal_grad, grad_spatial_proj = lax.optimization_barrier(
        (spatial_term, temporal_grad, grad_spatial_proj)
    )
    grad_normed_one = project_back(grad_spatial_proj, spatial_weights[:, : 3 * model_width])
    grad_activity = (
        grad_middle_time.astype(jnp.float32)
        + norm_backward(activity, spatial_gain, inverse_one, grad_normed_one)
    ).astype(jnp.bfloat16)
    normed_cols = normed_one
    context_cols = spatial_context
    spatial_grad = jnp.concatenate(
        [
            reduce_rows(weight_term(normed_cols, grad_spatial_proj)),
            spatial_term,
        ],
        axis=1,
    )
    return (layer_out, grad_activity, spatial_grad, temporal_grad)


def solution(mesh):
    groups, wide = mesh.devices.shape
    mesh = Mesh(mesh.devices.reshape(groups, wide // 2, 2), ("groups", "outer", "core"))
    placed = (
        P(("groups", "outer", "core"), None, None),
        P("groups", ("outer", "core"), None),
        P(),
        P(),
        P(),
        P(),
        P(),
        P("groups"),
        P("groups"),
    )
    return jax.shard_map(
        per_device,
        mesh=mesh,
        in_specs=placed,
        out_specs=(
            P("groups", ("outer", "core"), None),
            P(("groups", "outer", "core"), None, None),
            P(("groups", "outer", "core"), None),
            P(("groups", "outer", "core"), None),
        ),
        check_vma=False,
    )
```

```python
import jax
import jax.numpy as jnp
from jax import lax
from jax.sharding import Mesh, PartitionSpec as P

HEADS = 8


eps_norm = 1e-05
block_channels = 128


def norm_inverse(rows):
    values = rows.astype(jnp.float32)
    return lax.rsqrt(jnp.mean(values * values, axis=-1, keepdims=True) + eps_norm)


def norm_forward(rows, gain):
    inverse = norm_inverse(rows)
    return ((rows.astype(jnp.float32) * inverse * gain).astype(jnp.bfloat16), inverse)


def norm_backward(rows, gain, inverse, grad_normed):
    values = rows.astype(jnp.float32)
    scaled = grad_normed * gain
    inner = jnp.mean(values * scaled, axis=-1, keepdims=True)
    return inverse * scaled - values * inverse * inverse * inverse * inner


def normalized_affinity(asking_vectors, lookup_array, admissible_pairs, sharpness_divisor):
    unnormalized_affinities = (
        jnp.einsum(
            "...uo,...ao->...ua", asking_vectors, lookup_array, preferred_element_type=jnp.float32
        )
        * sharpness_divisor
    )
    unnormalized_affinities = jnp.where(admissible_pairs, unnormalized_affinities, -1e30)
    row_max = jnp.max(unnormalized_affinities, axis=-1, keepdims=True)
    expo = jnp.exp(unnormalized_affinities - row_max)
    return expo / jnp.sum(expo, axis=-1, keepdims=True)


def compute_affinity_outputs(
    asking_vectors, lookup_array, payload_array, admissible_pairs, sharpness_divisor
):
    truncated_outcome = normalized_affinity(
        asking_vectors, lookup_array, admissible_pairs, sharpness_divisor
    ).astype(jnp.bfloat16)
    return jnp.einsum(
        "...qk,...kd->...qd", truncated_outcome, payload_array, preferred_element_type=jnp.float32
    ).astype(jnp.bfloat16)


def compute_affinity_derivatives(
    asking_vectors,
    lookup_array,
    payload_array,
    admissible_pairs,
    sharpness_divisor,
    combined_output,
    blended_output_derivative,
):
    coefficient_array = normalized_affinity(
        asking_vectors, lookup_array, admissible_pairs, sharpness_divisor
    )
    truncated_outcome = coefficient_array.astype(jnp.bfloat16)
    grad_values = jnp.einsum(
        "...qk,...qd->...kd",
        truncated_outcome,
        blended_output_derivative,
        preferred_element_type=jnp.float32,
    )
    coefficient_derivative = jnp.einsum(
        "...uo,...ao->...ua",
        blended_output_derivative,
        payload_array,
        preferred_element_type=jnp.float32,
    )
    paired_inner_sums = jnp.sum(
        blended_output_derivative.astype(jnp.float32) * combined_output.astype(jnp.float32),
        axis=-1,
        keepdims=True,
    )
    affinity_derivative = (
        coefficient_array * (coefficient_derivative - paired_inner_sums) * sharpness_divisor
    ).astype(jnp.bfloat16)
    grad_queries = jnp.einsum(
        "...qk,...kd->...qd", affinity_derivative, lookup_array, preferred_element_type=jnp.float32
    )
    grad_keys = jnp.einsum(
        "...qk,...qd->...kd",
        affinity_derivative,
        asking_vectors,
        preferred_element_type=jnp.float32,
    )
    return (
        grad_queries.astype(jnp.bfloat16),
        grad_keys.astype(jnp.bfloat16),
        grad_values.astype(jnp.bfloat16),
    )


def temporal_split(projected):
    pieces = projected.reshape(projected.shape[0], 3, HEADS, projected.shape[1] // (3 * HEADS))
    return [pieces[:, index].transpose(1, 0, 2) for index in range(3)]


def temporal_forward(projected, admissible_pairs):
    asking_vectors, lookup_array, payload_array = temporal_split(projected)
    sharpness_divisor = float(asking_vectors.shape[-1]) ** (-0.5)
    combined_output = compute_affinity_outputs(
        asking_vectors, lookup_array, payload_array, admissible_pairs[None], sharpness_divisor
    )
    return combined_output.transpose(1, 0, 2).reshape(projected.shape[0], -1)


def temporal_backward(projected, admissible_pairs, combined_output, blended_output_derivative):
    asking_vectors, lookup_array, payload_array = temporal_split(projected)
    sharpness_divisor = float(asking_vectors.shape[-1]) ** (-0.5)
    bins = projected.shape[0]
    subspace_outputs = combined_output.reshape(bins, HEADS, -1).transpose(1, 0, 2)
    subspace_derivative = blended_output_derivative.reshape(bins, HEADS, -1).transpose(1, 0, 2)
    derivative_collection = compute_affinity_derivatives(
        asking_vectors,
        lookup_array,
        payload_array,
        admissible_pairs[None],
        sharpness_divisor,
        subspace_outputs,
        subspace_derivative,
    )
    return jnp.stack(derivative_collection, axis=0).transpose(2, 0, 1, 3).reshape(bins, -1)


def spatial_split(projected):
    pieces = projected.reshape(
        projected.shape[0], projected.shape[1], 3, HEADS, projected.shape[2] // (3 * HEADS)
    )
    return [pieces[:, :, index].transpose(0, 2, 1, 3) for index in range(3)]


def spatial_forward(projected, admissible_pairs):
    asking_vectors, lookup_array, payload_array = spatial_split(projected)
    sharpness_divisor = float(asking_vectors.shape[-1]) ** (-0.5)
    combined_output = compute_affinity_outputs(
        asking_vectors, lookup_array, payload_array, admissible_pairs, sharpness_divisor
    )
    return combined_output.transpose(0, 2, 1, 3).reshape(projected.shape[0], projected.shape[1], -1)


def spatial_backward(projected, admissible_pairs, combined_output, blended_output_derivative):
    asking_vectors, lookup_array, payload_array = spatial_split(projected)
    sharpness_divisor = float(asking_vectors.shape[-1]) ** (-0.5)
    bins, blocks = (projected.shape[0], projected.shape[1])
    subspace_outputs = combined_output.reshape(bins, blocks, HEADS, -1).transpose(0, 2, 1, 3)
    subspace_derivative = blended_output_derivative.reshape(bins, blocks, HEADS, -1).transpose(
        0, 2, 1, 3
    )
    derivative_collection = compute_affinity_derivatives(
        asking_vectors,
        lookup_array,
        payload_array,
        admissible_pairs,
        sharpness_divisor,
        subspace_outputs,
        subspace_derivative,
    )
    return (
        jnp.stack(derivative_collection, axis=0).transpose(1, 3, 0, 2, 4).reshape(bins, blocks, -1)
    )


def spatial_allowed(sessions_here, channel_count, adjacency):
    block_count = adjacency.shape[0]
    block_ids = jnp.arange(block_count, dtype=jnp.int32)
    session_pick = (
        sessions_here[:, None] == jnp.arange(channel_count.shape[0], dtype=jnp.int32)[None, :]
    ).astype(jnp.int32)
    count_rows = jnp.sum(session_pick * channel_count[None, :], axis=1)
    live_block = block_ids[None, :] * block_channels < count_rows[:, None]
    linked = adjacency > 0
    itself = block_ids[:, None] == block_ids[None, :]
    admissible_pairs = linked[None, :, :] & live_block[:, None, :] | itself[None, :, :]
    return admissible_pairs[:, None, :, :]


def project(rows, coefficient_array):
    return jnp.einsum("tbd,de->tbe", rows, coefficient_array, preferred_element_type=jnp.float32)


def project_back(derivative_collection, coefficient_array):
    return jnp.einsum(
        "tbe,de->tbd", derivative_collection, coefficient_array, preferred_element_type=jnp.float32
    )


def weight_term(left, right):
    return jnp.einsum("tbd,tbe->de", left, right, preferred_element_type=jnp.float32)


def reduce_rows(partial):
    rows, cols = partial.shape
    outer = lax.psum(1, "outer")
    pieces = partial.reshape(outer, 2, rows // (2 * outer), cols)
    first = lax.axis_index("core") == 0
    kept = jnp.where(first, pieces[:, 0], pieces[:, 1])
    given = jnp.where(first, pieces[:, 1], pieces[:, 0]).astype(jnp.bfloat16)
    taken = lax.ppermute(given, "core", [(0, 1), (1, 0)])
    pieces = (kept + taken.astype(jnp.float32)).astype(jnp.bfloat16)
    pieces = lax.all_to_all(pieces, "outer", 0, 0, tiled=True)
    return jnp.sum(pieces.astype(jnp.float32), axis=0)


def scatter_rows(partial):
    return lax.psum_scatter(
        partial.astype(jnp.bfloat16), ("outer", "core"), scatter_dimension=0, tiled=True
    ).astype(jnp.float32)


def per_device(
    activity,
    grad_out,
    spatial_weights,
    temporal_weights,
    spatial_gain,
    temporal_gain,
    adjacency,
    channel_count,
    session_id,
):
    local_bins = activity.shape[0]
    model_width = activity.shape[2]
    first_bin = (lax.axis_index("outer") * 2 + lax.axis_index("core")) * local_bins
    sessions_here = lax.dynamic_slice_in_dim(session_id, first_bin, local_bins)
    normed_one, inverse_one = norm_forward(activity, spatial_gain)
    spatial_proj = project(normed_one, spatial_weights[:, : 3 * model_width]).astype(jnp.bfloat16)
    allowed_space = spatial_allowed(sessions_here, channel_count, adjacency)
    spatial_context = spatial_forward(spatial_proj, allowed_space)
    middle = (
        activity.astype(jnp.float32)
        + project(spatial_context, spatial_weights[:, 3 * model_width :])
    ).astype(jnp.bfloat16)
    middle_block = lax.all_to_all(middle, ("outer", "core"), split_axis=1, concat_axis=0, tiled=True)
    normed_two, inverse_two = norm_forward(middle_block, temporal_gain)
    temporal_proj = project(normed_two, temporal_weights[:, : 3 * model_width]).astype(jnp.bfloat16)
    allowed_time = session_id[:, None] == session_id[None, :]
    by_block = jnp.moveaxis(temporal_proj, 1, 0)
    temporal_context = jnp.moveaxis(
        lax.map(lambda block_rows: temporal_forward(block_rows, allowed_time), by_block), 0, 1
    )
    layer_out = (
        middle_block.astype(jnp.float32)
        + project(temporal_context, temporal_weights[:, 3 * model_width :])
    ).astype(jnp.bfloat16)
    grad_temporal_context = project_back(grad_out, temporal_weights[:, 3 * model_width :]).astype(
        jnp.bfloat16
    )
    stacked = (
        by_block,
        jnp.moveaxis(temporal_context, 1, 0),
        jnp.moveaxis(grad_temporal_context, 1, 0),
    )
    grad_temporal_proj = jnp.moveaxis(
        lax.map(
            lambda items: temporal_backward(items[0], allowed_time, items[1], items[2]), stacked
        ),
        0,
        1,
    )
    grad_normed_two = project_back(grad_temporal_proj, temporal_weights[:, : 3 * model_width])
    grad_middle = (
        grad_out.astype(jnp.float32)
        + norm_backward(middle_block, temporal_gain, inverse_two, grad_normed_two)
    ).astype(jnp.bfloat16)
    normed_cols = normed_two
    context_cols = temporal_context
    temporal_partial = jnp.concatenate(
        [weight_term(normed_cols, grad_temporal_proj), weight_term(context_cols, grad_out)],
        axis=1,
    ).astype(jnp.bfloat16)
    temporal_partial, grad_middle = lax.optimization_barrier((temporal_partial, grad_middle))
    temporal_grad = scatter_rows(temporal_partial)
    grad_middle_time = lax.all_to_all(grad_middle, ("outer", "core"), split_axis=0, concat_axis=1, tiled=True)
    spatial_term = weight_term(spatial_context, grad_middle_time)
    spatial_term, grad_middle_time = lax.optimization_barrier((spatial_term, grad_middle_time))
    grad_spatial_context = project_back(
        grad_middle_time, spatial_weights[:, 3 * model_width :]
    ).astype(jnp.bfloat16)
    grad_spatial_proj = spatial_backward(
        spatial_proj, allowed_space, spatial_context, grad_spatial_context
    )
    spatial_term = reduce_rows(spatial_term)
    spatial_term, grad_spatial_proj = lax.optimization_barrier((spatial_term, grad_spatial_proj))
    grad_normed_one = project_back(grad_spatial_proj, spatial_weights[:, : 3 * model_width])
    grad_activity = (
        grad_middle_time.astype(jnp.float32)
        + norm_backward(activity, spatial_gain, inverse_one, grad_normed_one)
    ).astype(jnp.bfloat16)
    normed_cols = normed_one
    context_cols = spatial_context
    spatial_grad = jnp.concatenate(
        [
            reduce_rows(weight_term(normed_cols, grad_spatial_proj)),
            spatial_term,
        ],
        axis=1,
    )
    return (layer_out, grad_activity, spatial_grad, temporal_grad)


def solution(mesh):
    groups, wide = mesh.devices.shape
    mesh = Mesh(mesh.devices.reshape(groups, wide // 2, 2), ("groups", "outer", "core"))
    placed = (
        P(("groups", "outer", "core"), None, None),
        P("groups", ("outer", "core"), None),
        P(),
        P(),
        P(),
        P(),
        P(),
        P("groups"),
        P("groups"),
    )
    return jax.shard_map(
        per_device,
        mesh=mesh,
        in_specs=placed,
        out_specs=(
            P("groups", ("outer", "core"), None),
            P(("groups", "outer", "core"), None, None),
            P(("groups", "outer", "core"), None),
            P(("groups", "outer", "core"), None),
        ),
        check_vma=False,
    )
```

```python
import jax
import jax.numpy as jnp
from jax import lax
from jax.sharding import Mesh, PartitionSpec as P

HEADS = 8


eps_norm = 1e-05
block_channels = 128


def norm_inverse(rows):
    values = rows.astype(jnp.float32)
    return lax.rsqrt(jnp.mean(values * values, axis=-1, keepdims=True) + eps_norm)


def norm_forward(rows, gain):
    inverse = norm_inverse(rows)
    return ((rows.astype(jnp.float32) * inverse * gain).astype(jnp.bfloat16), inverse)


def norm_backward(rows, gain, inverse, grad_normed):
    values = rows.astype(jnp.float32)
    scaled = grad_normed * gain
    inner = jnp.mean(values * scaled, axis=-1, keepdims=True)
    return inverse * scaled - values * inverse * inverse * inverse * inner


def normalized_affinity(asking_vectors, lookup_array, admissible_pairs, sharpness_divisor):
    unnormalized_affinities = (
        jnp.einsum(
            "...uo,...ao->...ua", asking_vectors, lookup_array, preferred_element_type=jnp.float32
        )
        * sharpness_divisor
    )
    unnormalized_affinities = jnp.where(admissible_pairs, unnormalized_affinities, -1e30)
    row_max = jnp.max(unnormalized_affinities, axis=-1, keepdims=True)
    expo = jnp.exp(unnormalized_affinities - row_max)
    return expo / jnp.sum(expo, axis=-1, keepdims=True)


def compute_affinity_outputs(
    asking_vectors, lookup_array, payload_array, admissible_pairs, sharpness_divisor
):
    truncated_outcome = normalized_affinity(
        asking_vectors, lookup_array, admissible_pairs, sharpness_divisor
    ).astype(jnp.bfloat16)
    return jnp.einsum(
        "...qk,...kd->...qd", truncated_outcome, payload_array, preferred_element_type=jnp.float32
    ).astype(jnp.bfloat16)


def compute_affinity_derivatives(
    asking_vectors,
    lookup_array,
    payload_array,
    admissible_pairs,
    sharpness_divisor,
    combined_output,
    blended_output_derivative,
):
    coefficient_array = normalized_affinity(
        asking_vectors, lookup_array, admissible_pairs, sharpness_divisor
    )
    truncated_outcome = coefficient_array.astype(jnp.bfloat16)
    grad_values = jnp.einsum(
        "...qk,...qd->...kd",
        truncated_outcome,
        blended_output_derivative,
        preferred_element_type=jnp.float32,
    )
    coefficient_derivative = jnp.einsum(
        "...uo,...ao->...ua",
        blended_output_derivative,
        payload_array,
        preferred_element_type=jnp.float32,
    )
    paired_inner_sums = jnp.sum(
        blended_output_derivative.astype(jnp.float32) * combined_output.astype(jnp.float32),
        axis=-1,
        keepdims=True,
    )
    affinity_derivative = (
        coefficient_array * (coefficient_derivative - paired_inner_sums) * sharpness_divisor
    ).astype(jnp.bfloat16)
    grad_queries = jnp.einsum(
        "...qk,...kd->...qd", affinity_derivative, lookup_array, preferred_element_type=jnp.float32
    )
    grad_keys = jnp.einsum(
        "...qk,...qd->...kd",
        affinity_derivative,
        asking_vectors,
        preferred_element_type=jnp.float32,
    )
    return (
        grad_queries.astype(jnp.bfloat16),
        grad_keys.astype(jnp.bfloat16),
        grad_values.astype(jnp.bfloat16),
    )


def temporal_split(projected):
    pieces = projected.reshape(projected.shape[0], 3, HEADS, projected.shape[1] // (3 * HEADS))
    return [pieces[:, index].transpose(1, 0, 2) for index in range(3)]


def temporal_forward(projected, admissible_pairs):
    asking_vectors, lookup_array, payload_array = temporal_split(projected)
    sharpness_divisor = float(asking_vectors.shape[-1]) ** (-0.5)
    combined_output = compute_affinity_outputs(
        asking_vectors, lookup_array, payload_array, admissible_pairs[None], sharpness_divisor
    )
    return combined_output.transpose(1, 0, 2).reshape(projected.shape[0], -1)


def temporal_backward(projected, admissible_pairs, combined_output, blended_output_derivative):
    asking_vectors, lookup_array, payload_array = temporal_split(projected)
    sharpness_divisor = float(asking_vectors.shape[-1]) ** (-0.5)
    bins = projected.shape[0]
    subspace_outputs = combined_output.reshape(bins, HEADS, -1).transpose(1, 0, 2)
    subspace_derivative = blended_output_derivative.reshape(bins, HEADS, -1).transpose(1, 0, 2)
    derivative_collection = compute_affinity_derivatives(
        asking_vectors,
        lookup_array,
        payload_array,
        admissible_pairs[None],
        sharpness_divisor,
        subspace_outputs,
        subspace_derivative,
    )
    return jnp.stack(derivative_collection, axis=0).transpose(2, 0, 1, 3).reshape(bins, -1)


def spatial_split(projected):
    pieces = projected.reshape(
        projected.shape[0], projected.shape[1], 3, HEADS, projected.shape[2] // (3 * HEADS)
    )
    return [pieces[:, :, index].transpose(0, 2, 1, 3) for index in range(3)]


def spatial_forward(projected, admissible_pairs):
    asking_vectors, lookup_array, payload_array = spatial_split(projected)
    sharpness_divisor = float(asking_vectors.shape[-1]) ** (-0.5)
    combined_output = compute_affinity_outputs(
        asking_vectors, lookup_array, payload_array, admissible_pairs, sharpness_divisor
    )
    return combined_output.transpose(0, 2, 1, 3).reshape(projected.shape[0], projected.shape[1], -1)


def spatial_backward(projected, admissible_pairs, combined_output, blended_output_derivative):
    asking_vectors, lookup_array, payload_array = spatial_split(projected)
    sharpness_divisor = float(asking_vectors.shape[-1]) ** (-0.5)
    bins, blocks = (projected.shape[0], projected.shape[1])
    subspace_outputs = combined_output.reshape(bins, blocks, HEADS, -1).transpose(0, 2, 1, 3)
    subspace_derivative = blended_output_derivative.reshape(bins, blocks, HEADS, -1).transpose(
        0, 2, 1, 3
    )
    derivative_collection = compute_affinity_derivatives(
        asking_vectors,
        lookup_array,
        payload_array,
        admissible_pairs,
        sharpness_divisor,
        subspace_outputs,
        subspace_derivative,
    )
    return (
        jnp.stack(derivative_collection, axis=0).transpose(1, 3, 0, 2, 4).reshape(bins, blocks, -1)
    )


def head_mask(width):
    column_head = jnp.arange(width, dtype=jnp.int32) // (width // HEADS)
    return column_head[None, :] == jnp.arange(HEADS, dtype=jnp.int32)[:, None]


def masked_rows(rows):
    keep = head_mask(rows.shape[-1])[None, :, None, :]
    return jnp.where(keep, rows[:, None, :, :], jnp.zeros((), rows.dtype))


def masked_cols(rows):
    keep = head_mask(rows.shape[-1])[None, None, :, :]
    return jnp.where(keep, rows[:, :, None, :], jnp.zeros((), rows.dtype))


def spatial_probs(asking, lookup, admissible_pairs, sharpness_divisor):
    scores = (
        jnp.einsum(
            "tbd,thcd->tbhc", asking, masked_rows(lookup), preferred_element_type=jnp.float32
        )
        * sharpness_divisor
    )
    scores = jnp.where(admissible_pairs[:, 0][:, :, None, :], scores, -1e30)
    row_max = jnp.max(scores, axis=-1, keepdims=True)
    expo = jnp.exp(scores - row_max)
    return expo / jnp.sum(expo, axis=-1, keepdims=True)


def spatial_forward_heads(projected, admissible_pairs):
    width = projected.shape[-1] // 3
    asking, lookup, payload = [projected[..., i * width : (i + 1) * width] for i in range(3)]
    sharpness_divisor = float(width // HEADS) ** (-0.5)
    probs = spatial_probs(asking, lookup, admissible_pairs, sharpness_divisor).astype(jnp.bfloat16)
    return jnp.einsum(
        "tbhc,thcd->tbd", probs, masked_rows(payload), preferred_element_type=jnp.float32
    ).astype(jnp.bfloat16)


def spatial_backward_heads(projected, admissible_pairs, combined_output, output_derivative):
    width = projected.shape[-1] // 3
    asking, lookup, payload = [projected[..., i * width : (i + 1) * width] for i in range(3)]
    sharpness_divisor = float(width // HEADS) ** (-0.5)
    bins, blocks = projected.shape[0], projected.shape[1]
    probs = spatial_probs(asking, lookup, admissible_pairs, sharpness_divisor)
    grad_values = jnp.einsum(
        "tbhc,tbhd->tcd",
        probs.astype(jnp.bfloat16),
        masked_cols(output_derivative),
        preferred_element_type=jnp.float32,
    )
    probs_derivative = jnp.einsum(
        "tbd,thcd->tbhc", output_derivative, masked_rows(payload), preferred_element_type=jnp.float32
    )
    inner = jnp.einsum(
        "tbd,hd->tbh",
        output_derivative.astype(jnp.float32) * combined_output.astype(jnp.float32),
        head_mask(width).astype(jnp.float32),
        precision=lax.Precision.HIGHEST,
        preferred_element_type=jnp.float32,
    )[..., None]
    scores_derivative = (probs * (probs_derivative - inner) * sharpness_divisor).astype(
        jnp.bfloat16
    )
    grad_queries = jnp.einsum(
        "tbhc,thcd->tbd", scores_derivative, masked_rows(lookup), preferred_element_type=jnp.float32
    )
    grad_keys = jnp.einsum(
        "tbhc,tbhd->tcd", scores_derivative, masked_cols(asking), preferred_element_type=jnp.float32
    )
    return jnp.concatenate(
        [grad_queries.astype(jnp.bfloat16), grad_keys.astype(jnp.bfloat16), grad_values.astype(jnp.bfloat16)],
        axis=-1,
    )


def spatial_allowed(sessions_here, channel_count, adjacency):
    block_count = adjacency.shape[0]
    block_ids = jnp.arange(block_count, dtype=jnp.int32)
    session_pick = (
        sessions_here[:, None] == jnp.arange(channel_count.shape[0], dtype=jnp.int32)[None, :]
    ).astype(jnp.int32)
    count_rows = jnp.sum(session_pick * channel_count[None, :], axis=1)
    live_block = block_ids[None, :] * block_channels < count_rows[:, None]
    linked = adjacency > 0
    itself = block_ids[:, None] == block_ids[None, :]
    admissible_pairs = linked[None, :, :] & live_block[:, None, :] | itself[None, :, :]
    return admissible_pairs[:, None, :, :]


def project(rows, coefficient_array):
    return jnp.einsum("tbd,de->tbe", rows, coefficient_array, preferred_element_type=jnp.float32)


def project_back(derivative_collection, coefficient_array):
    return jnp.einsum(
        "tbe,de->tbd", derivative_collection, coefficient_array, preferred_element_type=jnp.float32
    )


def weight_term(left, right):
    return jnp.einsum("tbd,tbe->de", left, right, preferred_element_type=jnp.float32)


def reduce_rows(partial):
    rows, cols = partial.shape
    outer = lax.psum(1, "outer")
    pieces = partial.reshape(outer, 2, rows // (2 * outer), cols)
    first = lax.axis_index("core") == 0
    kept = jnp.where(first, pieces[:, 0], pieces[:, 1])
    given = jnp.where(first, pieces[:, 1], pieces[:, 0]).astype(jnp.bfloat16)
    taken = lax.ppermute(given, "core", [(0, 1), (1, 0)])
    pieces = (kept + taken.astype(jnp.float32)).astype(jnp.bfloat16)
    pieces = lax.all_to_all(pieces, "outer", 0, 0, tiled=True)
    return jnp.sum(pieces.astype(jnp.float32), axis=0)


def scatter_rows(partial):
    return lax.psum_scatter(
        partial.astype(jnp.bfloat16), ("outer", "core"), scatter_dimension=0, tiled=True
    ).astype(jnp.float32)


def per_device(
    activity,
    grad_out,
    spatial_weights,
    temporal_weights,
    spatial_gain,
    temporal_gain,
    adjacency,
    channel_count,
    session_id,
):
    local_bins = activity.shape[0]
    model_width = activity.shape[2]
    first_bin = (lax.axis_index("outer") * 2 + lax.axis_index("core")) * local_bins
    sessions_here = lax.dynamic_slice_in_dim(session_id, first_bin, local_bins)
    normed_one, inverse_one = norm_forward(activity, spatial_gain)
    spatial_proj = project(normed_one, spatial_weights[:, : 3 * model_width]).astype(jnp.bfloat16)
    allowed_space = spatial_allowed(sessions_here, channel_count, adjacency)
    spatial_context = spatial_forward_heads(spatial_proj, allowed_space)
    middle = (
        activity.astype(jnp.float32)
        + project(spatial_context, spatial_weights[:, 3 * model_width :])
    ).astype(jnp.bfloat16)
    middle_block = lax.all_to_all(middle, ("outer", "core"), split_axis=1, concat_axis=0, tiled=True)
    normed_two, inverse_two = norm_forward(middle_block, temporal_gain)
    temporal_proj = project(normed_two, temporal_weights[:, : 3 * model_width]).astype(jnp.bfloat16)
    allowed_time = session_id[:, None] == session_id[None, :]
    by_block = jnp.moveaxis(temporal_proj, 1, 0)
    temporal_context = jnp.moveaxis(
        lax.map(lambda block_rows: temporal_forward(block_rows, allowed_time), by_block), 0, 1
    )
    layer_out = (
        middle_block.astype(jnp.float32)
        + project(temporal_context, temporal_weights[:, 3 * model_width :])
    ).astype(jnp.bfloat16)
    grad_temporal_context = project_back(grad_out, temporal_weights[:, 3 * model_width :]).astype(
        jnp.bfloat16
    )
    stacked = (
        by_block,
        jnp.moveaxis(temporal_context, 1, 0),
        jnp.moveaxis(grad_temporal_context, 1, 0),
    )
    grad_temporal_proj = jnp.moveaxis(
        lax.map(
            lambda items: temporal_backward(items[0], allowed_time, items[1], items[2]), stacked
        ),
        0,
        1,
    )
    grad_normed_two = project_back(grad_temporal_proj, temporal_weights[:, : 3 * model_width])
    grad_middle = (
        grad_out.astype(jnp.float32)
        + norm_backward(middle_block, temporal_gain, inverse_two, grad_normed_two)
    ).astype(jnp.bfloat16)
    grad_middle_time = lax.all_to_all(grad_middle, ("outer", "core"), split_axis=0, concat_axis=1, tiled=True)
    normed_cols = normed_two
    context_cols = temporal_context
    temporal_grad = scatter_rows(
        jnp.concatenate(
            [weight_term(normed_cols, grad_temporal_proj), weight_term(context_cols, grad_out)],
            axis=1,
        )
    )
    spatial_term = weight_term(spatial_context, grad_middle_time)
    spatial_term, grad_middle_time = lax.optimization_barrier((spatial_term, grad_middle_time))
    grad_spatial_context = project_back(
        grad_middle_time, spatial_weights[:, 3 * model_width :]
    ).astype(jnp.bfloat16)
    grad_spatial_proj = spatial_backward_heads(
        spatial_proj, allowed_space, spatial_context, grad_spatial_context
    )
    spatial_term = reduce_rows(spatial_term)
    spatial_term, grad_spatial_proj = lax.optimization_barrier((spatial_term, grad_spatial_proj))
    grad_normed_one = project_back(grad_spatial_proj, spatial_weights[:, : 3 * model_width])
    grad_activity = (
        grad_middle_time.astype(jnp.float32)
        + norm_backward(activity, spatial_gain, inverse_one, grad_normed_one)
    ).astype(jnp.bfloat16)
    normed_cols = normed_one
    context_cols = spatial_context
    spatial_grad = jnp.concatenate(
        [
            reduce_rows(weight_term(normed_cols, grad_spatial_proj)),
            spatial_term,
        ],
        axis=1,
    )
    return (layer_out, grad_activity, spatial_grad, temporal_grad)


def solution(mesh):
    groups, wide = mesh.devices.shape
    mesh = Mesh(mesh.devices.reshape(groups, wide // 2, 2), ("groups", "outer", "core"))
    placed = (
        P(("groups", "outer", "core"), None, None),
        P("groups", ("outer", "core"), None),
        P(),
        P(),
        P(),
        P(),
        P(),
        P("groups"),
        P("groups"),
    )
    return jax.shard_map(
        per_device,
        mesh=mesh,
        in_specs=placed,
        out_specs=(
            P("groups", ("outer", "core"), None),
            P(("groups", "outer", "core"), None, None),
            P(("groups", "outer", "core"), None),
            P(("groups", "outer", "core"), None),
        ),
        check_vma=False,
    )
```

```python
import jax
import jax.numpy as jnp
from jax import lax
from jax.sharding import Mesh, PartitionSpec as P

HEADS = 8


eps_norm = 1e-05
block_channels = 128


def norm_inverse(rows):
    values = rows.astype(jnp.float32)
    return lax.rsqrt(jnp.mean(values * values, axis=-1, keepdims=True) + eps_norm)


def norm_forward(rows, gain):
    inverse = norm_inverse(rows)
    return ((rows.astype(jnp.float32) * inverse * gain).astype(jnp.bfloat16), inverse)


def norm_backward(rows, gain, inverse, grad_normed):
    values = rows.astype(jnp.float32)
    scaled = grad_normed * gain
    inner = jnp.mean(values * scaled, axis=-1, keepdims=True)
    return inverse * scaled - values * inverse * inverse * inverse * inner


def normalized_affinity(asking_vectors, lookup_array, admissible_pairs, sharpness_divisor):
    unnormalized_affinities = (
        jnp.einsum(
            "...uo,...ao->...ua", asking_vectors, lookup_array, preferred_element_type=jnp.float32
        )
        * sharpness_divisor
    )
    unnormalized_affinities = jnp.where(admissible_pairs, unnormalized_affinities, -1e30)
    row_max = jnp.max(unnormalized_affinities, axis=-1, keepdims=True)
    expo = jnp.exp(unnormalized_affinities - row_max)
    return expo / jnp.sum(expo, axis=-1, keepdims=True)


def compute_affinity_outputs(
    asking_vectors, lookup_array, payload_array, admissible_pairs, sharpness_divisor
):
    truncated_outcome = normalized_affinity(
        asking_vectors, lookup_array, admissible_pairs, sharpness_divisor
    ).astype(jnp.bfloat16)
    return jnp.einsum(
        "...qk,...kd->...qd", truncated_outcome, payload_array, preferred_element_type=jnp.float32
    ).astype(jnp.bfloat16)


def compute_affinity_derivatives(
    asking_vectors,
    lookup_array,
    payload_array,
    admissible_pairs,
    sharpness_divisor,
    combined_output,
    blended_output_derivative,
):
    coefficient_array = normalized_affinity(
        asking_vectors, lookup_array, admissible_pairs, sharpness_divisor
    )
    truncated_outcome = coefficient_array.astype(jnp.bfloat16)
    grad_values = jnp.einsum(
        "...qk,...qd->...kd",
        truncated_outcome,
        blended_output_derivative,
        preferred_element_type=jnp.float32,
    )
    coefficient_derivative = jnp.einsum(
        "...uo,...ao->...ua",
        blended_output_derivative,
        payload_array,
        preferred_element_type=jnp.float32,
    )
    paired_inner_sums = jnp.sum(
        blended_output_derivative.astype(jnp.float32) * combined_output.astype(jnp.float32),
        axis=-1,
        keepdims=True,
    )
    affinity_derivative = (
        coefficient_array * (coefficient_derivative - paired_inner_sums) * sharpness_divisor
    ).astype(jnp.bfloat16)
    grad_queries = jnp.einsum(
        "...qk,...kd->...qd", affinity_derivative, lookup_array, preferred_element_type=jnp.float32
    )
    grad_keys = jnp.einsum(
        "...qk,...qd->...kd",
        affinity_derivative,
        asking_vectors,
        preferred_element_type=jnp.float32,
    )
    return (
        grad_queries.astype(jnp.bfloat16),
        grad_keys.astype(jnp.bfloat16),
        grad_values.astype(jnp.bfloat16),
    )


def temporal_split(projected):
    pieces = projected.reshape(projected.shape[0], 3, HEADS, projected.shape[1] // (3 * HEADS))
    return [pieces[:, index].transpose(1, 0, 2) for index in range(3)]


def temporal_forward(projected, admissible_pairs):
    asking_vectors, lookup_array, payload_array = temporal_split(projected)
    sharpness_divisor = float(asking_vectors.shape[-1]) ** (-0.5)
    combined_output = compute_affinity_outputs(
        asking_vectors, lookup_array, payload_array, admissible_pairs[None], sharpness_divisor
    )
    return combined_output.transpose(1, 0, 2).reshape(projected.shape[0], -1)


def temporal_backward(projected, admissible_pairs, combined_output, blended_output_derivative):
    asking_vectors, lookup_array, payload_array = temporal_split(projected)
    sharpness_divisor = float(asking_vectors.shape[-1]) ** (-0.5)
    bins = projected.shape[0]
    subspace_outputs = combined_output.reshape(bins, HEADS, -1).transpose(1, 0, 2)
    subspace_derivative = blended_output_derivative.reshape(bins, HEADS, -1).transpose(1, 0, 2)
    derivative_collection = compute_affinity_derivatives(
        asking_vectors,
        lookup_array,
        payload_array,
        admissible_pairs[None],
        sharpness_divisor,
        subspace_outputs,
        subspace_derivative,
    )
    return jnp.stack(derivative_collection, axis=0).transpose(2, 0, 1, 3).reshape(bins, -1)


def spatial_split(projected):
    pieces = projected.reshape(
        projected.shape[0], projected.shape[1], 3, HEADS, projected.shape[2] // (3 * HEADS)
    )
    return [pieces[:, :, index].transpose(0, 2, 1, 3) for index in range(3)]


def spatial_forward(projected, admissible_pairs):
    asking_vectors, lookup_array, payload_array = spatial_split(projected)
    sharpness_divisor = float(asking_vectors.shape[-1]) ** (-0.5)
    combined_output = compute_affinity_outputs(
        asking_vectors, lookup_array, payload_array, admissible_pairs, sharpness_divisor
    )
    return combined_output.transpose(0, 2, 1, 3).reshape(projected.shape[0], projected.shape[1], -1)


def spatial_backward(projected, admissible_pairs, combined_output, blended_output_derivative):
    asking_vectors, lookup_array, payload_array = spatial_split(projected)
    sharpness_divisor = float(asking_vectors.shape[-1]) ** (-0.5)
    bins, blocks = (projected.shape[0], projected.shape[1])
    subspace_outputs = combined_output.reshape(bins, blocks, HEADS, -1).transpose(0, 2, 1, 3)
    subspace_derivative = blended_output_derivative.reshape(bins, blocks, HEADS, -1).transpose(
        0, 2, 1, 3
    )
    derivative_collection = compute_affinity_derivatives(
        asking_vectors,
        lookup_array,
        payload_array,
        admissible_pairs,
        sharpness_divisor,
        subspace_outputs,
        subspace_derivative,
    )
    return (
        jnp.stack(derivative_collection, axis=0).transpose(1, 3, 0, 2, 4).reshape(bins, blocks, -1)
    )


def head_mask(width):
    column_head = jnp.arange(width, dtype=jnp.int32) // (width // HEADS)
    return column_head[None, :] == jnp.arange(HEADS, dtype=jnp.int32)[:, None]


def masked_rows(rows):
    keep = head_mask(rows.shape[-1])[None, :, None, :]
    return jnp.where(keep, rows[:, None, :, :], jnp.zeros((), rows.dtype))


def masked_cols(rows):
    keep = head_mask(rows.shape[-1])[None, None, :, :]
    return jnp.where(keep, rows[:, :, None, :], jnp.zeros((), rows.dtype))


def spatial_probs(asking, lookup, admissible_pairs, sharpness_divisor):
    scores = (
        jnp.einsum(
            "tbd,thcd->tbhc", asking, masked_rows(lookup), preferred_element_type=jnp.float32
        )
        * sharpness_divisor
    )
    scores = jnp.where(admissible_pairs[:, 0][:, :, None, :], scores, -1e30)
    row_max = jnp.max(scores, axis=-1, keepdims=True)
    expo = jnp.exp(scores - row_max)
    return expo / jnp.sum(expo, axis=-1, keepdims=True)


def spatial_forward_heads(projected, admissible_pairs):
    width = projected.shape[-1] // 3
    asking, lookup, payload = [projected[..., i * width : (i + 1) * width] for i in range(3)]
    sharpness_divisor = float(width // HEADS) ** (-0.5)
    probs = spatial_probs(asking, lookup, admissible_pairs, sharpness_divisor).astype(jnp.bfloat16)
    return jnp.einsum(
        "tbhc,thcd->tbd", probs, masked_rows(payload), preferred_element_type=jnp.float32
    ).astype(jnp.bfloat16)


def spatial_backward_heads(projected, admissible_pairs, combined_output, output_derivative):
    width = projected.shape[-1] // 3
    asking, lookup, payload = [projected[..., i * width : (i + 1) * width] for i in range(3)]
    sharpness_divisor = float(width // HEADS) ** (-0.5)
    bins, blocks = projected.shape[0], projected.shape[1]
    probs = spatial_probs(asking, lookup, admissible_pairs, sharpness_divisor)
    grad_values = jnp.einsum(
        "tbhc,tbhd->tcd",
        probs.astype(jnp.bfloat16),
        masked_cols(output_derivative),
        preferred_element_type=jnp.float32,
    )
    probs_derivative = jnp.einsum(
        "tbd,thcd->tbhc", output_derivative, masked_rows(payload), preferred_element_type=jnp.float32
    )
    inner = jnp.einsum(
        "tbd,hd->tbh",
        output_derivative.astype(jnp.float32) * combined_output.astype(jnp.float32),
        head_mask(width).astype(jnp.float32),
        precision=lax.Precision.HIGHEST,
        preferred_element_type=jnp.float32,
    )[..., None]
    scores_derivative = (probs * (probs_derivative - inner) * sharpness_divisor).astype(
        jnp.bfloat16
    )
    grad_queries = jnp.einsum(
        "tbhc,thcd->tbd", scores_derivative, masked_rows(lookup), preferred_element_type=jnp.float32
    )
    grad_keys = jnp.einsum(
        "tbhc,tbhd->tcd", scores_derivative, masked_cols(asking), preferred_element_type=jnp.float32
    )
    return jnp.concatenate(
        [grad_queries.astype(jnp.bfloat16), grad_keys.astype(jnp.bfloat16), grad_values.astype(jnp.bfloat16)],
        axis=-1,
    )


def spatial_allowed(sessions_here, channel_count, adjacency):
    block_count = adjacency.shape[0]
    block_ids = jnp.arange(block_count, dtype=jnp.int32)
    session_pick = (
        sessions_here[:, None] == jnp.arange(channel_count.shape[0], dtype=jnp.int32)[None, :]
    ).astype(jnp.int32)
    count_rows = jnp.sum(session_pick * channel_count[None, :], axis=1)
    live_block = block_ids[None, :] * block_channels < count_rows[:, None]
    linked = adjacency > 0
    itself = block_ids[:, None] == block_ids[None, :]
    admissible_pairs = linked[None, :, :] & live_block[:, None, :] | itself[None, :, :]
    return admissible_pairs[:, None, :, :]


def project(rows, coefficient_array):
    return jnp.einsum("tbd,de->tbe", rows, coefficient_array, preferred_element_type=jnp.float32)


def project_back(derivative_collection, coefficient_array):
    return jnp.einsum(
        "tbe,de->tbd", derivative_collection, coefficient_array, preferred_element_type=jnp.float32
    )


def weight_term(left, right):
    return jnp.einsum("tbd,tbe->de", left, right, preferred_element_type=jnp.float32)


def reduce_rows(partial):
    rows, cols = partial.shape
    outer = lax.psum(1, "outer")
    pieces = partial.reshape(outer, 2, rows // (2 * outer), cols)
    first = lax.axis_index("core") == 0
    kept = jnp.where(first, pieces[:, 0], pieces[:, 1])
    given = jnp.where(first, pieces[:, 1], pieces[:, 0]).astype(jnp.bfloat16)
    taken = lax.ppermute(given, "core", [(0, 1), (1, 0)])
    pieces = (kept + taken.astype(jnp.float32)).astype(jnp.bfloat16)
    pieces = lax.all_to_all(pieces, "outer", 0, 0, tiled=True)
    return jnp.sum(pieces.astype(jnp.float32), axis=0)


def scatter_rows(partial):
    return lax.psum_scatter(
        partial.astype(jnp.bfloat16), ("outer", "core"), scatter_dimension=0, tiled=True
    ).astype(jnp.float32)


def per_device(
    activity,
    grad_out,
    spatial_weights,
    temporal_weights,
    spatial_gain,
    temporal_gain,
    adjacency,
    channel_count,
    session_id,
):
    local_bins = activity.shape[0]
    model_width = activity.shape[2]
    first_bin = (lax.axis_index("outer") * 2 + lax.axis_index("core")) * local_bins
    sessions_here = lax.dynamic_slice_in_dim(session_id, first_bin, local_bins)
    normed_one, inverse_one = norm_forward(activity, spatial_gain)
    spatial_proj = project(normed_one, spatial_weights[:, : 3 * model_width]).astype(jnp.bfloat16)
    allowed_space = spatial_allowed(sessions_here, channel_count, adjacency)
    spatial_context = spatial_forward_heads(spatial_proj, allowed_space)
    middle = (
        jnp.swapaxes(activity, 0, 1).astype(jnp.float32)
        + jnp.einsum(
            "tbd,de->bte",
            spatial_context,
            spatial_weights[:, 3 * model_width :],
            preferred_element_type=jnp.float32,
        )
    ).astype(jnp.bfloat16)
    middle_block = lax.all_to_all(
        middle, ("outer", "core"), split_axis=0, concat_axis=1, tiled=True
    ).reshape(session_id.shape[0], 1, model_width)
    normed_two, inverse_two = norm_forward(middle_block, temporal_gain)
    temporal_proj = project(normed_two, temporal_weights[:, : 3 * model_width]).astype(jnp.bfloat16)
    allowed_time = session_id[:, None] == session_id[None, :]
    by_block = jnp.moveaxis(temporal_proj, 1, 0)
    temporal_context = jnp.moveaxis(
        lax.map(lambda block_rows: temporal_forward(block_rows, allowed_time), by_block), 0, 1
    )
    layer_out = (
        middle_block.astype(jnp.float32)
        + project(temporal_context, temporal_weights[:, 3 * model_width :])
    ).astype(jnp.bfloat16)
    grad_temporal_context = project_back(grad_out, temporal_weights[:, 3 * model_width :]).astype(
        jnp.bfloat16
    )
    stacked = (
        by_block,
        jnp.moveaxis(temporal_context, 1, 0),
        jnp.moveaxis(grad_temporal_context, 1, 0),
    )
    grad_temporal_proj = jnp.moveaxis(
        lax.map(
            lambda items: temporal_backward(items[0], allowed_time, items[1], items[2]), stacked
        ),
        0,
        1,
    )
    grad_normed_two = project_back(grad_temporal_proj, temporal_weights[:, : 3 * model_width])
    grad_middle = (
        grad_out.astype(jnp.float32)
        + norm_backward(middle_block, temporal_gain, inverse_two, grad_normed_two)
    ).astype(jnp.bfloat16)
    grad_middle_time = lax.all_to_all(grad_middle, ("outer", "core"), split_axis=0, concat_axis=1, tiled=True)
    normed_cols = normed_two
    context_cols = temporal_context
    temporal_grad = scatter_rows(
        jnp.concatenate(
            [weight_term(normed_cols, grad_temporal_proj), weight_term(context_cols, grad_out)],
            axis=1,
        )
    )
    spatial_term = weight_term(spatial_context, grad_middle_time)
    spatial_term, grad_middle_time = lax.optimization_barrier((spatial_term, grad_middle_time))
    grad_spatial_context = project_back(
        grad_middle_time, spatial_weights[:, 3 * model_width :]
    ).astype(jnp.bfloat16)
    grad_spatial_proj = spatial_backward_heads(
        spatial_proj, allowed_space, spatial_context, grad_spatial_context
    )
    spatial_term = reduce_rows(spatial_term)
    spatial_term, grad_spatial_proj = lax.optimization_barrier((spatial_term, grad_spatial_proj))
    grad_normed_one = project_back(grad_spatial_proj, spatial_weights[:, : 3 * model_width])
    grad_activity = (
        grad_middle_time.astype(jnp.float32)
        + norm_backward(activity, spatial_gain, inverse_one, grad_normed_one)
    ).astype(jnp.bfloat16)
    normed_cols = normed_one
    context_cols = spatial_context
    spatial_grad = jnp.concatenate(
        [
            reduce_rows(weight_term(normed_cols, grad_spatial_proj)),
            spatial_term,
        ],
        axis=1,
    )
    return (layer_out, grad_activity, spatial_grad, temporal_grad)


def solution(mesh):
    groups, wide = mesh.devices.shape
    mesh = Mesh(mesh.devices.reshape(groups, wide // 2, 2), ("groups", "outer", "core"))
    placed = (
        P(("groups", "outer", "core"), None, None),
        P("groups", ("outer", "core"), None),
        P(),
        P(),
        P(),
        P(),
        P(),
        P("groups"),
        P("groups"),
    )
    return jax.shard_map(
        per_device,
        mesh=mesh,
        in_specs=placed,
        out_specs=(
            P("groups", ("outer", "core"), None),
            P(("groups", "outer", "core"), None, None),
            P(("groups", "outer", "core"), None),
            P(("groups", "outer", "core"), None),
        ),
        check_vma=False,
    )
```

```python
import jax
import jax.numpy as jnp
from jax import lax
from jax.sharding import Mesh, PartitionSpec as P

HEADS = 8


eps_norm = 1e-05
block_channels = 128


def norm_inverse(rows):
    values = rows.astype(jnp.float32)
    return lax.rsqrt(jnp.mean(values * values, axis=-1, keepdims=True) + eps_norm)


def norm_forward(rows, gain):
    inverse = norm_inverse(rows)
    return ((rows.astype(jnp.float32) * inverse * gain).astype(jnp.bfloat16), inverse)


def norm_backward(rows, gain, inverse, grad_normed):
    values = rows.astype(jnp.float32)
    scaled = grad_normed * gain
    inner = jnp.mean(values * scaled, axis=-1, keepdims=True)
    return inverse * scaled - values * inverse * inverse * inverse * inner


def normalized_affinity(asking_vectors, lookup_array, admissible_pairs, sharpness_divisor):
    unnormalized_affinities = (
        jnp.einsum(
            "...uo,...ao->...ua", asking_vectors, lookup_array, preferred_element_type=jnp.float32
        )
        * sharpness_divisor
    )
    unnormalized_affinities = jnp.where(admissible_pairs, unnormalized_affinities, -1e30)
    row_max = jnp.max(unnormalized_affinities, axis=-1, keepdims=True)
    expo = jnp.exp(unnormalized_affinities - row_max)
    return expo / jnp.sum(expo, axis=-1, keepdims=True)


def compute_affinity_outputs(
    asking_vectors, lookup_array, payload_array, admissible_pairs, sharpness_divisor
):
    truncated_outcome = normalized_affinity(
        asking_vectors, lookup_array, admissible_pairs, sharpness_divisor
    ).astype(jnp.bfloat16)
    return jnp.einsum(
        "...qk,...kd->...qd", truncated_outcome, payload_array, preferred_element_type=jnp.float32
    ).astype(jnp.bfloat16)


def compute_affinity_derivatives(
    asking_vectors,
    lookup_array,
    payload_array,
    admissible_pairs,
    sharpness_divisor,
    combined_output,
    blended_output_derivative,
):
    coefficient_array = normalized_affinity(
        asking_vectors, lookup_array, admissible_pairs, sharpness_divisor
    )
    truncated_outcome = coefficient_array.astype(jnp.bfloat16)
    grad_values = jnp.einsum(
        "...qk,...qd->...kd",
        truncated_outcome,
        blended_output_derivative,
        preferred_element_type=jnp.float32,
    )
    coefficient_derivative = jnp.einsum(
        "...uo,...ao->...ua",
        blended_output_derivative,
        payload_array,
        preferred_element_type=jnp.float32,
    )
    paired_inner_sums = jnp.sum(
        blended_output_derivative.astype(jnp.float32) * combined_output.astype(jnp.float32),
        axis=-1,
        keepdims=True,
    )
    affinity_derivative = (
        coefficient_array * (coefficient_derivative - paired_inner_sums) * sharpness_divisor
    ).astype(jnp.bfloat16)
    grad_queries = jnp.einsum(
        "...qk,...kd->...qd", affinity_derivative, lookup_array, preferred_element_type=jnp.float32
    )
    grad_keys = jnp.einsum(
        "...qk,...qd->...kd",
        affinity_derivative,
        asking_vectors,
        preferred_element_type=jnp.float32,
    )
    return (
        grad_queries.astype(jnp.bfloat16),
        grad_keys.astype(jnp.bfloat16),
        grad_values.astype(jnp.bfloat16),
    )


def temporal_split(projected):
    return [
        part.reshape(part.shape[0], HEADS, part.shape[1] // HEADS).transpose(1, 0, 2)
        for part in projected
    ]


def temporal_forward(projected, admissible_pairs):
    asking_vectors, lookup_array, payload_array = temporal_split(projected)
    sharpness_divisor = float(asking_vectors.shape[-1]) ** (-0.5)
    combined_output = compute_affinity_outputs(
        asking_vectors, lookup_array, payload_array, admissible_pairs[None], sharpness_divisor
    )
    return combined_output.transpose(1, 0, 2).reshape(projected[0].shape[0], -1)


def temporal_backward(projected, admissible_pairs, combined_output, blended_output_derivative):
    asking_vectors, lookup_array, payload_array = temporal_split(projected)
    sharpness_divisor = float(asking_vectors.shape[-1]) ** (-0.5)
    bins = projected[0].shape[0]
    subspace_outputs = combined_output.reshape(bins, HEADS, -1).transpose(1, 0, 2)
    subspace_derivative = blended_output_derivative.reshape(bins, HEADS, -1).transpose(1, 0, 2)
    derivative_collection = compute_affinity_derivatives(
        asking_vectors,
        lookup_array,
        payload_array,
        admissible_pairs[None],
        sharpness_divisor,
        subspace_outputs,
        subspace_derivative,
    )
    return jnp.stack(derivative_collection, axis=0).transpose(2, 0, 1, 3).reshape(bins, -1)


def spatial_split(projected):
    pieces = projected.reshape(
        projected.shape[0], projected.shape[1], 3, HEADS, projected.shape[2] // (3 * HEADS)
    )
    return [pieces[:, :, index].transpose(0, 2, 1, 3) for index in range(3)]


def spatial_forward(projected, admissible_pairs):
    asking_vectors, lookup_array, payload_array = spatial_split(projected)
    sharpness_divisor = float(asking_vectors.shape[-1]) ** (-0.5)
    combined_output = compute_affinity_outputs(
        asking_vectors, lookup_array, payload_array, admissible_pairs, sharpness_divisor
    )
    return combined_output.transpose(0, 2, 1, 3).reshape(projected.shape[0], projected.shape[1], -1)


def spatial_backward(projected, admissible_pairs, combined_output, blended_output_derivative):
    asking_vectors, lookup_array, payload_array = spatial_split(projected)
    sharpness_divisor = float(asking_vectors.shape[-1]) ** (-0.5)
    bins, blocks = (projected.shape[0], projected.shape[1])
    subspace_outputs = combined_output.reshape(bins, blocks, HEADS, -1).transpose(0, 2, 1, 3)
    subspace_derivative = blended_output_derivative.reshape(bins, blocks, HEADS, -1).transpose(
        0, 2, 1, 3
    )
    derivative_collection = compute_affinity_derivatives(
        asking_vectors,
        lookup_array,
        payload_array,
        admissible_pairs,
        sharpness_divisor,
        subspace_outputs,
        subspace_derivative,
    )
    return (
        jnp.stack(derivative_collection, axis=0).transpose(1, 3, 0, 2, 4).reshape(bins, blocks, -1)
    )


def head_mask(width):
    column_head = jnp.arange(width, dtype=jnp.int32) // (width // HEADS)
    return column_head[None, :] == jnp.arange(HEADS, dtype=jnp.int32)[:, None]


def masked_rows(rows):
    keep = head_mask(rows.shape[-1])[None, :, None, :]
    return jnp.where(keep, rows[:, None, :, :], jnp.zeros((), rows.dtype))


def masked_cols(rows):
    keep = head_mask(rows.shape[-1])[None, None, :, :]
    return jnp.where(keep, rows[:, :, None, :], jnp.zeros((), rows.dtype))


def spatial_probs(asking, lookup, admissible_pairs, sharpness_divisor):
    scores = (
        jnp.einsum(
            "tbd,thcd->tbhc", asking, masked_rows(lookup), preferred_element_type=jnp.float32
        )
        * sharpness_divisor
    )
    scores = jnp.where(admissible_pairs[:, 0][:, :, None, :], scores, -1e30)
    row_max = jnp.max(scores, axis=-1, keepdims=True)
    expo = jnp.exp(scores - row_max)
    return expo / jnp.sum(expo, axis=-1, keepdims=True)


def spatial_forward_heads(projected, admissible_pairs):
    width = projected.shape[-1] // 3
    asking, lookup, payload = [projected[..., i * width : (i + 1) * width] for i in range(3)]
    sharpness_divisor = float(width // HEADS) ** (-0.5)
    probs = spatial_probs(asking, lookup, admissible_pairs, sharpness_divisor).astype(jnp.bfloat16)
    return jnp.einsum(
        "tbhc,thcd->tbd", probs, masked_rows(payload), preferred_element_type=jnp.float32
    ).astype(jnp.bfloat16)


def spatial_backward_heads(projected, admissible_pairs, combined_output, output_derivative):
    width = projected.shape[-1] // 3
    asking, lookup, payload = [projected[..., i * width : (i + 1) * width] for i in range(3)]
    sharpness_divisor = float(width // HEADS) ** (-0.5)
    bins, blocks = projected.shape[0], projected.shape[1]
    probs = spatial_probs(asking, lookup, admissible_pairs, sharpness_divisor)
    grad_values = jnp.einsum(
        "tbhc,tbhd->tcd",
        probs.astype(jnp.bfloat16),
        masked_cols(output_derivative),
        preferred_element_type=jnp.float32,
    )
    probs_derivative = jnp.einsum(
        "tbd,thcd->tbhc", output_derivative, masked_rows(payload), preferred_element_type=jnp.float32
    )
    inner = jnp.einsum(
        "tbd,hd->tbh",
        output_derivative.astype(jnp.float32) * combined_output.astype(jnp.float32),
        head_mask(width).astype(jnp.float32),
        precision=lax.Precision.HIGHEST,
        preferred_element_type=jnp.float32,
    )[..., None]
    scores_derivative = (probs * (probs_derivative - inner) * sharpness_divisor).astype(
        jnp.bfloat16
    )
    grad_queries = jnp.einsum(
        "tbhc,thcd->tbd", scores_derivative, masked_rows(lookup), preferred_element_type=jnp.float32
    )
    grad_keys = jnp.einsum(
        "tbhc,tbhd->tcd", scores_derivative, masked_cols(asking), preferred_element_type=jnp.float32
    )
    return jnp.concatenate(
        [grad_queries.astype(jnp.bfloat16), grad_keys.astype(jnp.bfloat16), grad_values.astype(jnp.bfloat16)],
        axis=-1,
    )


def spatial_allowed(sessions_here, channel_count, adjacency):
    block_count = adjacency.shape[0]
    block_ids = jnp.arange(block_count, dtype=jnp.int32)
    session_pick = (
        sessions_here[:, None] == jnp.arange(channel_count.shape[0], dtype=jnp.int32)[None, :]
    ).astype(jnp.int32)
    count_rows = jnp.sum(session_pick * channel_count[None, :], axis=1)
    live_block = block_ids[None, :] * block_channels < count_rows[:, None]
    linked = adjacency > 0
    itself = block_ids[:, None] == block_ids[None, :]
    admissible_pairs = linked[None, :, :] & live_block[:, None, :] | itself[None, :, :]
    return admissible_pairs[:, None, :, :]


def project(rows, coefficient_array):
    return jnp.einsum("tbd,de->tbe", rows, coefficient_array, preferred_element_type=jnp.float32)


def project_back(derivative_collection, coefficient_array):
    return jnp.einsum(
        "tbe,de->tbd", derivative_collection, coefficient_array, preferred_element_type=jnp.float32
    )


def weight_term(left, right):
    return jnp.einsum("tbd,tbe->de", left, right, preferred_element_type=jnp.float32)


def reduce_rows(partial):
    rows, cols = partial.shape
    outer = lax.psum(1, "outer")
    pieces = partial.reshape(outer, 2, rows // (2 * outer), cols)
    first = lax.axis_index("core") == 0
    kept = jnp.where(first, pieces[:, 0], pieces[:, 1])
    given = jnp.where(first, pieces[:, 1], pieces[:, 0]).astype(jnp.bfloat16)
    taken = lax.ppermute(given, "core", [(0, 1), (1, 0)])
    pieces = (kept + taken.astype(jnp.float32)).astype(jnp.bfloat16)
    pieces = lax.all_to_all(pieces, "outer", 0, 0, tiled=True)
    return jnp.sum(pieces.astype(jnp.float32), axis=0)


def scatter_rows(partial):
    return lax.psum_scatter(
        partial.astype(jnp.bfloat16), ("outer", "core"), scatter_dimension=0, tiled=True
    ).astype(jnp.float32)


def per_device(
    activity,
    grad_out,
    spatial_weights,
    temporal_weights,
    spatial_gain,
    temporal_gain,
    adjacency,
    channel_count,
    session_id,
):
    local_bins = activity.shape[0]
    model_width = activity.shape[2]
    first_bin = (lax.axis_index("outer") * 2 + lax.axis_index("core")) * local_bins
    sessions_here = lax.dynamic_slice_in_dim(session_id, first_bin, local_bins)
    normed_one, inverse_one = norm_forward(activity, spatial_gain)
    spatial_proj = project(normed_one, spatial_weights[:, : 3 * model_width]).astype(jnp.bfloat16)
    allowed_space = spatial_allowed(sessions_here, channel_count, adjacency)
    spatial_context = spatial_forward_heads(spatial_proj, allowed_space)
    middle = (
        activity.astype(jnp.float32)
        + project(spatial_context, spatial_weights[:, 3 * model_width :])
    ).astype(jnp.bfloat16)
    middle_block = lax.all_to_all(middle, ("outer", "core"), split_axis=1, concat_axis=0, tiled=True)
    normed_two, inverse_two = norm_forward(middle_block, temporal_gain)
    temporal_proj = tuple(
        project(normed_two, temporal_weights[:, i * model_width : (i + 1) * model_width]).astype(
            jnp.bfloat16
        )
        for i in range(3)
    )
    allowed_time = session_id[:, None] == session_id[None, :]
    by_block = tuple(jnp.moveaxis(part, 1, 0) for part in temporal_proj)
    temporal_context = jnp.moveaxis(
        lax.map(lambda block_rows: temporal_forward(block_rows, allowed_time), by_block), 0, 1
    )
    layer_out = (
        middle_block.astype(jnp.float32)
        + project(temporal_context, temporal_weights[:, 3 * model_width :])
    ).astype(jnp.bfloat16)
    grad_temporal_context = project_back(grad_out, temporal_weights[:, 3 * model_width :]).astype(
        jnp.bfloat16
    )
    stacked = (
        by_block,
        jnp.moveaxis(temporal_context, 1, 0),
        jnp.moveaxis(grad_temporal_context, 1, 0),
    )
    grad_temporal_proj = jnp.moveaxis(
        lax.map(
            lambda items: temporal_backward(items[0], allowed_time, items[1], items[2]), stacked
        ),
        0,
        1,
    )
    grad_normed_two = project_back(grad_temporal_proj, temporal_weights[:, : 3 * model_width])
    grad_middle = (
        grad_out.astype(jnp.float32)
        + norm_backward(middle_block, temporal_gain, inverse_two, grad_normed_two)
    ).astype(jnp.bfloat16)
    grad_middle_time = lax.all_to_all(grad_middle, ("outer", "core"), split_axis=0, concat_axis=1, tiled=True)
    normed_cols = normed_two
    context_cols = temporal_context
    temporal_grad = scatter_rows(
        jnp.concatenate(
            [weight_term(normed_cols, grad_temporal_proj), weight_term(context_cols, grad_out)],
            axis=1,
        )
    )
    spatial_term = weight_term(spatial_context, grad_middle_time)
    spatial_term, grad_middle_time = lax.optimization_barrier((spatial_term, grad_middle_time))
    grad_spatial_context = project_back(
        grad_middle_time, spatial_weights[:, 3 * model_width :]
    ).astype(jnp.bfloat16)
    grad_spatial_proj = spatial_backward_heads(
        spatial_proj, allowed_space, spatial_context, grad_spatial_context
    )
    spatial_term = reduce_rows(spatial_term)
    spatial_term, grad_spatial_proj = lax.optimization_barrier((spatial_term, grad_spatial_proj))
    grad_normed_one = project_back(grad_spatial_proj, spatial_weights[:, : 3 * model_width])
    grad_activity = (
        grad_middle_time.astype(jnp.float32)
        + norm_backward(activity, spatial_gain, inverse_one, grad_normed_one)
    ).astype(jnp.bfloat16)
    normed_cols = normed_one
    context_cols = spatial_context
    spatial_grad = jnp.concatenate(
        [
            reduce_rows(weight_term(normed_cols, grad_spatial_proj)),
            spatial_term,
        ],
        axis=1,
    )
    return (layer_out, grad_activity, spatial_grad, temporal_grad)


def solution(mesh):
    groups, wide = mesh.devices.shape
    mesh = Mesh(mesh.devices.reshape(groups, wide // 2, 2), ("groups", "outer", "core"))
    placed = (
        P(("groups", "outer", "core"), None, None),
        P("groups", ("outer", "core"), None),
        P(),
        P(),
        P(),
        P(),
        P(),
        P("groups"),
        P("groups"),
    )
    return jax.shard_map(
        per_device,
        mesh=mesh,
        in_specs=placed,
        out_specs=(
            P("groups", ("outer", "core"), None),
            P(("groups", "outer", "core"), None, None),
            P(("groups", "outer", "core"), None),
            P(("groups", "outer", "core"), None),
        ),
        check_vma=False,
    )
```

```python
import jax
import jax.numpy as jnp
from jax import lax
from jax.sharding import Mesh, PartitionSpec as P

HEADS = 8


eps_norm = 1e-05
block_channels = 128


def norm_inverse(rows):
    values = rows.astype(jnp.float32)
    return lax.rsqrt(jnp.mean(values * values, axis=-1, keepdims=True) + eps_norm)


def norm_forward(rows, gain):
    inverse = norm_inverse(rows)
    return ((rows.astype(jnp.float32) * inverse * gain).astype(jnp.bfloat16), inverse)


def norm_backward(rows, gain, inverse, grad_normed):
    values = rows.astype(jnp.float32)
    scaled = grad_normed * gain
    inner = jnp.mean(values * scaled, axis=-1, keepdims=True)
    return inverse * scaled - values * inverse * inverse * inverse * inner


def normalized_affinity(asking_vectors, lookup_array, admissible_pairs, sharpness_divisor):
    unnormalized_affinities = (
        jnp.einsum(
            "...uo,...ao->...ua", asking_vectors, lookup_array, preferred_element_type=jnp.float32
        )
        * sharpness_divisor
    )
    unnormalized_affinities = jnp.where(admissible_pairs, unnormalized_affinities, -1e30)
    row_max = jnp.max(unnormalized_affinities, axis=-1, keepdims=True)
    expo = jnp.exp(unnormalized_affinities - row_max)
    return expo / jnp.sum(expo, axis=-1, keepdims=True)


def compute_affinity_outputs(
    asking_vectors, lookup_array, payload_array, admissible_pairs, sharpness_divisor
):
    truncated_outcome = normalized_affinity(
        asking_vectors, lookup_array, admissible_pairs, sharpness_divisor
    ).astype(jnp.bfloat16)
    return jnp.einsum(
        "...qk,...kd->...qd", truncated_outcome, payload_array, preferred_element_type=jnp.float32
    ).astype(jnp.bfloat16)


def compute_affinity_derivatives(
    asking_vectors,
    lookup_array,
    payload_array,
    admissible_pairs,
    sharpness_divisor,
    combined_output,
    blended_output_derivative,
):
    coefficient_array = normalized_affinity(
        asking_vectors, lookup_array, admissible_pairs, sharpness_divisor
    )
    truncated_outcome = coefficient_array.astype(jnp.bfloat16)
    grad_values = jnp.einsum(
        "...qk,...qd->...kd",
        truncated_outcome,
        blended_output_derivative,
        preferred_element_type=jnp.float32,
    )
    coefficient_derivative = jnp.einsum(
        "...uo,...ao->...ua",
        blended_output_derivative,
        payload_array,
        preferred_element_type=jnp.float32,
    )
    paired_inner_sums = jnp.sum(
        blended_output_derivative.astype(jnp.float32) * combined_output.astype(jnp.float32),
        axis=-1,
        keepdims=True,
    )
    affinity_derivative = (
        coefficient_array * (coefficient_derivative - paired_inner_sums) * sharpness_divisor
    ).astype(jnp.bfloat16)
    grad_queries = jnp.einsum(
        "...qk,...kd->...qd", affinity_derivative, lookup_array, preferred_element_type=jnp.float32
    )
    grad_keys = jnp.einsum(
        "...qk,...qd->...kd",
        affinity_derivative,
        asking_vectors,
        preferred_element_type=jnp.float32,
    )
    return (
        grad_queries.astype(jnp.bfloat16),
        grad_keys.astype(jnp.bfloat16),
        grad_values.astype(jnp.bfloat16),
    )


def temporal_split(projected):
    pieces = projected.reshape(projected.shape[0], 3, HEADS, projected.shape[1] // (3 * HEADS))
    return [pieces[:, index].transpose(1, 0, 2) for index in range(3)]


def temporal_forward(projected, admissible_pairs):
    asking_vectors, lookup_array, payload_array = temporal_split(projected)
    sharpness_divisor = float(asking_vectors.shape[-1]) ** (-0.5)
    combined_output = compute_affinity_outputs(
        asking_vectors, lookup_array, payload_array, admissible_pairs[None], sharpness_divisor
    )
    return combined_output.transpose(1, 0, 2).reshape(projected.shape[0], -1)


def temporal_backward(projected, admissible_pairs, combined_output, blended_output_derivative):
    asking_vectors, lookup_array, payload_array = temporal_split(projected)
    sharpness_divisor = float(asking_vectors.shape[-1]) ** (-0.5)
    bins = projected.shape[0]
    subspace_outputs = combined_output.reshape(bins, HEADS, -1).transpose(1, 0, 2)
    subspace_derivative = blended_output_derivative.reshape(bins, HEADS, -1).transpose(1, 0, 2)
    derivative_collection = compute_affinity_derivatives(
        asking_vectors,
        lookup_array,
        payload_array,
        admissible_pairs[None],
        sharpness_divisor,
        subspace_outputs,
        subspace_derivative,
    )
    return jnp.stack(derivative_collection, axis=0).transpose(2, 0, 1, 3).reshape(bins, -1)


def spatial_split(projected):
    pieces = projected.reshape(
        projected.shape[0], projected.shape[1], 3, HEADS, projected.shape[2] // (3 * HEADS)
    )
    return [pieces[:, :, index].transpose(0, 2, 1, 3) for index in range(3)]


def spatial_forward(projected, admissible_pairs):
    asking_vectors, lookup_array, payload_array = spatial_split(projected)
    sharpness_divisor = float(asking_vectors.shape[-1]) ** (-0.5)
    combined_output = compute_affinity_outputs(
        asking_vectors, lookup_array, payload_array, admissible_pairs, sharpness_divisor
    )
    return combined_output.transpose(0, 2, 1, 3).reshape(projected.shape[0], projected.shape[1], -1)


def spatial_backward(projected, admissible_pairs, combined_output, blended_output_derivative):
    asking_vectors, lookup_array, payload_array = spatial_split(projected)
    sharpness_divisor = float(asking_vectors.shape[-1]) ** (-0.5)
    bins, blocks = (projected.shape[0], projected.shape[1])
    subspace_outputs = combined_output.reshape(bins, blocks, HEADS, -1).transpose(0, 2, 1, 3)
    subspace_derivative = blended_output_derivative.reshape(bins, blocks, HEADS, -1).transpose(
        0, 2, 1, 3
    )
    derivative_collection = compute_affinity_derivatives(
        asking_vectors,
        lookup_array,
        payload_array,
        admissible_pairs,
        sharpness_divisor,
        subspace_outputs,
        subspace_derivative,
    )
    return (
        jnp.stack(derivative_collection, axis=0).transpose(1, 3, 0, 2, 4).reshape(bins, blocks, -1)
    )


def head_mask(width):
    column_head = jnp.arange(width, dtype=jnp.int32) // (width // HEADS)
    return column_head[None, :] == jnp.arange(HEADS, dtype=jnp.int32)[:, None]


def masked_rows(rows):
    keep = head_mask(rows.shape[-1])[None, :, None, :]
    return jnp.where(keep, rows[:, None, :, :], jnp.zeros((), rows.dtype))


def masked_cols(rows):
    keep = head_mask(rows.shape[-1])[None, None, :, :]
    return jnp.where(keep, rows[:, :, None, :], jnp.zeros((), rows.dtype))


def spatial_probs(asking, lookup, admissible_pairs, sharpness_divisor):
    scores = (
        jnp.einsum(
            "tbd,thcd->tbhc", asking, masked_rows(lookup), preferred_element_type=jnp.float32
        )
        * sharpness_divisor
    )
    scores = jnp.where(admissible_pairs[:, 0][:, :, None, :], scores, -1e30)
    row_max = jnp.max(scores, axis=-1, keepdims=True)
    expo = jnp.exp(scores - row_max)
    return expo / jnp.sum(expo, axis=-1, keepdims=True)


def spatial_forward_heads(projected, admissible_pairs):
    width = projected.shape[-1] // 3
    asking, lookup, payload = [projected[..., i * width : (i + 1) * width] for i in range(3)]
    sharpness_divisor = float(width // HEADS) ** (-0.5)
    probs = spatial_probs(asking, lookup, admissible_pairs, sharpness_divisor).astype(jnp.bfloat16)
    return jnp.einsum(
        "tbhc,thcd->tbd", probs, masked_rows(payload), preferred_element_type=jnp.float32
    ).astype(jnp.bfloat16)


def spatial_backward_heads(projected, admissible_pairs, combined_output, output_derivative):
    width = projected.shape[-1] // 3
    asking, lookup, payload = [projected[..., i * width : (i + 1) * width] for i in range(3)]
    sharpness_divisor = float(width // HEADS) ** (-0.5)
    bins, blocks = projected.shape[0], projected.shape[1]
    probs = spatial_probs(asking, lookup, admissible_pairs, sharpness_divisor)
    grad_values = jnp.einsum(
        "tbhc,tbhd->tcd",
        probs.astype(jnp.bfloat16),
        masked_cols(output_derivative),
        preferred_element_type=jnp.float32,
    )
    probs_derivative = jnp.einsum(
        "tbd,thcd->tbhc", output_derivative, masked_rows(payload), preferred_element_type=jnp.float32
    )
    inner = jnp.einsum(
        "tbd,hd->tbh",
        output_derivative.astype(jnp.float32) * combined_output.astype(jnp.float32),
        head_mask(width).astype(jnp.float32),
        precision=lax.Precision.HIGHEST,
        preferred_element_type=jnp.float32,
    )[..., None]
    scores_derivative = (probs * (probs_derivative - inner) * sharpness_divisor).astype(
        jnp.bfloat16
    )
    grad_queries = jnp.einsum(
        "tbhc,thcd->tbd", scores_derivative, masked_rows(lookup), preferred_element_type=jnp.float32
    )
    grad_keys = jnp.einsum(
        "tbhc,tbhd->tcd", scores_derivative, masked_cols(asking), preferred_element_type=jnp.float32
    )
    return jnp.concatenate(
        [grad_queries.astype(jnp.bfloat16), grad_keys.astype(jnp.bfloat16), grad_values.astype(jnp.bfloat16)],
        axis=-1,
    )


def spatial_allowed(sessions_here, channel_count, adjacency):
    block_count = adjacency.shape[0]
    block_ids = jnp.arange(block_count, dtype=jnp.int32)
    session_pick = (
        sessions_here[:, None] == jnp.arange(channel_count.shape[0], dtype=jnp.int32)[None, :]
    ).astype(jnp.int32)
    count_rows = jnp.sum(session_pick * channel_count[None, :], axis=1)
    live_block = block_ids[None, :] * block_channels < count_rows[:, None]
    linked = adjacency > 0
    itself = block_ids[:, None] == block_ids[None, :]
    admissible_pairs = linked[None, :, :] & live_block[:, None, :] | itself[None, :, :]
    return admissible_pairs[:, None, :, :]


def project(rows, coefficient_array):
    return jnp.einsum("tbd,de->tbe", rows, coefficient_array, preferred_element_type=jnp.float32)


def project_back(derivative_collection, coefficient_array):
    return jnp.einsum(
        "tbe,de->tbd", derivative_collection, coefficient_array, preferred_element_type=jnp.float32
    )


def weight_term(left, right):
    return jnp.einsum("tbd,tbe->de", left, right, preferred_element_type=jnp.float32)


def reduce_rows(partial):
    rows, cols = partial.shape
    outer = lax.psum(1, "outer")
    pieces = partial.reshape(outer, 2, rows // (2 * outer), cols)
    first = lax.axis_index("core") == 0
    kept = jnp.where(first, pieces[:, 0], pieces[:, 1])
    given = jnp.where(first, pieces[:, 1], pieces[:, 0]).astype(jnp.bfloat16)
    taken = lax.ppermute(given, "core", [(0, 1), (1, 0)])
    pieces = (kept + taken.astype(jnp.float32)).astype(jnp.bfloat16)
    pieces = lax.all_to_all(pieces, "outer", 0, 0, tiled=True)
    return jnp.sum(pieces.astype(jnp.float32), axis=0)


def scatter_rows(partial):
    return lax.psum_scatter(
        partial.astype(jnp.bfloat16), ("outer", "core"), scatter_dimension=0, tiled=True
    ).astype(jnp.float32)


def per_device(
    activity,
    grad_out,
    spatial_weights,
    temporal_weights,
    spatial_gain,
    temporal_gain,
    adjacency,
    channel_count,
    session_id,
):
    local_bins = activity.shape[0]
    model_width = activity.shape[2]
    first_bin = (lax.axis_index("outer") * 2 + lax.axis_index("core")) * local_bins
    sessions_here = lax.dynamic_slice_in_dim(session_id, first_bin, local_bins)
    normed_one, inverse_one = norm_forward(activity, spatial_gain)
    spatial_proj = project(normed_one, spatial_weights[:, : 3 * model_width]).astype(jnp.bfloat16)
    allowed_space = spatial_allowed(sessions_here, channel_count, adjacency)
    spatial_context = spatial_forward_heads(spatial_proj, allowed_space)
    middle = (
        activity.astype(jnp.float32)
        + project(spatial_context, spatial_weights[:, 3 * model_width :])
    ).astype(jnp.bfloat16)
    middle_block = lax.all_to_all(middle, ("outer", "core"), split_axis=1, concat_axis=0, tiled=True)
    normed_two, inverse_two = norm_forward(middle_block, temporal_gain)
    temporal_proj = project(normed_two, temporal_weights[:, : 3 * model_width]).astype(jnp.bfloat16)
    allowed_time = session_id[:, None] == session_id[None, :]
    by_block = jnp.moveaxis(temporal_proj, 1, 0)
    temporal_context = jnp.moveaxis(
        lax.map(lambda block_rows: temporal_forward(block_rows, allowed_time), by_block), 0, 1
    )
    layer_out = (
        middle_block.astype(jnp.float32)
        + project(temporal_context, temporal_weights[:, 3 * model_width :])
    ).astype(jnp.bfloat16)
    grad_temporal_context = project_back(grad_out, temporal_weights[:, 3 * model_width :]).astype(
        jnp.bfloat16
    )
    stacked = (
        by_block,
        jnp.moveaxis(temporal_context, 1, 0),
        jnp.moveaxis(grad_temporal_context, 1, 0),
    )
    grad_temporal_proj = jnp.moveaxis(
        lax.map(
            lambda items: temporal_backward(items[0], allowed_time, items[1], items[2]), stacked
        ),
        0,
        1,
    )
    grad_normed_two = project_back(grad_temporal_proj, temporal_weights[:, : 3 * model_width])
    grad_middle = (
        grad_out.astype(jnp.float32)
        + norm_backward(middle_block, temporal_gain, inverse_two, grad_normed_two)
    ).astype(jnp.bfloat16)
    grad_middle_time = lax.all_to_all(grad_middle, ("outer", "core"), split_axis=0, concat_axis=1, tiled=True)
    normed_cols = normed_two
    context_cols = temporal_context
    temporal_grad = scatter_rows(
        jnp.concatenate(
            [weight_term(normed_cols, grad_temporal_proj), weight_term(context_cols, grad_out)],
            axis=1,
        )
    )
    spatial_term = weight_term(spatial_context, grad_middle_time)
    spatial_term, grad_middle_time = lax.optimization_barrier((spatial_term, grad_middle_time))
    grad_spatial_context = project_back(
        grad_middle_time, spatial_weights[:, 3 * model_width :]
    ).astype(jnp.bfloat16)
    grad_spatial_proj = spatial_backward_heads(
        spatial_proj, allowed_space, spatial_context, grad_spatial_context
    )
    grad_normed_one = project_back(grad_spatial_proj, spatial_weights[:, : 3 * model_width])
    grad_activity = (
        grad_middle_time.astype(jnp.float32)
        + norm_backward(activity, spatial_gain, inverse_one, grad_normed_one)
    ).astype(jnp.bfloat16)
    normed_term = weight_term(normed_one, grad_spatial_proj)
    spatial_term, normed_term, grad_activity = lax.optimization_barrier(
        (reduce_rows(spatial_term), normed_term, grad_activity)
    )
    spatial_grad = jnp.concatenate(
        [
            reduce_rows(normed_term),
            spatial_term,
        ],
        axis=1,
    )
    return (layer_out, grad_activity, spatial_grad, temporal_grad)


def solution(mesh):
    groups, wide = mesh.devices.shape
    mesh = Mesh(mesh.devices.reshape(groups, wide // 2, 2), ("groups", "outer", "core"))
    placed = (
        P(("groups", "outer", "core"), None, None),
        P("groups", ("outer", "core"), None),
        P(),
        P(),
        P(),
        P(),
        P(),
        P("groups"),
        P("groups"),
    )
    return jax.shard_map(
        per_device,
        mesh=mesh,
        in_specs=placed,
        out_specs=(
            P("groups", ("outer", "core"), None),
            P(("groups", "outer", "core"), None, None),
            P(("groups", "outer", "core"), None),
            P(("groups", "outer", "core"), None),
        ),
        check_vma=False,
    )
```

```python
import jax
import jax.numpy as jnp
from jax import lax
from jax.sharding import Mesh, PartitionSpec as P

HEADS = 8


eps_norm = 1e-05
block_channels = 128


def norm_inverse(rows):
    values = rows.astype(jnp.float32)
    return lax.rsqrt(jnp.mean(values * values, axis=-1, keepdims=True) + eps_norm)


def norm_forward(rows, gain):
    inverse = norm_inverse(rows)
    return ((rows.astype(jnp.float32) * inverse * gain).astype(jnp.bfloat16), inverse)


def norm_backward(rows, gain, inverse, grad_normed):
    values = rows.astype(jnp.float32)
    scaled = grad_normed * gain
    inner = jnp.mean(values * scaled, axis=-1, keepdims=True)
    return inverse * scaled - values * inverse * inverse * inverse * inner


def normalized_affinity(asking_vectors, lookup_array, admissible_pairs, sharpness_divisor):
    unnormalized_affinities = (
        jnp.einsum(
            "...uo,...ao->...ua", asking_vectors, lookup_array, preferred_element_type=jnp.float32
        )
        * sharpness_divisor
    )
    unnormalized_affinities = jnp.where(admissible_pairs, unnormalized_affinities, -1e30)
    row_max = jnp.max(unnormalized_affinities, axis=-1, keepdims=True)
    expo = jnp.exp(unnormalized_affinities - row_max)
    return expo / jnp.sum(expo, axis=-1, keepdims=True)


def compute_affinity_outputs(
    asking_vectors, lookup_array, payload_array, admissible_pairs, sharpness_divisor
):
    truncated_outcome = normalized_affinity(
        asking_vectors, lookup_array, admissible_pairs, sharpness_divisor
    ).astype(jnp.bfloat16)
    return jnp.einsum(
        "...qk,...kd->...qd", truncated_outcome, payload_array, preferred_element_type=jnp.float32
    ).astype(jnp.bfloat16)


def compute_affinity_derivatives(
    asking_vectors,
    lookup_array,
    payload_array,
    admissible_pairs,
    sharpness_divisor,
    combined_output,
    blended_output_derivative,
    paired_inner_sums=None,
):
    coefficient_array = normalized_affinity(
        asking_vectors, lookup_array, admissible_pairs, sharpness_divisor
    )
    truncated_outcome = coefficient_array.astype(jnp.bfloat16)
    grad_values = jnp.einsum(
        "...qk,...qd->...kd",
        truncated_outcome,
        blended_output_derivative,
        preferred_element_type=jnp.float32,
    )
    coefficient_derivative = jnp.einsum(
        "...uo,...ao->...ua",
        blended_output_derivative,
        payload_array,
        preferred_element_type=jnp.float32,
    )
    if paired_inner_sums is None:
        paired_inner_sums = jnp.sum(
            blended_output_derivative.astype(jnp.float32) * combined_output.astype(jnp.float32),
            axis=-1,
            keepdims=True,
        )
    affinity_derivative = (
        coefficient_array * (coefficient_derivative - paired_inner_sums) * sharpness_divisor
    ).astype(jnp.bfloat16)
    grad_queries = jnp.einsum(
        "...qk,...kd->...qd", affinity_derivative, lookup_array, preferred_element_type=jnp.float32
    )
    grad_keys = jnp.einsum(
        "...qk,...qd->...kd",
        affinity_derivative,
        asking_vectors,
        preferred_element_type=jnp.float32,
    )
    return (
        grad_queries.astype(jnp.bfloat16),
        grad_keys.astype(jnp.bfloat16),
        grad_values.astype(jnp.bfloat16),
    )


def temporal_split(projected):
    pieces = projected.reshape(projected.shape[0], 3, HEADS, projected.shape[1] // (3 * HEADS))
    return [pieces[:, index].transpose(1, 0, 2) for index in range(3)]


def temporal_forward(projected, admissible_pairs):
    asking_vectors, lookup_array, payload_array = temporal_split(projected)
    sharpness_divisor = float(asking_vectors.shape[-1]) ** (-0.5)
    combined_output = compute_affinity_outputs(
        asking_vectors, lookup_array, payload_array, admissible_pairs[None], sharpness_divisor
    )
    return combined_output.transpose(1, 0, 2).reshape(projected.shape[0], -1)


def temporal_backward(projected, admissible_pairs, combined_output, blended_output_derivative):
    asking_vectors, lookup_array, payload_array = temporal_split(projected)
    sharpness_divisor = float(asking_vectors.shape[-1]) ** (-0.5)
    bins = projected.shape[0]
    subspace_derivative = blended_output_derivative.reshape(bins, HEADS, -1).transpose(1, 0, 2)
    inner = jnp.einsum(
        "td,hd->ht",
        blended_output_derivative.astype(jnp.float32) * combined_output.astype(jnp.float32),
        head_mask(combined_output.shape[-1]).astype(jnp.float32),
        precision=lax.Precision.HIGHEST,
        preferred_element_type=jnp.float32,
    )[..., None]
    derivative_collection = compute_affinity_derivatives(
        asking_vectors,
        lookup_array,
        payload_array,
        admissible_pairs[None],
        sharpness_divisor,
        None,
        subspace_derivative,
        inner,
    )
    return jnp.stack(derivative_collection, axis=0).transpose(2, 0, 1, 3).reshape(bins, -1)


def spatial_split(projected):
    pieces = projected.reshape(
        projected.shape[0], projected.shape[1], 3, HEADS, projected.shape[2] // (3 * HEADS)
    )
    return [pieces[:, :, index].transpose(0, 2, 1, 3) for index in range(3)]


def spatial_forward(projected, admissible_pairs):
    asking_vectors, lookup_array, payload_array = spatial_split(projected)
    sharpness_divisor = float(asking_vectors.shape[-1]) ** (-0.5)
    combined_output = compute_affinity_outputs(
        asking_vectors, lookup_array, payload_array, admissible_pairs, sharpness_divisor
    )
    return combined_output.transpose(0, 2, 1, 3).reshape(projected.shape[0], projected.shape[1], -1)


def spatial_backward(projected, admissible_pairs, combined_output, blended_output_derivative):
    asking_vectors, lookup_array, payload_array = spatial_split(projected)
    sharpness_divisor = float(asking_vectors.shape[-1]) ** (-0.5)
    bins, blocks = (projected.shape[0], projected.shape[1])
    subspace_outputs = combined_output.reshape(bins, blocks, HEADS, -1).transpose(0, 2, 1, 3)
    subspace_derivative = blended_output_derivative.reshape(bins, blocks, HEADS, -1).transpose(
        0, 2, 1, 3
    )
    derivative_collection = compute_affinity_derivatives(
        asking_vectors,
        lookup_array,
        payload_array,
        admissible_pairs,
        sharpness_divisor,
        subspace_outputs,
        subspace_derivative,
    )
    return (
        jnp.stack(derivative_collection, axis=0).transpose(1, 3, 0, 2, 4).reshape(bins, blocks, -1)
    )


def head_mask(width):
    column_head = jnp.arange(width, dtype=jnp.int32) // (width // HEADS)
    return column_head[None, :] == jnp.arange(HEADS, dtype=jnp.int32)[:, None]


def masked_rows(rows):
    keep = head_mask(rows.shape[-1])[None, :, None, :]
    return jnp.where(keep, rows[:, None, :, :], jnp.zeros((), rows.dtype))


def masked_cols(rows):
    keep = head_mask(rows.shape[-1])[None, None, :, :]
    return jnp.where(keep, rows[:, :, None, :], jnp.zeros((), rows.dtype))


def spatial_probs(asking, lookup, admissible_pairs, sharpness_divisor):
    scores = (
        jnp.einsum(
            "tbd,thcd->tbhc", asking, masked_rows(lookup), preferred_element_type=jnp.float32
        )
        * sharpness_divisor
    )
    scores = jnp.where(admissible_pairs[:, 0][:, :, None, :], scores, -1e30)
    row_max = jnp.max(scores, axis=-1, keepdims=True)
    expo = jnp.exp(scores - row_max)
    return expo / jnp.sum(expo, axis=-1, keepdims=True)


def spatial_forward_heads(projected, admissible_pairs):
    width = projected.shape[-1] // 3
    asking, lookup, payload = [projected[..., i * width : (i + 1) * width] for i in range(3)]
    sharpness_divisor = float(width // HEADS) ** (-0.5)
    probs = spatial_probs(asking, lookup, admissible_pairs, sharpness_divisor).astype(jnp.bfloat16)
    return jnp.einsum(
        "tbhc,thcd->tbd", probs, masked_rows(payload), preferred_element_type=jnp.float32
    ).astype(jnp.bfloat16)


def spatial_backward_heads(projected, admissible_pairs, combined_output, output_derivative):
    width = projected.shape[-1] // 3
    asking, lookup, payload = [projected[..., i * width : (i + 1) * width] for i in range(3)]
    sharpness_divisor = float(width // HEADS) ** (-0.5)
    bins, blocks = projected.shape[0], projected.shape[1]
    probs = spatial_probs(asking, lookup, admissible_pairs, sharpness_divisor)
    grad_values = jnp.einsum(
        "tbhc,tbhd->tcd",
        probs.astype(jnp.bfloat16),
        masked_cols(output_derivative),
        preferred_element_type=jnp.float32,
    )
    probs_derivative = jnp.einsum(
        "tbd,thcd->tbhc", output_derivative, masked_rows(payload), preferred_element_type=jnp.float32
    )
    inner = jnp.einsum(
        "tbd,hd->tbh",
        output_derivative.astype(jnp.float32) * combined_output.astype(jnp.float32),
        head_mask(width).astype(jnp.float32),
        precision=lax.Precision.HIGHEST,
        preferred_element_type=jnp.float32,
    )[..., None]
    scores_derivative = (probs * (probs_derivative - inner) * sharpness_divisor).astype(
        jnp.bfloat16
    )
    grad_queries = jnp.einsum(
        "tbhc,thcd->tbd", scores_derivative, masked_rows(lookup), preferred_element_type=jnp.float32
    )
    grad_keys = jnp.einsum(
        "tbhc,tbhd->tcd", scores_derivative, masked_cols(asking), preferred_element_type=jnp.float32
    )
    return jnp.concatenate(
        [grad_queries.astype(jnp.bfloat16), grad_keys.astype(jnp.bfloat16), grad_values.astype(jnp.bfloat16)],
        axis=-1,
    )


def spatial_allowed(sessions_here, channel_count, adjacency):
    block_count = adjacency.shape[0]
    block_ids = jnp.arange(block_count, dtype=jnp.int32)
    session_pick = (
        sessions_here[:, None] == jnp.arange(channel_count.shape[0], dtype=jnp.int32)[None, :]
    ).astype(jnp.int32)
    count_rows = jnp.sum(session_pick * channel_count[None, :], axis=1)
    live_block = block_ids[None, :] * block_channels < count_rows[:, None]
    linked = adjacency > 0
    itself = block_ids[:, None] == block_ids[None, :]
    admissible_pairs = linked[None, :, :] & live_block[:, None, :] | itself[None, :, :]
    return admissible_pairs[:, None, :, :]


def project(rows, coefficient_array):
    return jnp.einsum("tbd,de->tbe", rows, coefficient_array, preferred_element_type=jnp.float32)


def project_back(derivative_collection, coefficient_array):
    return jnp.einsum(
        "tbe,de->tbd", derivative_collection, coefficient_array, preferred_element_type=jnp.float32
    )


def weight_term(left, right):
    return jnp.einsum("tbd,tbe->de", left, right, preferred_element_type=jnp.float32)


def reduce_rows(partial):
    rows, cols = partial.shape
    outer = lax.psum(1, "outer")
    pieces = partial.reshape(outer, 2, rows // (2 * outer), cols)
    first = lax.axis_index("core") == 0
    kept = jnp.where(first, pieces[:, 0], pieces[:, 1])
    given = jnp.where(first, pieces[:, 1], pieces[:, 0]).astype(jnp.bfloat16)
    taken = lax.ppermute(given, "core", [(0, 1), (1, 0)])
    pieces = (kept + taken.astype(jnp.float32)).astype(jnp.bfloat16)
    pieces = lax.all_to_all(pieces, "outer", 0, 0, tiled=True)
    return jnp.sum(pieces.astype(jnp.float32), axis=0)


def scatter_rows(partial):
    return lax.psum_scatter(
        partial.astype(jnp.bfloat16), ("outer", "core"), scatter_dimension=0, tiled=True
    ).astype(jnp.float32)


def per_device(
    activity,
    grad_out,
    spatial_weights,
    temporal_weights,
    spatial_gain,
    temporal_gain,
    adjacency,
    channel_count,
    session_id,
):
    local_bins = activity.shape[0]
    model_width = activity.shape[2]
    first_bin = (lax.axis_index("outer") * 2 + lax.axis_index("core")) * local_bins
    sessions_here = lax.dynamic_slice_in_dim(session_id, first_bin, local_bins)
    normed_one, inverse_one = norm_forward(activity, spatial_gain)
    spatial_proj = project(normed_one, spatial_weights[:, : 3 * model_width]).astype(jnp.bfloat16)
    allowed_space = spatial_allowed(sessions_here, channel_count, adjacency)
    spatial_context = spatial_forward_heads(spatial_proj, allowed_space)
    middle = (
        activity.astype(jnp.float32)
        + project(spatial_context, spatial_weights[:, 3 * model_width :])
    ).astype(jnp.bfloat16)
    middle_block = lax.all_to_all(middle, ("outer", "core"), split_axis=1, concat_axis=0, tiled=True)
    normed_two, inverse_two = norm_forward(middle_block, temporal_gain)
    temporal_proj = project(normed_two, temporal_weights[:, : 3 * model_width]).astype(jnp.bfloat16)
    allowed_time = session_id[:, None] == session_id[None, :]
    by_block = jnp.moveaxis(temporal_proj, 1, 0)
    temporal_context = jnp.moveaxis(
        lax.map(lambda block_rows: temporal_forward(block_rows, allowed_time), by_block), 0, 1
    )
    layer_out = (
        middle_block.astype(jnp.float32)
        + project(temporal_context, temporal_weights[:, 3 * model_width :])
    ).astype(jnp.bfloat16)
    grad_temporal_context = project_back(grad_out, temporal_weights[:, 3 * model_width :]).astype(
        jnp.bfloat16
    )
    stacked = (
        by_block,
        jnp.moveaxis(temporal_context, 1, 0),
        jnp.moveaxis(grad_temporal_context, 1, 0),
    )
    grad_temporal_proj = jnp.moveaxis(
        lax.map(
            lambda items: temporal_backward(items[0], allowed_time, items[1], items[2]), stacked
        ),
        0,
        1,
    )
    grad_normed_two = project_back(grad_temporal_proj, temporal_weights[:, : 3 * model_width])
    grad_middle = (
        grad_out.astype(jnp.float32)
        + norm_backward(middle_block, temporal_gain, inverse_two, grad_normed_two)
    ).astype(jnp.bfloat16)
    grad_middle_time = lax.all_to_all(grad_middle, ("outer", "core"), split_axis=0, concat_axis=1, tiled=True)
    normed_cols = normed_two
    context_cols = temporal_context
    temporal_grad = scatter_rows(
        jnp.concatenate(
            [weight_term(normed_cols, grad_temporal_proj), weight_term(context_cols, grad_out)],
            axis=1,
        )
    )
    spatial_term = weight_term(spatial_context, grad_middle_time)
    spatial_term, grad_middle_time = lax.optimization_barrier((spatial_term, grad_middle_time))
    grad_spatial_context = project_back(
        grad_middle_time, spatial_weights[:, 3 * model_width :]
    ).astype(jnp.bfloat16)
    grad_spatial_proj = spatial_backward_heads(
        spatial_proj, allowed_space, spatial_context, grad_spatial_context
    )
    spatial_term = reduce_rows(spatial_term)
    spatial_term, grad_spatial_proj = lax.optimization_barrier((spatial_term, grad_spatial_proj))
    grad_normed_one = project_back(grad_spatial_proj, spatial_weights[:, : 3 * model_width])
    grad_activity = (
        grad_middle_time.astype(jnp.float32)
        + norm_backward(activity, spatial_gain, inverse_one, grad_normed_one)
    ).astype(jnp.bfloat16)
    normed_cols = normed_one
    context_cols = spatial_context
    spatial_grad = jnp.concatenate(
        [
            reduce_rows(weight_term(normed_cols, grad_spatial_proj)),
            spatial_term,
        ],
        axis=1,
    )
    return (layer_out, grad_activity, spatial_grad, temporal_grad)


def solution(mesh):
    groups, wide = mesh.devices.shape
    mesh = Mesh(mesh.devices.reshape(groups, wide // 2, 2), ("groups", "outer", "core"))
    placed = (
        P(("groups", "outer", "core"), None, None),
        P("groups", ("outer", "core"), None),
        P(),
        P(),
        P(),
        P(),
        P(),
        P("groups"),
        P("groups"),
    )
    return jax.shard_map(
        per_device,
        mesh=mesh,
        in_specs=placed,
        out_specs=(
            P("groups", ("outer", "core"), None),
            P(("groups", "outer", "core"), None, None),
            P(("groups", "outer", "core"), None),
            P(("groups", "outer", "core"), None),
        ),
        check_vma=False,
    )
```

```python
import jax
import jax.numpy as jnp
from jax import lax
from jax.sharding import Mesh, PartitionSpec as P

HEADS = 8


eps_norm = 1e-05
block_channels = 128


def norm_inverse(rows):
    values = rows.astype(jnp.float32)
    return lax.rsqrt(jnp.mean(values * values, axis=-1, keepdims=True) + eps_norm)


def norm_forward(rows, gain):
    inverse = norm_inverse(rows)
    return ((rows.astype(jnp.float32) * inverse * gain).astype(jnp.bfloat16), inverse)


def norm_backward(rows, gain, inverse, grad_normed):
    values = rows.astype(jnp.float32)
    scaled = grad_normed * gain
    inner = jnp.mean(values * scaled, axis=-1, keepdims=True)
    return inverse * scaled - values * inverse * inverse * inverse * inner


def normalized_affinity(asking_vectors, lookup_array, admissible_pairs, sharpness_divisor):
    unnormalized_affinities = (
        jnp.einsum(
            "...uo,...ao->...ua", asking_vectors, lookup_array, preferred_element_type=jnp.float32
        )
        * sharpness_divisor
    )
    unnormalized_affinities = jnp.where(admissible_pairs, unnormalized_affinities, -1e30)
    row_max = jnp.max(unnormalized_affinities, axis=-1, keepdims=True)
    expo = jnp.exp(unnormalized_affinities - row_max)
    return expo / jnp.sum(expo, axis=-1, keepdims=True)


def compute_affinity_outputs(
    asking_vectors, lookup_array, payload_array, admissible_pairs, sharpness_divisor
):
    truncated_outcome = normalized_affinity(
        asking_vectors, lookup_array, admissible_pairs, sharpness_divisor
    ).astype(jnp.bfloat16)
    return jnp.einsum(
        "...qk,...kd->...qd", truncated_outcome, payload_array, preferred_element_type=jnp.float32
    ).astype(jnp.bfloat16)


def compute_affinity_derivatives(
    asking_vectors,
    lookup_array,
    payload_array,
    admissible_pairs,
    sharpness_divisor,
    combined_output,
    blended_output_derivative,
):
    coefficient_array = normalized_affinity(
        asking_vectors, lookup_array, admissible_pairs, sharpness_divisor
    )
    truncated_outcome = coefficient_array.astype(jnp.bfloat16)
    grad_values = jnp.einsum(
        "...qk,...qd->...kd",
        truncated_outcome,
        blended_output_derivative,
        preferred_element_type=jnp.float32,
    )
    coefficient_derivative = jnp.einsum(
        "...uo,...ao->...ua",
        blended_output_derivative,
        payload_array,
        preferred_element_type=jnp.float32,
    )
    paired_inner_sums = jnp.sum(
        blended_output_derivative.astype(jnp.float32) * combined_output.astype(jnp.float32),
        axis=-1,
        keepdims=True,
    )
    affinity_derivative = (
        coefficient_array * (coefficient_derivative - paired_inner_sums) * sharpness_divisor
    ).astype(jnp.bfloat16)
    grad_queries = jnp.einsum(
        "...qk,...kd->...qd", affinity_derivative, lookup_array, preferred_element_type=jnp.float32
    )
    grad_keys = jnp.einsum(
        "...qk,...qd->...kd",
        affinity_derivative,
        asking_vectors,
        preferred_element_type=jnp.float32,
    )
    return (
        grad_queries.astype(jnp.bfloat16),
        grad_keys.astype(jnp.bfloat16),
        grad_values.astype(jnp.bfloat16),
    )


def temporal_split(projected):
    pieces = projected.reshape(projected.shape[0], 3, HEADS, projected.shape[1] // (3 * HEADS))
    return [pieces[:, index].transpose(1, 0, 2) for index in range(3)]


def temporal_forward(projected, admissible_pairs):
    asking_vectors, lookup_array, payload_array = temporal_split(projected)
    sharpness_divisor = float(asking_vectors.shape[-1]) ** (-0.5)
    combined_output = compute_affinity_outputs(
        asking_vectors, lookup_array, payload_array, admissible_pairs[None], sharpness_divisor
    )
    return combined_output.transpose(1, 0, 2).reshape(projected.shape[0], -1)


def temporal_backward(projected, admissible_pairs, combined_output, blended_output_derivative):
    asking_vectors, lookup_array, payload_array = temporal_split(projected)
    sharpness_divisor = float(asking_vectors.shape[-1]) ** (-0.5)
    bins = projected.shape[0]
    subspace_outputs = combined_output.reshape(bins, HEADS, -1).transpose(1, 0, 2)
    subspace_derivative = blended_output_derivative.reshape(bins, HEADS, -1).transpose(1, 0, 2)
    derivative_collection = compute_affinity_derivatives(
        asking_vectors,
        lookup_array,
        payload_array,
        admissible_pairs[None],
        sharpness_divisor,
        subspace_outputs,
        subspace_derivative,
    )
    return jnp.stack(derivative_collection, axis=0).transpose(2, 0, 1, 3).reshape(bins, -1)


def spatial_split(projected):
    pieces = projected.reshape(
        projected.shape[0], projected.shape[1], 3, HEADS, projected.shape[2] // (3 * HEADS)
    )
    return [pieces[:, :, index].transpose(0, 2, 1, 3) for index in range(3)]


def spatial_forward(projected, admissible_pairs):
    asking_vectors, lookup_array, payload_array = spatial_split(projected)
    sharpness_divisor = float(asking_vectors.shape[-1]) ** (-0.5)
    combined_output = compute_affinity_outputs(
        asking_vectors, lookup_array, payload_array, admissible_pairs, sharpness_divisor
    )
    return combined_output.transpose(0, 2, 1, 3).reshape(projected.shape[0], projected.shape[1], -1)


def spatial_backward(projected, admissible_pairs, combined_output, blended_output_derivative):
    asking_vectors, lookup_array, payload_array = spatial_split(projected)
    sharpness_divisor = float(asking_vectors.shape[-1]) ** (-0.5)
    bins, blocks = (projected.shape[0], projected.shape[1])
    subspace_outputs = combined_output.reshape(bins, blocks, HEADS, -1).transpose(0, 2, 1, 3)
    subspace_derivative = blended_output_derivative.reshape(bins, blocks, HEADS, -1).transpose(
        0, 2, 1, 3
    )
    derivative_collection = compute_affinity_derivatives(
        asking_vectors,
        lookup_array,
        payload_array,
        admissible_pairs,
        sharpness_divisor,
        subspace_outputs,
        subspace_derivative,
    )
    return (
        jnp.stack(derivative_collection, axis=0).transpose(1, 3, 0, 2, 4).reshape(bins, blocks, -1)
    )


def head_mask(width):
    column_head = jnp.arange(width, dtype=jnp.int32) // (width // HEADS)
    return column_head[None, :] == jnp.arange(HEADS, dtype=jnp.int32)[:, None]


def masked_rows(rows):
    keep = head_mask(rows.shape[-1])[None, :, None, :]
    return jnp.where(keep, rows[:, None, :, :], jnp.zeros((), rows.dtype))


def masked_cols(rows):
    keep = head_mask(rows.shape[-1])[None, None, :, :]
    return jnp.where(keep, rows[:, :, None, :], jnp.zeros((), rows.dtype))


def spatial_probs(asking, lookup, admissible_pairs, sharpness_divisor):
    scores = (
        jnp.einsum(
            "tbd,thcd->tbhc", asking, masked_rows(lookup), preferred_element_type=jnp.float32
        )
        * sharpness_divisor
    )
    scores = jnp.where(admissible_pairs[:, 0][:, :, None, :], scores, -1e30)
    row_max = jnp.max(scores, axis=-1, keepdims=True)
    expo = jnp.exp(scores - row_max)
    return expo / jnp.sum(expo, axis=-1, keepdims=True)


def spatial_forward_heads(projected, admissible_pairs):
    width = projected.shape[-1] // 3
    asking, lookup, payload = [projected[..., i * width : (i + 1) * width] for i in range(3)]
    sharpness_divisor = float(width // HEADS) ** (-0.5)
    probs = spatial_probs(asking, lookup, admissible_pairs, sharpness_divisor).astype(jnp.bfloat16)
    return jnp.einsum(
        "tbhc,thcd->tbd", probs, masked_rows(payload), preferred_element_type=jnp.float32
    ).astype(jnp.bfloat16)


def spatial_backward_heads(projected, admissible_pairs, combined_output, output_derivative):
    width = projected.shape[-1] // 3
    asking, lookup, payload = [projected[..., i * width : (i + 1) * width] for i in range(3)]
    sharpness_divisor = float(width // HEADS) ** (-0.5)
    bins, blocks = projected.shape[0], projected.shape[1]
    probs = spatial_probs(asking, lookup, admissible_pairs, sharpness_divisor)
    grad_values = jnp.einsum(
        "tbhc,tbhd->tcd",
        probs.astype(jnp.bfloat16),
        masked_cols(output_derivative),
        preferred_element_type=jnp.float32,
    )
    probs_derivative = jnp.einsum(
        "tbd,thcd->tbhc", output_derivative, masked_rows(payload), preferred_element_type=jnp.float32
    )
    inner = jnp.einsum(
        "tbd,hd->tbh",
        output_derivative.astype(jnp.float32) * combined_output.astype(jnp.float32),
        head_mask(width).astype(jnp.float32),
        precision=lax.Precision.HIGHEST,
        preferred_element_type=jnp.float32,
    )[..., None]
    scores_derivative = (probs * (probs_derivative - inner) * sharpness_divisor).astype(
        jnp.bfloat16
    )
    grad_queries = jnp.einsum(
        "tbhc,thcd->tbd", scores_derivative, masked_rows(lookup), preferred_element_type=jnp.float32
    )
    grad_keys = jnp.einsum(
        "tbhc,tbhd->tcd", scores_derivative, masked_cols(asking), preferred_element_type=jnp.float32
    )
    return jnp.concatenate(
        [grad_queries.astype(jnp.bfloat16), grad_keys.astype(jnp.bfloat16), grad_values.astype(jnp.bfloat16)],
        axis=-1,
    )


def spatial_allowed(sessions_here, channel_count, adjacency):
    block_count = adjacency.shape[0]
    block_ids = jnp.arange(block_count, dtype=jnp.int32)
    session_pick = (
        sessions_here[:, None] == jnp.arange(channel_count.shape[0], dtype=jnp.int32)[None, :]
    ).astype(jnp.int32)
    count_rows = jnp.sum(session_pick * channel_count[None, :], axis=1)
    live_block = block_ids[None, :] * block_channels < count_rows[:, None]
    linked = adjacency > 0
    itself = block_ids[:, None] == block_ids[None, :]
    admissible_pairs = linked[None, :, :] & live_block[:, None, :] | itself[None, :, :]
    return admissible_pairs[:, None, :, :]


def project(rows, coefficient_array):
    return jnp.einsum("tbd,de->tbe", rows, coefficient_array, preferred_element_type=jnp.float32)


def project_back(derivative_collection, coefficient_array):
    return jnp.einsum(
        "tbe,de->tbd", derivative_collection, coefficient_array, preferred_element_type=jnp.float32
    )


def weight_term(left, right):
    return jnp.einsum("tbd,tbe->de", left, right, preferred_element_type=jnp.float32)


def reduce_rows(partial):
    rows, cols = partial.shape
    outer = lax.psum(1, "outer")
    pieces = partial.reshape(outer, 2, rows // (2 * outer), cols)
    first = lax.axis_index("core") == 0
    kept = jnp.where(first, pieces[:, 0], pieces[:, 1])
    given = jnp.where(first, pieces[:, 1], pieces[:, 0]).astype(jnp.bfloat16)
    taken = lax.ppermute(given, "core", [(0, 1), (1, 0)])
    pieces = (kept + taken.astype(jnp.float32)).astype(jnp.bfloat16)
    pieces = lax.all_to_all(pieces, "outer", 0, 0, tiled=True)
    return jnp.sum(pieces.astype(jnp.float32), axis=0)


def scatter_rows(partial):
    return lax.psum_scatter(
        partial.astype(jnp.bfloat16), ("outer", "core"), scatter_dimension=0, tiled=True
    ).astype(jnp.float32)


def per_device(
    activity,
    grad_out,
    spatial_weights,
    temporal_weights,
    spatial_gain,
    temporal_gain,
    adjacency,
    channel_count,
    session_id,
):
    local_bins = activity.shape[0]
    model_width = activity.shape[2]
    first_bin = (lax.axis_index("outer") * 2 + lax.axis_index("core")) * local_bins
    sessions_here = lax.dynamic_slice_in_dim(session_id, first_bin, local_bins)
    normed_one, inverse_one = norm_forward(activity, spatial_gain)
    spatial_proj = project(normed_one, spatial_weights[:, : 3 * model_width]).astype(jnp.bfloat16)
    allowed_space = spatial_allowed(sessions_here, channel_count, adjacency)
    spatial_context = spatial_forward_heads(spatial_proj, allowed_space)
    middle = (
        activity.astype(jnp.float32)
        + project(spatial_context, spatial_weights[:, 3 * model_width :])
    ).astype(jnp.bfloat16)
    middle_block = lax.all_to_all(middle, ("outer", "core"), split_axis=1, concat_axis=0, tiled=True)
    normed_two, inverse_two = norm_forward(middle_block, temporal_gain)
    temporal_proj = project(normed_two, temporal_weights[:, : 3 * model_width]).astype(jnp.bfloat16)
    allowed_time = session_id[:, None] == session_id[None, :]
    by_block = jnp.moveaxis(temporal_proj, 1, 0)
    temporal_context = jnp.moveaxis(
        lax.map(lambda block_rows: temporal_forward(block_rows, allowed_time), by_block), 0, 1
    )
    layer_out = (
        middle_block.astype(jnp.float32)
        + project(temporal_context, temporal_weights[:, 3 * model_width :])
    ).astype(jnp.bfloat16)
    grad_temporal_context = project_back(grad_out, temporal_weights[:, 3 * model_width :]).astype(
        jnp.bfloat16
    )
    stacked = (
        by_block,
        jnp.moveaxis(temporal_context, 1, 0),
        jnp.moveaxis(grad_temporal_context, 1, 0),
    )
    grad_temporal_proj = jnp.moveaxis(
        lax.map(
            lambda items: temporal_backward(items[0], allowed_time, items[1], items[2]), stacked
        ),
        0,
        1,
    )
    grad_normed_two = project_back(grad_temporal_proj, temporal_weights[:, : 3 * model_width])
    grad_middle = (
        grad_out.astype(jnp.float32)
        + norm_backward(middle_block, temporal_gain, inverse_two, grad_normed_two)
    ).astype(jnp.bfloat16)
    grad_middle_time = lax.all_to_all(grad_middle, ("outer", "core"), split_axis=0, concat_axis=1, tiled=True)
    normed_cols = normed_two
    context_cols = temporal_context
    temporal_grad = scatter_rows(
        jnp.concatenate(
            [weight_term(normed_cols, grad_temporal_proj), weight_term(context_cols, grad_out)],
            axis=1,
        )
    )
    spatial_term = weight_term(spatial_context, grad_middle_time)
    grad_spatial_context = project_back(
        grad_middle_time, spatial_weights[:, 3 * model_width :]
    ).astype(jnp.bfloat16)
    grad_spatial_proj = spatial_backward_heads(
        spatial_proj, allowed_space, spatial_context, grad_spatial_context
    )
    spatial_term = reduce_rows(spatial_term)
    spatial_term, grad_spatial_proj = lax.optimization_barrier((spatial_term, grad_spatial_proj))
    grad_normed_one = project_back(grad_spatial_proj, spatial_weights[:, : 3 * model_width])
    grad_activity = (
        grad_middle_time.astype(jnp.float32)
        + norm_backward(activity, spatial_gain, inverse_one, grad_normed_one)
    ).astype(jnp.bfloat16)
    normed_cols = normed_one
    context_cols = spatial_context
    spatial_grad = jnp.concatenate(
        [
            reduce_rows(weight_term(normed_cols, grad_spatial_proj)),
            spatial_term,
        ],
        axis=1,
    )
    return (layer_out, grad_activity, spatial_grad, temporal_grad)


def solution(mesh):
    groups, wide = mesh.devices.shape
    mesh = Mesh(mesh.devices.reshape(groups, wide // 2, 2), ("groups", "outer", "core"))
    placed = (
        P(("groups", "outer", "core"), None, None),
        P("groups", ("outer", "core"), None),
        P(),
        P(),
        P(),
        P(),
        P(),
        P("groups"),
        P("groups"),
    )
    return jax.shard_map(
        per_device,
        mesh=mesh,
        in_specs=placed,
        out_specs=(
            P("groups", ("outer", "core"), None),
            P(("groups", "outer", "core"), None, None),
            P(("groups", "outer", "core"), None),
            P(("groups", "outer", "core"), None),
        ),
        check_vma=False,
    )
```
